32 devices in a mesh: ctx: 8 (over y, x, core), uly: 4 (over z).
Axes of the slice: x: 2, y: 2, z: 4, core: 2. Of those that a mesh axis runs over, the one named last changes fastest.
Arguments:
- query_states: bfloat16 [1024, 2048], P(('ctx', 'uly')), may hold values from -8 to 8
- key_states: bfloat16 [1024, 2048], P(('ctx', 'uly')), may hold values from -8 to 8
- value_states: bfloat16 [1024, 2048], P(('ctx', 'uly')), may hold values from -6 to 6
- score_kernel: float32 [16, 6, 11], P('uly'), may hold values from -0.4 to 1.2
- head_mixing: float32 [16, 4], P('uly'), may hold values from 0.25 to 1
- head_gain: float32 [2048], P('uly'), may hold values from 0.5 to 1.5
Outputs:
- attended: bfloat16 [1024, 2048], P(('ctx', 'uly'))
The draws below stay inside these ranges and needn't reach their ends.
All inputs are finite; a program needn't handle non-finite values.
Results may differ from the reference program's by a relative error of at most 0.0049.
Values may be sent and summed in bfloat16 or wider, within the bound.
No kernel may reach another device: no remote copies, remote signals or barrier semaphores. Data moves between devices by JAX's collectives and lax.ppermute only.
A program may use at most 64 MiB of HBM per device.

```python
import math
import jax
import jax.numpy as jnp
from jax import lax

HEADS = 16
HEAD_DIM = 128
GROUP = 4
QCONV = 6
KCONV = 11
SEQ = 1024


def draw_query_states(key, part):
    width = HEADS * HEAD_DIM
    result = jnp.clip(jax.random.normal(jax.random.fold_in(key, 1), (SEQ, width), jnp.float32), -6.0, 6.0)
    return result.astype(jnp.bfloat16)


def draw_key_states(key, part):
    width = HEADS * HEAD_DIM
    result = jnp.clip(jax.random.normal(jax.random.fold_in(key, 2), (SEQ, width), jnp.float32), -6.0, 6.0)
    return result.astype(jnp.bfloat16)


def draw_score_kernel(key, part):
    shape = (HEADS, QCONV, KCONV)
    beside_all = 0.1 * jnp.clip(jax.random.normal(jax.random.fold_in(key, 52), shape, jnp.float32), -4.0, 4.0)
    center = jax.random.uniform(jax.random.fold_in(key, 53), shape, minval=0.9, maxval=1.2)
    at_anchor = (jnp.arange(QCONV)[None, :, None] == 0) & (jnp.arange(KCONV)[None, None, :] == 0)
    return jnp.where(at_anchor, center, beside_all).astype(jnp.float32)


def shard_levels(stream_key, dims, pieces, low, top_value):
    def one(dim, blocks):
        draws = jax.random.uniform(jax.random.fold_in(jax.random.fold_in(stream_key, 6), dim), (blocks,), jnp.float32, low / len(pieces), top_value / len(pieces))
        return jnp.repeat(jnp.exp(draws), dims[dim] // blocks).reshape((-1,) + (1,) * (len(dims) - dim - 1))

    level = one(*pieces[0])
    for cut in pieces[1:]:
        level = level * one(*cut)
    return level


def gaussian(stream_key, shape, scale, limit, split=(), kind=jnp.bfloat16):
    values = scale * jax.random.normal(stream_key, shape, jnp.float32)
    if split:
        values = values * shard_levels(stream_key, shape, split, -0.22, 0.18)
    return jnp.clip(values, -limit, limit).astype(kind)


def setup_inputs(seed: int = 0) -> dict:
    splits = jax.random.split(jax.random.key(seed), 7)
    query_states = draw_query_states(jax.random.fold_in(splits[6], 71), 0)
    key_states = draw_key_states(jax.random.fold_in(splits[6], 71), 0)
    value_states = gaussian(splits[2], (SEQ, HEADS * HEAD_DIM), 1.0, 6.0, ((0, 32),))
    score_kernel = draw_score_kernel(jax.random.fold_in(splits[6], 71), 0)
    head_mixing = jnp.clip(0.25 + 0.75 * jax.random.uniform(splits[4], (HEADS, GROUP), jnp.float32) ** shard_levels(splits[4], (HEADS, GROUP), ((0, 4),), -0.2, 0.2), 0.25, 1.0)
    head_gain = jnp.clip(1.0 + 0.1 * jax.random.normal(splits[5], (HEADS * HEAD_DIM,), jnp.float32), 0.5, 1.5)
    return dict(query_states=query_states, key_states=key_states, value_states=value_states, score_kernel=score_kernel, head_mixing=head_mixing, head_gain=head_gain)


lowest = -1e+30
epsilon = 1e-06

def reference(query_states, key_states, value_states, score_kernel, head_mixing, head_gain):
    seq_len, width = query_states.shape
    heads = score_kernel.shape[0]
    head_dim = width // heads
    groups = heads // GROUP
    row_lead = QCONV - 1
    col_lead = KCONV - 1
    block = math.gcd(seq_len, 512)
    group_width = GROUP * head_dim
    query_pad = jnp.concatenate([jnp.zeros((row_lead, width), query_states.dtype), query_states], axis=0)
    key_pad = jnp.concatenate([jnp.zeros((col_lead, width), key_states.dtype), key_states], axis=0)
    key_pos = lax.iota(jnp.int32, seq_len + col_lead) - col_lead
    anchor = jnp.zeros((), jnp.int32)

    def one_group(group_id):
        cols = (group_id * group_width).astype(jnp.int32)
        first_head = (group_id * GROUP).astype(jnp.int32)
        key_rows = lax.dynamic_slice(key_pad, (anchor, cols), (seq_len + col_lead, group_width))
        key_rows = key_rows.astype(jnp.float32).reshape(seq_len + col_lead, GROUP, head_dim)
        value_rows = lax.dynamic_slice(value_states, (anchor, cols), (seq_len, group_width))
        value_rows = value_rows.astype(jnp.float32).reshape(seq_len, GROUP, head_dim)
        weights = lax.dynamic_slice(head_mixing, (first_head, anchor), (GROUP, GROUP))
        taps = lax.dynamic_slice(score_kernel, (first_head, anchor, anchor), (GROUP, QCONV, KCONV))
        scale_group = lax.dynamic_slice(head_gain, (cols,), (group_width,)).reshape(GROUP, head_dim)

        def one_block(block_id):
            start = (block_id * block).astype(jnp.int32)
            query_rows = lax.dynamic_slice(query_pad, (start, cols), (block + row_lead, group_width))
            query_rows = query_rows.astype(jnp.float32).reshape(block + row_lead, GROUP, head_dim)
            dot_scores = jnp.einsum('qhd,khd->hqk', query_rows, key_rows, precision=lax.Precision.HIGHEST)
            dot_scores = dot_scores * head_dim ** (-0.5)
            query_pos = start - row_lead + lax.iota(jnp.int32, block + row_lead)
            inside = (key_pos[None, :] <= query_pos[:, None]) & (key_pos[None, :] >= 0) & (query_pos[:, None] >= 0)
            dot_scores = jnp.where(inside[None], dot_scores, 0.0)
            convolved = jnp.zeros((GROUP, block, seq_len), jnp.float32)
            for row_lag in range(QCONV):
                for col_lag in range(KCONV):
                    window = dot_scores[:, row_lead - row_lag:row_lead - row_lag + block, col_lead - col_lag:col_lead - col_lag + seq_len]
                    convolved = convolved + taps[:, row_lag, col_lag][:, None, None] * window
            causal = key_pos[None, col_lead:] <= query_pos[row_lead:, None]
            logits = jnp.where(causal[None], convolved, lowest)
            peak = lax.optimization_barrier(jnp.max(logits, axis=2, keepdims=True))
            expd = jnp.exp(logits - peak)
            probabilities = expd / lax.optimization_barrier(jnp.sum(expd, axis=2, keepdims=True))
            mixed_probs = jnp.zeros_like(probabilities)
            for source in range(GROUP):
                mixed_probs = mixed_probs + weights[:, source][:, None, None] * probabilities[source][None]
            mixed_probs = mixed_probs.astype(jnp.bfloat16)
            weighted = jnp.einsum('hqk,khd->qhd', mixed_probs.astype(jnp.float32), value_rows, precision=lax.Precision.HIGHEST)
            factor = lax.rsqrt(lax.optimization_barrier(jnp.mean(weighted * weighted, axis=2, keepdims=True)) + epsilon)
            normed = weighted * factor * scale_group[None]
            return normed.astype(jnp.bfloat16).reshape(block, group_width)
        outputs = lax.map(one_block, jnp.arange(seq_len // block, dtype=jnp.int32))
        return outputs.reshape(seq_len, group_width)
    grouped = lax.map(one_group, jnp.arange(groups, dtype=jnp.int32))
    return jnp.transpose(grouped, (1, 0, 2)).reshape(seq_len, width)
```

```python
import jax
import jax.numpy as jnp
from jax import lax
from jax.sharding import PartitionSpec as P

GROUP = 4
QCONV = 6
KCONV = 11
KEY_BLOCK = 128
ROW_CHUNK = 128
KEY_GROUP = 8


lowest = -1e30
epsilon = 1e-06


def passed_along(shard, axis, by):
    peers = lax.axis_size(axis)
    pairs = [(i, i + by) for i in range(peers) if 0 <= i + by < peers]
    return lax.ppermute(shard, axis, pairs)


def split_bf16(values):
    high = lax.reduce_precision(values, exponent_bits=8, mantissa_bits=7)
    low = values - high
    return high.astype(jnp.bfloat16), low.astype(jnp.bfloat16)


def toeplitz_terms(score_kernel, head_dim):
    col_lead = KCONV - 1
    scaled = score_kernel * head_dim ** (-0.5)
    lag = (
        lax.iota(jnp.int32, KEY_BLOCK)[:, None]
        + col_lead
        - lax.iota(jnp.int32, KEY_BLOCK + col_lead)[None, :]
    )
    toeplitz = jnp.zeros(score_kernel.shape[:2] + lag.shape, jnp.float32)
    for col_lag in range(KCONV):
        toeplitz = jnp.where(lag == col_lag, scaled[:, :, col_lag, None, None], toeplitz)
    return split_bf16(toeplitz)


def convolved_keys(key_windows, terms):
    high, low = terms
    heads = high.shape[0]
    key_heads = key_windows.reshape(key_windows.shape[:2] + (heads, -1))
    conv_keys = jnp.einsum(
        "harc,nchd->nhard", high, key_heads, preferred_element_type=jnp.float32
    ) + jnp.einsum("harc,nchd->nhard", low, key_heads, preferred_element_type=jnp.float32)
    return split_bf16(conv_keys)


def band_terms(query_rows, query_first, key_flat, score_kernel):
    row_lead = QCONV - 1
    heads = score_kernel.shape[0]
    ext_count = query_rows.shape[0]
    row_count = ext_count - row_lead
    near = lax.dynamic_slice_in_dim(key_flat, query_first + 4, ext_count + QCONV - 2, 0)
    query_heads = query_rows.reshape(ext_count, heads, -1).astype(jnp.float32)
    near_heads = near.reshape(near.shape[0], heads, -1).astype(jnp.float32)
    scale = query_heads.shape[2] ** (-0.5)
    diagonals = [
        jnp.sum(query_heads * near_heads[lag - 1 : lag - 1 + ext_count], axis=2) * scale
        for lag in range(1, QCONV)
    ]
    band = []
    for gap in range(QCONV - 1):
        acc = jnp.zeros((row_count, heads), jnp.float32)
        for row_lag in range(gap + 1, QCONV):
            for col_lag in range(row_lag - gap):
                lag = row_lag - col_lag - gap
                acc = acc - score_kernel[None, :, row_lag, col_lag] * diagonals[lag - 1][
                    row_lead - row_lag : row_lead - row_lag + row_count
                ]
        band.append(acc.T)
    return jnp.stack(band)


def group_logits(shifted, key_windows, terms):
    keys_high, keys_low = convolved_keys(key_windows, terms)
    return jnp.einsum(
        "ihad,nhard->hinr", shifted, keys_high, preferred_element_type=jnp.float32
    ) + jnp.einsum("ihad,nhard->hinr", shifted, keys_low, preferred_element_type=jnp.float32)


def attend_chunk(shifted, band, query_first, key_windows, terms, value_heads, head_mixing):
    row_count, heads = shifted.shape[:2]
    seq_len = value_heads.shape[0]
    window_count = key_windows.shape[0]
    if window_count <= KEY_GROUP:
        convolved = group_logits(shifted, key_windows, terms)
    else:
        grouped_windows = key_windows.reshape(
            (window_count // KEY_GROUP, KEY_GROUP) + key_windows.shape[1:]
        )
        convolved = lax.map(lambda windows: group_logits(shifted, windows, terms), grouped_windows)
        convolved = jnp.moveaxis(convolved, 0, 2)
    convolved = convolved.reshape(heads, row_count, seq_len)
    query_pos = query_first + lax.iota(jnp.int32, row_count)
    gap = query_pos[:, None] - lax.iota(jnp.int32, seq_len)[None, :]
    for lag in range(QCONV - 1):
        convolved = convolved + jnp.where(gap == lag, band[lag][:, :, None], 0.0)
    logits = jnp.where(gap >= 0, convolved, lowest)
    peak = jnp.max(logits, axis=2, keepdims=True)
    expd = jnp.exp(logits - peak)
    probabilities = expd / jnp.sum(expd, axis=2, keepdims=True)
    grouped = probabilities.reshape(heads // GROUP, GROUP, row_count, seq_len)
    weights = head_mixing.reshape(heads // GROUP, GROUP, GROUP)
    mixed_probs = jnp.zeros_like(grouped)
    for source in range(GROUP):
        mixed_probs = mixed_probs + weights[:, :, source, None, None] * grouped[:, source, None]
    mixed_probs = mixed_probs.reshape(heads, row_count, seq_len).astype(jnp.bfloat16)
    return jnp.einsum(
        "hik,khd->ihd", mixed_probs, value_heads, preferred_element_type=jnp.float32
    )


def normalize(weighted, gain_local):
    factor = lax.rsqrt(jnp.mean(weighted * weighted, axis=2, keepdims=True) + epsilon)
    return (
        (weighted * factor * gain_local[None]).astype(jnp.bfloat16).reshape(weighted.shape[0], -1)
    )


def shards(query_states, key_states, value_states, score_kernel, head_mixing, head_gain):
    query_local, key_local, value_local = (
        lax.all_to_all(query_states, "uly", split_axis=1, concat_axis=0, tiled=True),
        lax.all_to_all(key_states, "uly", split_axis=1, concat_axis=0, tiled=True),
        lax.all_to_all(value_states, "uly", split_axis=1, concat_axis=0, tiled=True),
    )
    shard_rows = query_local.shape[0]
    width = query_local.shape[1]
    row_lead = QCONV - 1
    col_lead = KCONV - 1
    heads = score_kernel.shape[0]
    head_dim = width // heads
    ctx_place = lax.axis_index("ctx")
    query_first = ctx_place * shard_rows
    earlier = passed_along(query_local[shard_rows - row_lead :], "ctx", 1)
    query_ext = jnp.concatenate([earlier, query_local], axis=0)
    key_all = lax.all_gather(key_local, "ctx", axis=0, tiled=True)
    value_all = lax.all_gather(value_local, "ctx", axis=0, tiled=True)
    seq_len = key_all.shape[0]
    key_pad = jnp.concatenate([jnp.zeros((col_lead, width), key_all.dtype), key_all], axis=0)
    key_windows = jnp.stack(
        [
            key_pad[start : start + KEY_BLOCK + col_lead]
            for start in range(0, seq_len, KEY_BLOCK)
        ]
    )
    terms = toeplitz_terms(score_kernel, head_dim)
    edge = jnp.zeros((8, width), key_all.dtype)
    key_flat = jnp.concatenate([edge, key_all, edge], axis=0)
    band = band_terms(query_ext, query_first, key_flat, score_kernel)
    query_heads = query_ext.reshape(shard_rows + row_lead, heads, head_dim)
    shifted = jnp.stack(
        [query_heads[row_lead - lag : row_lead - lag + shard_rows] for lag in range(QCONV)], axis=2
    )
    value_heads = value_all.reshape(seq_len, heads, head_dim)
    chunk = min(ROW_CHUNK * KEY_BLOCK * 8 // seq_len, shard_rows)
    if chunk == shard_rows:
        weighted = attend_chunk(
            shifted, band, query_first, key_windows, terms, value_heads, head_mixing
        )
    else:
        chunks = shard_rows // chunk

        def one_chunk(index):
            start = index * chunk
            return attend_chunk(
                lax.dynamic_slice_in_dim(shifted, start, chunk, 0),
                lax.dynamic_slice_in_dim(band, start, chunk, 2),
                query_first + start,
                key_windows,
                terms,
                value_heads,
                head_mixing,
            )

        weighted = lax.map(one_chunk, jnp.arange(chunks, dtype=jnp.int32))
        weighted = weighted.reshape((shard_rows,) + weighted.shape[2:])
    gain_local = head_gain.reshape(heads, head_dim)
    attended = normalize(weighted, gain_local)
    return lax.all_to_all(attended, "uly", split_axis=0, concat_axis=1, tiled=True)


def solution(mesh):
    placed = (
        P(("ctx", "uly"), None),
        P(("ctx", "uly"), None),
        P(("ctx", "uly"), None),
        P("uly", None, None),
        P("uly", None),
        P("uly"),
    )
    return jax.shard_map(
        shards, mesh=mesh, in_specs=placed, out_specs=P(("ctx", "uly"), None), check_vma=False
    )
```

```python
import jax
import jax.numpy as jnp
from jax import lax
from jax.sharding import PartitionSpec as P

GROUP = 4
QCONV = 6
KCONV = 11
KEY_BLOCK = 128
ROW_CHUNK = 128
KEY_GROUP = 8


lowest = -1e30
epsilon = 1e-06


def passed_along(shard, axis, by):
    peers = lax.axis_size(axis)
    pairs = [(i, i + by) for i in range(peers) if 0 <= i + by < peers]
    return lax.ppermute(shard, axis, pairs)


def split_bf16(values):
    high = lax.reduce_precision(values, exponent_bits=8, mantissa_bits=7)
    low = values - high
    return high.astype(jnp.bfloat16), low.astype(jnp.bfloat16)


def toeplitz_terms(score_kernel, head_dim):
    col_lead = KCONV - 1
    scaled = score_kernel * head_dim ** (-0.5)
    lag = (
        lax.iota(jnp.int32, KEY_BLOCK)[:, None]
        + col_lead
        - lax.iota(jnp.int32, KEY_BLOCK + col_lead)[None, :]
    )
    toeplitz = jnp.zeros(score_kernel.shape[:2] + lag.shape, jnp.float32)
    for col_lag in range(KCONV):
        toeplitz = jnp.where(lag == col_lag, scaled[:, :, col_lag, None, None], toeplitz)
    return split_bf16(toeplitz)


def convolved_keys(key_windows, terms):
    high, low = terms
    heads = high.shape[0]
    key_heads = key_windows.reshape(key_windows.shape[:2] + (heads, -1))
    conv_keys = jnp.einsum(
        "harc,nchd->nhard", high, key_heads, preferred_element_type=jnp.float32
    ) + jnp.einsum("harc,nchd->nhard", low, key_heads, preferred_element_type=jnp.float32)
    return split_bf16(conv_keys)


def band_terms(query_rows, query_first, key_flat, score_kernel):
    row_lead = QCONV - 1
    heads = score_kernel.shape[0]
    ext_count = query_rows.shape[0]
    row_count = ext_count - row_lead
    near = lax.dynamic_slice_in_dim(key_flat, query_first + 4, ext_count + QCONV - 2, 0)
    query_heads = query_rows.reshape(ext_count, heads, -1).astype(jnp.float32)
    near_heads = near.reshape(near.shape[0], heads, -1).astype(jnp.float32)
    scale = query_heads.shape[2] ** (-0.5)
    diagonals = [
        jnp.sum(query_heads * near_heads[lag - 1 : lag - 1 + ext_count], axis=2) * scale
        for lag in range(1, QCONV)
    ]
    band = []
    for gap in range(QCONV - 1):
        acc = jnp.zeros((row_count, heads), jnp.float32)
        for row_lag in range(gap + 1, QCONV):
            for col_lag in range(row_lag - gap):
                lag = row_lag - col_lag - gap
                acc = acc - score_kernel[None, :, row_lag, col_lag] * diagonals[lag - 1][
                    row_lead - row_lag : row_lead - row_lag + row_count
                ]
        band.append(acc.T)
    return jnp.stack(band)


def group_logits(shifted, key_windows, terms):
    keys_high, keys_low = convolved_keys(key_windows, terms)
    return jnp.einsum(
        "ihad,nhard->hinr", shifted, keys_high, preferred_element_type=jnp.float32
    ) + jnp.einsum("ihad,nhard->hinr", shifted, keys_low, preferred_element_type=jnp.float32)


def attend_chunk(shifted, band, query_first, key_windows, terms, value_heads, head_mixing):
    row_count, heads = shifted.shape[:2]
    seq_len = value_heads.shape[0]
    window_count = key_windows.shape[0]
    if window_count <= KEY_GROUP:
        convolved = group_logits(shifted, key_windows, terms)
    else:
        grouped_windows = key_windows.reshape(
            (window_count // KEY_GROUP, KEY_GROUP) + key_windows.shape[1:]
        )
        convolved = lax.map(lambda windows: group_logits(shifted, windows, terms), grouped_windows)
        convolved = jnp.moveaxis(convolved, 0, 2)
    convolved = convolved.reshape(heads, row_count, seq_len)
    query_pos = query_first + lax.iota(jnp.int32, row_count)
    gap = query_pos[:, None] - lax.iota(jnp.int32, seq_len)[None, :]
    for lag in range(QCONV - 1):
        convolved = convolved + jnp.where(gap == lag, band[lag][:, :, None], 0.0)
    logits = jnp.where(gap >= 0, convolved, lowest)
    peak = jnp.max(logits, axis=2, keepdims=True)
    expd = jnp.exp(logits - peak)
    probabilities = expd / jnp.sum(expd, axis=2, keepdims=True)
    grouped = probabilities.reshape(heads // GROUP, GROUP, row_count, seq_len)
    weights = head_mixing.reshape(heads // GROUP, GROUP, GROUP)
    mixed_probs = jnp.zeros_like(grouped)
    for source in range(GROUP):
        mixed_probs = mixed_probs + weights[:, :, source, None, None] * grouped[:, source, None]
    mixed_probs = mixed_probs.reshape(heads, row_count, seq_len).astype(jnp.bfloat16)
    return jnp.einsum(
        "hik,khd->ihd", mixed_probs, value_heads, preferred_element_type=jnp.float32
    )


def normalize(weighted, gain_local):
    factor = lax.rsqrt(jnp.mean(weighted * weighted, axis=2, keepdims=True) + epsilon)
    return (
        (weighted * factor * gain_local[None]).astype(jnp.bfloat16).reshape(weighted.shape[0], -1)
    )


def shards(query_states, key_states, value_states, score_kernel, head_mixing, head_gain):
    stacked = jnp.stack([query_states, key_states, value_states])
    query_local, key_local, value_local = lax.all_to_all(
        stacked, "uly", split_axis=2, concat_axis=1, tiled=True
    )
    shard_rows = query_local.shape[0]
    width = query_local.shape[1]
    row_lead = QCONV - 1
    col_lead = KCONV - 1
    heads = score_kernel.shape[0]
    head_dim = width // heads
    ctx_place = lax.axis_index("ctx")
    query_first = ctx_place * shard_rows
    earlier = passed_along(query_local[shard_rows - row_lead :], "ctx", 1)
    query_ext = jnp.concatenate([earlier, query_local], axis=0)
    key_all, value_all = lax.all_gather(
        jnp.stack([key_local, value_local]), "ctx", axis=1, tiled=True
    )
    seq_len = key_all.shape[0]
    key_pad = jnp.concatenate([jnp.zeros((col_lead, width), key_all.dtype), key_all], axis=0)
    key_windows = jnp.stack(
        [
            key_pad[start : start + KEY_BLOCK + col_lead]
            for start in range(0, seq_len, KEY_BLOCK)
        ]
    )
    terms = toeplitz_terms(score_kernel, head_dim)
    edge = jnp.zeros((8, width), key_all.dtype)
    key_flat = jnp.concatenate([edge, key_all, edge], axis=0)
    band = band_terms(query_ext, query_first, key_flat, score_kernel)
    query_heads = query_ext.reshape(shard_rows + row_lead, heads, head_dim)
    shifted = jnp.stack(
        [query_heads[row_lead - lag : row_lead - lag + shard_rows] for lag in range(QCONV)], axis=2
    )
    value_heads = value_all.reshape(seq_len, heads, head_dim)
    chunk = min(ROW_CHUNK * KEY_BLOCK * 8 // seq_len, shard_rows)
    if chunk == shard_rows:
        weighted = attend_chunk(
            shifted, band, query_first, key_windows, terms, value_heads, head_mixing
        )
    else:
        chunks = shard_rows // chunk

        def one_chunk(index):
            start = index * chunk
            return attend_chunk(
                lax.dynamic_slice_in_dim(shifted, start, chunk, 0),
                lax.dynamic_slice_in_dim(band, start, chunk, 2),
                query_first + start,
                key_windows,
                terms,
                value_heads,
                head_mixing,
            )

        weighted = lax.map(one_chunk, jnp.arange(chunks, dtype=jnp.int32))
        weighted = weighted.reshape((shard_rows,) + weighted.shape[2:])
    gain_local = head_gain.reshape(heads, head_dim)
    attended = normalize(weighted, gain_local)
    return lax.all_to_all(attended, "uly", split_axis=0, concat_axis=1, tiled=True)


def solution(mesh):
    placed = (
        P(("ctx", "uly"), None),
        P(("ctx", "uly"), None),
        P(("ctx", "uly"), None),
        P("uly", None, None),
        P("uly", None),
        P("uly"),
    )
    return jax.shard_map(
        shards, mesh=mesh, in_specs=placed, out_specs=P(("ctx", "uly"), None), check_vma=False
    )
```

```python
import jax
import jax.numpy as jnp
from jax import lax
from jax.sharding import PartitionSpec as P

GROUP = 4
QCONV = 6
KCONV = 11
KEY_BLOCK = 128
ROW_CHUNK = 128
KEY_GROUP = 8


lowest = -1e30
epsilon = 1e-06


def passed_along(shard, axis, by):
    peers = lax.axis_size(axis)
    pairs = [(i, i + by) for i in range(peers) if 0 <= i + by < peers]
    return lax.ppermute(shard, axis, pairs)


def split_bf16(values):
    high = lax.reduce_precision(values, exponent_bits=8, mantissa_bits=7)
    low = values - high
    return high.astype(jnp.bfloat16), low.astype(jnp.bfloat16)


def exchanged(pieces_of, axis):
    peers = lax.axis_size(axis)
    place = lax.axis_index(axis)
    received = [pieces_of(place)]
    for shift in range(1, peers):
        outgoing = pieces_of((place + shift) % peers)
        pairs = [(i, (i + shift) % peers) for i in range(peers)]
        received.append(lax.ppermute(outgoing, axis, pairs))
    order = (place - jnp.arange(peers, dtype=jnp.int32)) % peers
    return jnp.take(jnp.stack(received), order, axis=0)


def gathered(shard, axis):
    peers = lax.axis_size(axis)
    place = lax.axis_index(axis)
    if peers & (peers - 1):
        return lax.all_gather(shard, axis, axis=0, tiled=False)
    bits = peers.bit_length() - 1
    held = shard[None]
    for level in reversed(range(bits)):
        bit = 1 << level
        incoming = lax.ppermute(held, axis, [(i, i ^ bit) for i in range(peers)])
        upper = (place & bit) != 0
        held = jnp.where(
            upper,
            jnp.concatenate([incoming, held], axis=0),
            jnp.concatenate([held, incoming], axis=0),
        )
    held = held.reshape((2,) * bits + shard.shape)
    return jnp.transpose(held, tuple(reversed(range(bits))) + tuple(range(bits, held.ndim)))


def toeplitz_terms(score_kernel, head_dim):
    col_lead = KCONV - 1
    scaled = score_kernel * head_dim ** (-0.5)
    lag = (
        lax.iota(jnp.int32, KEY_BLOCK)[:, None]
        + col_lead
        - lax.iota(jnp.int32, KEY_BLOCK + col_lead)[None, :]
    )
    toeplitz = jnp.zeros(score_kernel.shape[:2] + lag.shape, jnp.float32)
    for col_lag in range(KCONV):
        toeplitz = jnp.where(lag == col_lag, scaled[:, :, col_lag, None, None], toeplitz)
    return split_bf16(toeplitz)


def convolved_keys(key_windows, terms):
    high, low = terms
    heads = high.shape[0]
    key_heads = key_windows.reshape(key_windows.shape[:2] + (heads, -1))
    conv_keys = jnp.einsum(
        "harc,nchd->nhard", high, key_heads, preferred_element_type=jnp.float32
    ) + jnp.einsum("harc,nchd->nhard", low, key_heads, preferred_element_type=jnp.float32)
    return split_bf16(conv_keys)


def band_terms(query_rows, query_first, key_flat, score_kernel):
    row_lead = QCONV - 1
    heads = score_kernel.shape[0]
    ext_count = query_rows.shape[0]
    row_count = ext_count - row_lead
    near = lax.dynamic_slice_in_dim(key_flat, query_first + 4, ext_count + QCONV - 2, 0)
    query_heads = query_rows.reshape(ext_count, heads, -1).astype(jnp.float32)
    near_heads = near.reshape(near.shape[0], heads, -1).astype(jnp.float32)
    scale = query_heads.shape[2] ** (-0.5)
    diagonals = [
        jnp.sum(query_heads * near_heads[lag - 1 : lag - 1 + ext_count], axis=2) * scale
        for lag in range(1, QCONV)
    ]
    band = []
    for gap in range(QCONV - 1):
        acc = jnp.zeros((row_count, heads), jnp.float32)
        for row_lag in range(gap + 1, QCONV):
            for col_lag in range(row_lag - gap):
                lag = row_lag - col_lag - gap
                acc = acc - score_kernel[None, :, row_lag, col_lag] * diagonals[lag - 1][
                    row_lead - row_lag : row_lead - row_lag + row_count
                ]
        band.append(acc.T)
    return jnp.stack(band)


def group_logits(shifted, key_windows, terms):
    keys_high, keys_low = convolved_keys(key_windows, terms)
    return jnp.einsum(
        "ihad,nhard->hinr", shifted, keys_high, preferred_element_type=jnp.float32
    ) + jnp.einsum("ihad,nhard->hinr", shifted, keys_low, preferred_element_type=jnp.float32)


def attend_chunk(shifted, band, query_first, key_windows, terms, value_heads, head_mixing):
    row_count, heads = shifted.shape[:2]
    seq_len = value_heads.shape[0]
    window_count = key_windows.shape[0]
    if window_count <= KEY_GROUP:
        convolved = group_logits(shifted, key_windows, terms)
    else:
        grouped_windows = key_windows.reshape(
            (window_count // KEY_GROUP, KEY_GROUP) + key_windows.shape[1:]
        )
        convolved = lax.map(lambda windows: group_logits(shifted, windows, terms), grouped_windows)
        convolved = jnp.moveaxis(convolved, 0, 2)
    convolved = convolved.reshape(heads, row_count, seq_len)
    query_pos = query_first + lax.iota(jnp.int32, row_count)
    gap = query_pos[:, None] - lax.iota(jnp.int32, seq_len)[None, :]
    for lag in range(QCONV - 1):
        convolved = convolved + jnp.where(gap == lag, band[lag][:, :, None], 0.0)
    logits = jnp.where(gap >= 0, convolved, lowest)
    peak = jnp.max(logits, axis=2, keepdims=True)
    expd = jnp.exp(logits - peak)
    probabilities = expd / jnp.sum(expd, axis=2, keepdims=True)
    grouped = probabilities.reshape(heads // GROUP, GROUP, row_count, seq_len)
    weights = head_mixing.reshape(heads // GROUP, GROUP, GROUP)
    mixed_probs = jnp.zeros_like(grouped)
    for source in range(GROUP):
        mixed_probs = mixed_probs + weights[:, :, source, None, None] * grouped[:, source, None]
    mixed_probs = mixed_probs.reshape(heads, row_count, seq_len).astype(jnp.bfloat16)
    return jnp.einsum(
        "hik,khd->ihd", mixed_probs, value_heads, preferred_element_type=jnp.float32
    )


def normalize(weighted, gain_local):
    factor = lax.rsqrt(jnp.mean(weighted * weighted, axis=2, keepdims=True) + epsilon)
    return (
        (weighted * factor * gain_local[None]).astype(jnp.bfloat16).reshape(weighted.shape[0], -1)
    )


def shards(query_states, key_states, value_states, score_kernel, head_mixing, head_gain):
    groups = lax.axis_size("uly")
    stacked = jnp.stack([query_states, key_states, value_states])
    group_width = stacked.shape[2] // groups
    pieces = exchanged(
        lambda group: lax.dynamic_slice_in_dim(stacked, group * group_width, group_width, 2),
        "uly",
    )
    pieces = jnp.moveaxis(pieces, 0, 1)
    query_local, key_local, value_local = pieces.reshape(
        (pieces.shape[0], -1, pieces.shape[-1])
    )
    shard_rows = query_local.shape[0]
    width = query_local.shape[1]
    row_lead = QCONV - 1
    col_lead = KCONV - 1
    heads = score_kernel.shape[0]
    head_dim = width // heads
    ctx_place = lax.axis_index("ctx")
    query_first = ctx_place * shard_rows
    earlier = passed_along(query_local[shard_rows - row_lead :], "ctx", 1)
    query_ext = jnp.concatenate([earlier, query_local], axis=0)
    key_all = gathered(key_local, "ctx").reshape((-1, width))
    value_all = gathered(value_local, "ctx").reshape((-1, width))
    seq_len = key_all.shape[0]
    key_pad = jnp.concatenate([jnp.zeros((col_lead, width), key_all.dtype), key_all], axis=0)
    key_windows = jnp.stack(
        [
            key_pad[start : start + KEY_BLOCK + col_lead]
            for start in range(0, seq_len, KEY_BLOCK)
        ]
    )
    terms = toeplitz_terms(score_kernel, head_dim)
    edge = jnp.zeros((8, width), key_all.dtype)
    key_flat = jnp.concatenate([edge, key_all, edge], axis=0)
    band = band_terms(query_ext, query_first, key_flat, score_kernel)
    query_heads = query_ext.reshape(shard_rows + row_lead, heads, head_dim)
    shifted = jnp.stack(
        [query_heads[row_lead - lag : row_lead - lag + shard_rows] for lag in range(QCONV)], axis=2
    )
    value_heads = value_all.reshape(seq_len, heads, head_dim)
    chunk = min(ROW_CHUNK * KEY_BLOCK * 8 // seq_len, shard_rows)
    if chunk == shard_rows:
        weighted = attend_chunk(
            shifted, band, query_first, key_windows, terms, value_heads, head_mixing
        )
    else:
        chunks = shard_rows // chunk

        def one_chunk(index):
            start = index * chunk
            return attend_chunk(
                lax.dynamic_slice_in_dim(shifted, start, chunk, 0),
                lax.dynamic_slice_in_dim(band, start, chunk, 2),
                query_first + start,
                key_windows,
                terms,
                value_heads,
                head_mixing,
            )

        weighted = lax.map(one_chunk, jnp.arange(chunks, dtype=jnp.int32))
        weighted = weighted.reshape((shard_rows,) + weighted.shape[2:])
    gain_local = head_gain.reshape(heads, head_dim)
    attended = normalize(weighted, gain_local)
    block_rows = shard_rows // groups
    returned = exchanged(
        lambda group: lax.dynamic_slice_in_dim(attended, group * block_rows, block_rows, 0),
        "uly",
    )
    return jnp.moveaxis(returned, 0, 1).reshape((block_rows, -1))


def solution(mesh):
    placed = (
        P(("ctx", "uly"), None),
        P(("ctx", "uly"), None),
        P(("ctx", "uly"), None),
        P("uly", None, None),
        P("uly", None),
        P("uly"),
    )
    return jax.shard_map(
        shards, mesh=mesh, in_specs=placed, out_specs=P(("ctx", "uly"), None), check_vma=False
    )
```

```python
import jax
import jax.numpy as jnp
from jax import lax
from jax.experimental import pallas as pl
from jax.sharding import PartitionSpec as P

GROUP = 4
QCONV = 6
KCONV = 11
KEY_BLOCK = 128
ROW_CHUNK = 128


lowest = -1e30
epsilon = 1e-06


def passed_along(shard, axis, by):
    peers = lax.axis_size(axis)
    pairs = [(i, i + by) for i in range(peers) if 0 <= i + by < peers]
    return lax.ppermute(shard, axis, pairs)


def split_bf16(values):
    high = lax.reduce_precision(values, exponent_bits=8, mantissa_bits=7)
    low = values - high
    return high.astype(jnp.bfloat16), low.astype(jnp.bfloat16)


def exchanged(pieces_of, axis):
    peers = lax.axis_size(axis)
    place = lax.axis_index(axis)
    received = [pieces_of(place)]
    for shift in range(1, peers):
        outgoing = pieces_of((place + shift) % peers)
        pairs = [(i, (i + shift) % peers) for i in range(peers)]
        received.append(lax.ppermute(outgoing, axis, pairs))
    order = (place - jnp.arange(peers, dtype=jnp.int32)) % peers
    return jnp.take(jnp.stack(received), order, axis=0)


def gathered(shard, axis):
    peers = lax.axis_size(axis)
    place = lax.axis_index(axis)
    if peers & (peers - 1):
        return lax.all_gather(shard, axis, axis=0, tiled=False)
    bits = peers.bit_length() - 1
    held = shard[None]
    for level in reversed(range(bits)):
        bit = 1 << level
        incoming = lax.ppermute(held, axis, [(i, i ^ bit) for i in range(peers)])
        upper = (place & bit) != 0
        held = jnp.where(
            upper,
            jnp.concatenate([incoming, held], axis=0),
            jnp.concatenate([held, incoming], axis=0),
        )
    held = held.reshape((2,) * bits + shard.shape)
    return jnp.transpose(held, tuple(reversed(range(bits))) + tuple(range(bits, held.ndim)))


def toeplitz_terms(score_kernel, head_dim):
    scaled = score_kernel * head_dim ** (-0.5)
    lag = (
        lax.iota(jnp.int32, KEY_BLOCK)[:, None]
        + KEY_BLOCK
        - lax.iota(jnp.int32, 2 * KEY_BLOCK)[None, :]
    )
    toeplitz = jnp.zeros(score_kernel.shape[:2] + lag.shape, jnp.float32)
    for col_lag in range(KCONV):
        toeplitz = jnp.where(lag == col_lag, scaled[:, :, col_lag, None, None], toeplitz)
    toeplitz = toeplitz.reshape((toeplitz.shape[0], -1, toeplitz.shape[3]))
    return split_bf16(toeplitz)


def logits_kernel(query_ref, high_ref, low_ref, before_ref, current_ref, out_ref):
    window = pl.program_id(1)
    before = jnp.where(
        window > 0, before_ref[...], jnp.zeros(before_ref.shape, before_ref.dtype)
    )
    current = current_ref[...]
    high = high_ref[0]
    low = low_ref[0]
    conv_keys = (
        jnp.dot(high[:, :KEY_BLOCK], before, preferred_element_type=jnp.float32)
        + jnp.dot(high[:, KEY_BLOCK:], current, preferred_element_type=jnp.float32)
        + jnp.dot(low[:, :KEY_BLOCK], before, preferred_element_type=jnp.float32)
        + jnp.dot(low[:, KEY_BLOCK:], current, preferred_element_type=jnp.float32)
    )
    keys_high = conv_keys.astype(jnp.bfloat16)
    keys_low = (conv_keys - keys_high.astype(jnp.float32)).astype(jnp.bfloat16)
    query = query_ref[0]
    head_dim = current.shape[1]
    dims = (((1,), (1,)), ((), ()))
    acc = jnp.zeros(out_ref.shape[1:], jnp.float32)
    for row_lag in range(QCONV):
        part = query[:, row_lag * head_dim : (row_lag + 1) * head_dim]
        acc = acc + lax.dot_general(
            part,
            keys_high[row_lag * KEY_BLOCK : (row_lag + 1) * KEY_BLOCK],
            dims,
            preferred_element_type=jnp.float32,
        )
        acc = acc + lax.dot_general(
            part,
            keys_low[row_lag * KEY_BLOCK : (row_lag + 1) * KEY_BLOCK],
            dims,
            preferred_element_type=jnp.float32,
        )
    out_ref[0] = acc


def conv_logits(shifted_heads, terms, key_all):
    high, low = terms
    heads, row_count, contract = shifted_heads.shape
    seq_len, width = key_all.shape
    head_dim = width // heads
    windows = seq_len // KEY_BLOCK
    return pl.pallas_call(
        logits_kernel,
        grid=(heads, windows),
        in_specs=[
            pl.BlockSpec((1, row_count, contract), lambda h, n: (h, 0, 0)),
            pl.BlockSpec((1,) + high.shape[1:], lambda h, n: (h, 0, 0)),
            pl.BlockSpec((1,) + low.shape[1:], lambda h, n: (h, 0, 0)),
            pl.BlockSpec((KEY_BLOCK, head_dim), lambda h, n: (jnp.maximum(n - 1, 0), h)),
            pl.BlockSpec((KEY_BLOCK, head_dim), lambda h, n: (n, h)),
        ],
        out_specs=pl.BlockSpec((1, row_count, KEY_BLOCK), lambda h, n: (h, 0, n)),
        out_shape=jax.ShapeDtypeStruct((heads, row_count, seq_len), jnp.float32),
    )(shifted_heads, high, low, key_all, key_all)


def band_terms(query_rows, query_first, key_flat, score_kernel):
    row_lead = QCONV - 1
    heads = score_kernel.shape[0]
    ext_count = query_rows.shape[0]
    row_count = ext_count - row_lead
    near = lax.dynamic_slice_in_dim(key_flat, query_first + 4, ext_count + QCONV - 2, 0)
    query_heads = query_rows.reshape(ext_count, heads, -1).astype(jnp.float32)
    near_heads = near.reshape(near.shape[0], heads, -1).astype(jnp.float32)
    scale = query_heads.shape[2] ** (-0.5)
    diagonals = [
        jnp.sum(query_heads * near_heads[lag - 1 : lag - 1 + ext_count], axis=2) * scale
        for lag in range(1, QCONV)
    ]
    band = []
    for gap in range(QCONV - 1):
        acc = jnp.zeros((row_count, heads), jnp.float32)
        for row_lag in range(gap + 1, QCONV):
            for col_lag in range(row_lag - gap):
                lag = row_lag - col_lag - gap
                acc = acc - score_kernel[None, :, row_lag, col_lag] * diagonals[lag - 1][
                    row_lead - row_lag : row_lead - row_lag + row_count
                ]
        band.append(acc.T)
    return jnp.stack(band)


def attend_chunk(shifted, band, query_first, key_all, terms, value_heads, head_mixing):
    row_count, heads = shifted.shape[:2]
    seq_len = value_heads.shape[0]
    shifted_heads = jnp.transpose(shifted, (1, 0, 2, 3)).reshape((heads, row_count, -1))
    convolved = conv_logits(shifted_heads, terms, key_all)
    query_pos = query_first + lax.iota(jnp.int32, row_count)
    gap = query_pos[:, None] - lax.iota(jnp.int32, seq_len)[None, :]
    for lag in range(QCONV - 1):
        convolved = convolved + jnp.where(gap == lag, band[lag][:, :, None], 0.0)
    logits = jnp.where(gap >= 0, convolved, lowest)
    peak = jnp.max(logits, axis=2, keepdims=True)
    expd = jnp.exp(logits - peak)
    probabilities = expd / jnp.sum(expd, axis=2, keepdims=True)
    grouped = probabilities.reshape(heads // GROUP, GROUP, row_count, seq_len)
    weights = head_mixing.reshape(heads // GROUP, GROUP, GROUP)
    mixed_probs = jnp.zeros_like(grouped)
    for source in range(GROUP):
        mixed_probs = mixed_probs + weights[:, :, source, None, None] * grouped[:, source, None]
    mixed_probs = mixed_probs.reshape(heads, row_count, seq_len).astype(jnp.bfloat16)
    return jnp.einsum(
        "hik,khd->ihd", mixed_probs, value_heads, preferred_element_type=jnp.float32
    )


def normalize(weighted, gain_local):
    factor = lax.rsqrt(jnp.mean(weighted * weighted, axis=2, keepdims=True) + epsilon)
    return (
        (weighted * factor * gain_local[None]).astype(jnp.bfloat16).reshape(weighted.shape[0], -1)
    )


def shards(query_states, key_states, value_states, score_kernel, head_mixing, head_gain):
    groups = lax.axis_size("uly")
    stacked = jnp.stack([query_states, key_states, value_states])
    group_width = stacked.shape[2] // groups
    pieces = exchanged(
        lambda group: lax.dynamic_slice_in_dim(stacked, group * group_width, group_width, 2),
        "uly",
    )
    pieces = jnp.moveaxis(pieces, 0, 1)
    query_local, key_local, value_local = pieces.reshape(
        (pieces.shape[0], -1, pieces.shape[-1])
    )
    shard_rows = query_local.shape[0]
    width = query_local.shape[1]
    row_lead = QCONV - 1
    heads = score_kernel.shape[0]
    head_dim = width // heads
    ctx_place = lax.axis_index("ctx")
    query_first = ctx_place * shard_rows
    earlier = passed_along(query_local[shard_rows - row_lead :], "ctx", 1)
    query_ext = jnp.concatenate([earlier, query_local], axis=0)
    key_all = gathered(key_local, "ctx").reshape((-1, width))
    value_all = gathered(value_local, "ctx").reshape((-1, width))
    seq_len = key_all.shape[0]
    terms = toeplitz_terms(score_kernel, head_dim)
    edge = jnp.zeros((8, width), key_all.dtype)
    key_flat = jnp.concatenate([edge, key_all, edge], axis=0)
    band = band_terms(query_ext, query_first, key_flat, score_kernel)
    query_heads = query_ext.reshape(shard_rows + row_lead, heads, head_dim)
    shifted = jnp.stack(
        [query_heads[row_lead - lag : row_lead - lag + shard_rows] for lag in range(QCONV)], axis=2
    )
    value_heads = value_all.reshape(seq_len, heads, head_dim)
    chunk = min(ROW_CHUNK * KEY_BLOCK * 8 // seq_len, shard_rows)
    if chunk == shard_rows:
        weighted = attend_chunk(
            shifted, band, query_first, key_all, terms, value_heads, head_mixing
        )
    else:
        chunks = shard_rows // chunk

        def one_chunk(index):
            start = index * chunk
            return attend_chunk(
                lax.dynamic_slice_in_dim(shifted, start, chunk, 0),
                lax.dynamic_slice_in_dim(band, start, chunk, 2),
                query_first + start,
                key_all,
                terms,
                value_heads,
                head_mixing,
            )

        weighted = lax.map(one_chunk, jnp.arange(chunks, dtype=jnp.int32))
        weighted = weighted.reshape((shard_rows,) + weighted.shape[2:])
    gain_local = head_gain.reshape(heads, head_dim)
    attended = normalize(weighted, gain_local)
    block_rows = shard_rows // groups
    returned = exchanged(
        lambda group: lax.dynamic_slice_in_dim(attended, group * block_rows, block_rows, 0),
        "uly",
    )
    return jnp.moveaxis(returned, 0, 1).reshape((block_rows, -1))


def solution(mesh):
    placed = (
        P(("ctx", "uly"), None),
        P(("ctx", "uly"), None),
        P(("ctx", "uly"), None),
        P("uly", None, None),
        P("uly", None),
        P("uly"),
    )
    return jax.shard_map(
        shards, mesh=mesh, in_specs=placed, out_specs=P(("ctx", "uly"), None), check_vma=False
    )
```

```python
import jax
import jax.numpy as jnp
from jax import lax
from jax.experimental import pallas as pl
from jax.experimental.pallas import tpu as pltpu
from jax.sharding import PartitionSpec as P

GROUP = 4
QCONV = 6
KCONV = 11
KEY_BLOCK = 128
ROW_CHUNK = 128


lowest = -1e30
epsilon = 1e-06


def passed_along(shard, axis, by):
    peers = lax.axis_size(axis)
    pairs = [(i, i + by) for i in range(peers) if 0 <= i + by < peers]
    return lax.ppermute(shard, axis, pairs)


def split_bf16(values):
    high = lax.reduce_precision(values, exponent_bits=8, mantissa_bits=7)
    low = values - high
    return high.astype(jnp.bfloat16), low.astype(jnp.bfloat16)


def exchanged(pieces_of, axis):
    peers = lax.axis_size(axis)
    place = lax.axis_index(axis)
    received = [pieces_of(place)]
    for shift in range(1, peers):
        outgoing = pieces_of((place + shift) % peers)
        pairs = [(i, (i + shift) % peers) for i in range(peers)]
        received.append(lax.ppermute(outgoing, axis, pairs))
    order = (place - jnp.arange(peers, dtype=jnp.int32)) % peers
    return jnp.take(jnp.stack(received), order, axis=0)


def gathered(shard, axis):
    peers = lax.axis_size(axis)
    place = lax.axis_index(axis)
    if peers & (peers - 1):
        return lax.all_gather(shard, axis, axis=0, tiled=False)
    bits = peers.bit_length() - 1
    held = shard[None]
    for level in reversed(range(bits)):
        bit = 1 << level
        incoming = lax.ppermute(held, axis, [(i, i ^ bit) for i in range(peers)])
        upper = (place & bit) != 0
        held = jnp.where(
            upper,
            jnp.concatenate([incoming, held], axis=0),
            jnp.concatenate([held, incoming], axis=0),
        )
    held = held.reshape((2,) * bits + shard.shape)
    return jnp.transpose(held, tuple(reversed(range(bits))) + tuple(range(bits, held.ndim)))


def logits_kernel(taps_ref, query_ref, before_ref, current_ref, out_ref, high_ref, low_ref):
    head = pl.program_id(0)
    window = pl.program_id(1)

    @pl.when(window == 0)
    def _():
        lag = (
            lax.broadcasted_iota(jnp.int32, (2 * KEY_BLOCK, KEY_BLOCK), 1)
            + KEY_BLOCK
            - lax.broadcasted_iota(jnp.int32, (2 * KEY_BLOCK, KEY_BLOCK), 0)
        )
        for row_lag in range(QCONV):
            toeplitz = jnp.zeros(lag.shape, jnp.float32)
            for col_lag in range(KCONV):
                tap = taps_ref[(head * QCONV + row_lag) * KCONV + col_lag]
                toeplitz = jnp.where(lag == col_lag, tap, toeplitz)
            high = toeplitz.astype(jnp.bfloat16)
            low = (toeplitz - high.astype(jnp.float32)).astype(jnp.bfloat16)
            high_ref[:, row_lag * KEY_BLOCK : (row_lag + 1) * KEY_BLOCK] = high
            low_ref[:, row_lag * KEY_BLOCK : (row_lag + 1) * KEY_BLOCK] = low

    before = jnp.where(
        window > 0, before_ref[...], jnp.zeros(before_ref.shape, before_ref.dtype)
    )
    current = current_ref[...]
    conv_keys = (
        jnp.dot(before, high_ref[:KEY_BLOCK], preferred_element_type=jnp.float32)
        + jnp.dot(current, high_ref[KEY_BLOCK:], preferred_element_type=jnp.float32)
        + jnp.dot(before, low_ref[:KEY_BLOCK], preferred_element_type=jnp.float32)
        + jnp.dot(current, low_ref[KEY_BLOCK:], preferred_element_type=jnp.float32)
    )
    keys_high = conv_keys.astype(jnp.bfloat16)
    keys_low = (conv_keys - keys_high.astype(jnp.float32)).astype(jnp.bfloat16)
    query = query_ref[0]
    head_dim = current.shape[0]
    acc = jnp.zeros(out_ref.shape[1:], jnp.float32)
    for row_lag in range(QCONV):
        part = query[:, row_lag * head_dim : (row_lag + 1) * head_dim]
        cols = slice(row_lag * KEY_BLOCK, (row_lag + 1) * KEY_BLOCK)
        acc = acc + jnp.dot(part, keys_high[:, cols], preferred_element_type=jnp.float32)
        acc = acc + jnp.dot(part, keys_low[:, cols], preferred_element_type=jnp.float32)
    out_ref[0] = acc


def conv_logits(shifted_heads, score_kernel, keys_t):
    heads, row_count, contract = shifted_heads.shape
    width, seq_len = keys_t.shape
    head_dim = width // heads
    windows = seq_len // KEY_BLOCK
    taps = (score_kernel * head_dim ** (-0.5)).reshape(-1)
    return pl.pallas_call(
        logits_kernel,
        grid=(heads, windows),
        in_specs=[
            pl.BlockSpec(memory_space=pltpu.SMEM),
            pl.BlockSpec((1, row_count, contract), lambda h, n: (h, 0, 0)),
            pl.BlockSpec((head_dim, KEY_BLOCK), lambda h, n: (h, jnp.maximum(n - 1, 0))),
            pl.BlockSpec((head_dim, KEY_BLOCK), lambda h, n: (h, n)),
        ],
        out_specs=pl.BlockSpec((1, row_count, KEY_BLOCK), lambda h, n: (h, 0, n)),
        out_shape=jax.ShapeDtypeStruct((heads, row_count, seq_len), jnp.float32),
        scratch_shapes=[
            pltpu.VMEM((2 * KEY_BLOCK, QCONV * KEY_BLOCK), jnp.bfloat16),
            pltpu.VMEM((2 * KEY_BLOCK, QCONV * KEY_BLOCK), jnp.bfloat16),
        ],
    )(taps, shifted_heads, keys_t, keys_t)


def band_terms(query_rows, query_first, key_flat, score_kernel):
    row_lead = QCONV - 1
    heads = score_kernel.shape[0]
    ext_count = query_rows.shape[0]
    row_count = ext_count - row_lead
    near = lax.dynamic_slice_in_dim(key_flat, query_first + 4, ext_count + QCONV - 2, 0)
    query_heads = query_rows.reshape(ext_count, heads, -1).astype(jnp.float32)
    near_heads = near.reshape(near.shape[0], heads, -1).astype(jnp.float32)
    scale = query_heads.shape[2] ** (-0.5)
    diagonals = [
        jnp.sum(query_heads * near_heads[lag - 1 : lag - 1 + ext_count], axis=2) * scale
        for lag in range(1, QCONV)
    ]
    band = []
    for gap in range(QCONV - 1):
        acc = jnp.zeros((row_count, heads), jnp.float32)
        for row_lag in range(gap + 1, QCONV):
            for col_lag in range(row_lag - gap):
                lag = row_lag - col_lag - gap
                acc = acc - score_kernel[None, :, row_lag, col_lag] * diagonals[lag - 1][
                    row_lead - row_lag : row_lead - row_lag + row_count
                ]
        band.append(acc.T)
    return jnp.stack(band)


def attend_chunk(shifted, band, query_first, keys_t, score_kernel, value_heads, head_mixing):
    row_count, heads = shifted.shape[:2]
    seq_len = value_heads.shape[0]
    shifted_heads = jnp.transpose(shifted, (1, 0, 2, 3)).reshape((heads, row_count, -1))
    convolved = conv_logits(shifted_heads, score_kernel, keys_t)
    query_pos = query_first + lax.iota(jnp.int32, row_count)
    gap = query_pos[:, None] - lax.iota(jnp.int32, seq_len)[None, :]
    for lag in range(QCONV - 1):
        convolved = convolved + jnp.where(gap == lag, band[lag][:, :, None], 0.0)
    logits = jnp.where(gap >= 0, convolved, lowest)
    peak = jnp.max(logits, axis=2, keepdims=True)
    expd = jnp.exp(logits - peak)
    probabilities = expd / jnp.sum(expd, axis=2, keepdims=True)
    grouped = probabilities.reshape(heads // GROUP, GROUP, row_count, seq_len)
    weights = head_mixing.reshape(heads // GROUP, GROUP, GROUP)
    mixed_probs = jnp.zeros_like(grouped)
    for source in range(GROUP):
        mixed_probs = mixed_probs + weights[:, :, source, None, None] * grouped[:, source, None]
    mixed_probs = mixed_probs.reshape(heads, row_count, seq_len).astype(jnp.bfloat16)
    return jnp.einsum(
        "hik,khd->ihd", mixed_probs, value_heads, preferred_element_type=jnp.float32
    )


def normalize(weighted, gain_local):
    factor = lax.rsqrt(jnp.mean(weighted * weighted, axis=2, keepdims=True) + epsilon)
    return (
        (weighted * factor * gain_local[None]).astype(jnp.bfloat16).reshape(weighted.shape[0], -1)
    )


def shards(query_states, key_states, value_states, score_kernel, head_mixing, head_gain):
    groups = lax.axis_size("uly")
    stacked = jnp.stack([query_states, key_states, value_states])
    group_width = stacked.shape[2] // groups
    pieces = exchanged(
        lambda group: lax.dynamic_slice_in_dim(stacked, group * group_width, group_width, 2),
        "uly",
    )
    pieces = jnp.moveaxis(pieces, 0, 1)
    query_local, key_local, value_local = pieces.reshape(
        (pieces.shape[0], -1, pieces.shape[-1])
    )
    shard_rows = query_local.shape[0]
    width = query_local.shape[1]
    row_lead = QCONV - 1
    heads = score_kernel.shape[0]
    head_dim = width // heads
    ctx_place = lax.axis_index("ctx")
    query_first = ctx_place * shard_rows
    earlier = passed_along(query_local[shard_rows - row_lead :], "ctx", 1)
    query_ext = jnp.concatenate([earlier, query_local], axis=0)
    key_all = gathered(key_local, "ctx").reshape((-1, width))
    value_all = gathered(value_local, "ctx").reshape((-1, width))
    seq_len = key_all.shape[0]
    keys_t = key_all.T
    edge = jnp.zeros((8, width), key_all.dtype)
    key_flat = jnp.concatenate([edge, key_all, edge], axis=0)
    band = band_terms(query_ext, query_first, key_flat, score_kernel)
    query_heads = query_ext.reshape(shard_rows + row_lead, heads, head_dim)
    shifted = jnp.stack(
        [query_heads[row_lead - lag : row_lead - lag + shard_rows] for lag in range(QCONV)], axis=2
    )
    value_heads = value_all.reshape(seq_len, heads, head_dim)
    chunk = min(ROW_CHUNK * KEY_BLOCK * 8 // seq_len, shard_rows)
    if chunk == shard_rows:
        weighted = attend_chunk(
            shifted, band, query_first, keys_t, score_kernel, value_heads, head_mixing
        )
    else:
        chunks = shard_rows // chunk

        def one_chunk(index):
            start = index * chunk
            return attend_chunk(
                lax.dynamic_slice_in_dim(shifted, start, chunk, 0),
                lax.dynamic_slice_in_dim(band, start, chunk, 2),
                query_first + start,
                keys_t,
                score_kernel,
                value_heads,
                head_mixing,
            )

        weighted = lax.map(one_chunk, jnp.arange(chunks, dtype=jnp.int32))
        weighted = weighted.reshape((shard_rows,) + weighted.shape[2:])
    gain_local = head_gain.reshape(heads, head_dim)
    attended = normalize(weighted, gain_local)
    block_rows = shard_rows // groups
    returned = exchanged(
        lambda group: lax.dynamic_slice_in_dim(attended, group * block_rows, block_rows, 0),
        "uly",
    )
    return jnp.moveaxis(returned, 0, 1).reshape((block_rows, -1))


def solution(mesh):
    placed = (
        P(("ctx", "uly"), None),
        P(("ctx", "uly"), None),
        P(("ctx", "uly"), None),
        P("uly", None, None),
        P("uly", None),
        P("uly"),
    )
    return jax.shard_map(
        shards, mesh=mesh, in_specs=placed, out_specs=P(("ctx", "uly"), None), check_vma=False
    )
```

```python
import jax
import jax.numpy as jnp
from jax import lax
from jax.experimental import pallas as pl
from jax.experimental.pallas import tpu as pltpu
from jax.sharding import PartitionSpec as P

GROUP = 4
QCONV = 6
KCONV = 11
KEY_BLOCK = 128
KEY_SPAN = 1024
ROW_CHUNK = 128


lowest = -1e30
epsilon = 1e-06


def passed_along(shard, axis, by):
    peers = lax.axis_size(axis)
    pairs = [(i, i + by) for i in range(peers) if 0 <= i + by < peers]
    return lax.ppermute(shard, axis, pairs)


def exchanged(pieces_of, axis):
    peers = lax.axis_size(axis)
    place = lax.axis_index(axis)
    received = [pieces_of(place)]
    for shift in range(1, peers):
        outgoing = pieces_of((place + shift) % peers)
        pairs = [(i, (i + shift) % peers) for i in range(peers)]
        received.append(lax.ppermute(outgoing, axis, pairs))
    order = (place - jnp.arange(peers, dtype=jnp.int32)) % peers
    return jnp.take(jnp.stack(received), order, axis=0)


def gathered(shard, axis):
    peers = lax.axis_size(axis)
    place = lax.axis_index(axis)
    if peers & (peers - 1):
        return lax.all_gather(shard, axis, axis=0, tiled=False)
    bits = peers.bit_length() - 1
    held = shard[None]
    for level in reversed(range(bits)):
        bit = 1 << level
        incoming = lax.ppermute(held, axis, [(i, i ^ bit) for i in range(peers)])
        upper = (place & bit) != 0
        held = jnp.where(
            upper,
            jnp.concatenate([incoming, held], axis=0),
            jnp.concatenate([held, incoming], axis=0),
        )
    held = held.reshape((2,) * bits + shard.shape)
    return jnp.transpose(held, tuple(reversed(range(bits))) + tuple(range(bits, held.ndim)))


def logits_kernel(taps_ref, query_ref, keys_ref, out_ref, high_ref, low_ref, conv_ref):
    head = pl.program_id(0)
    group = pl.program_id(1)

    @pl.when(group == 0)
    def _():
        lag = (
            lax.broadcasted_iota(jnp.int32, (KEY_BLOCK, 2 * KEY_BLOCK), 0)
            + KEY_BLOCK
            - lax.broadcasted_iota(jnp.int32, (KEY_BLOCK, 2 * KEY_BLOCK), 1)
        )
        for row_lag in range(QCONV):
            toeplitz = jnp.zeros(lag.shape, jnp.float32)
            for col_lag in range(KCONV):
                tap = taps_ref[(head * QCONV + row_lag) * KCONV + col_lag]
                toeplitz = jnp.where(lag == col_lag, tap, toeplitz)
            high = toeplitz.astype(jnp.bfloat16)
            low = (toeplitz - high.astype(jnp.float32)).astype(jnp.bfloat16)
            high_ref[row_lag * KEY_BLOCK : (row_lag + 1) * KEY_BLOCK] = high
            low_ref[row_lag * KEY_BLOCK : (row_lag + 1) * KEY_BLOCK] = low

    blocks = conv_ref.shape[2] // KEY_BLOCK
    for block in range(blocks):
        start = pl.multiple_of((group * blocks + block) * KEY_BLOCK, KEY_BLOCK)
        window = keys_ref[pl.ds(start, 2 * KEY_BLOCK), :]
        conv_keys = jnp.dot(
            high_ref[...], window, preferred_element_type=jnp.float32
        ) + jnp.dot(low_ref[...], window, preferred_element_type=jnp.float32)
        keys_high = conv_keys.astype(jnp.bfloat16)
        keys_low = (conv_keys - keys_high.astype(jnp.float32)).astype(jnp.bfloat16)
        rows = slice(block * KEY_BLOCK, (block + 1) * KEY_BLOCK)
        for row_lag in range(QCONV):
            part = slice(row_lag * KEY_BLOCK, (row_lag + 1) * KEY_BLOCK)
            conv_ref[0, row_lag, rows] = keys_high[part]
            conv_ref[1, row_lag, rows] = keys_low[part]
    head_dim = keys_ref.shape[1]
    acc = jnp.zeros(out_ref.shape[1:], jnp.float32)
    for row_lag in range(QCONV):
        part = query_ref[0, row_lag * head_dim : (row_lag + 1) * head_dim, :]
        acc = acc + jnp.dot(conv_ref[0, row_lag], part, preferred_element_type=jnp.float32)
        acc = acc + jnp.dot(conv_ref[1, row_lag], part, preferred_element_type=jnp.float32)
    out_ref[0] = acc


def conv_logits(shifted_t, score_kernel, key_pad):
    heads, contract, row_count = shifted_t.shape
    seq_len = key_pad.shape[0] - KEY_BLOCK
    head_dim = key_pad.shape[1] // heads
    span = min(seq_len, KEY_SPAN)
    taps = (score_kernel * head_dim ** (-0.5)).reshape(-1)
    return pl.pallas_call(
        logits_kernel,
        grid=(heads, seq_len // span),
        in_specs=[
            pl.BlockSpec(memory_space=pltpu.SMEM),
            pl.BlockSpec((1, contract, row_count), lambda h, g: (h, 0, 0)),
            pl.BlockSpec((key_pad.shape[0], head_dim), lambda h, g: (0, h)),
        ],
        out_specs=pl.BlockSpec((1, span, row_count), lambda h, g: (h, g, 0)),
        out_shape=jax.ShapeDtypeStruct((heads, seq_len, row_count), jnp.float32),
        scratch_shapes=[
            pltpu.VMEM((QCONV * KEY_BLOCK, 2 * KEY_BLOCK), jnp.bfloat16),
            pltpu.VMEM((QCONV * KEY_BLOCK, 2 * KEY_BLOCK), jnp.bfloat16),
            pltpu.VMEM((2, QCONV, span, head_dim), jnp.bfloat16),
        ],
    )(taps, shifted_t, key_pad)


def band_terms(query_rows, query_first, key_flat, score_kernel):
    row_lead = QCONV - 1
    heads = score_kernel.shape[0]
    ext_count = query_rows.shape[0]
    row_count = ext_count - row_lead
    near = lax.dynamic_slice_in_dim(key_flat, query_first + 4, ext_count + QCONV - 2, 0)
    query_heads = query_rows.reshape(ext_count, heads, -1).astype(jnp.float32)
    near_heads = near.reshape(near.shape[0], heads, -1).astype(jnp.float32)
    scale = query_heads.shape[2] ** (-0.5)
    diagonals = [
        jnp.sum(query_heads * near_heads[lag - 1 : lag - 1 + ext_count], axis=2) * scale
        for lag in range(1, QCONV)
    ]
    band = []
    for gap in range(QCONV - 1):
        acc = jnp.zeros((row_count, heads), jnp.float32)
        for row_lag in range(gap + 1, QCONV):
            for col_lag in range(row_lag - gap):
                lag = row_lag - col_lag - gap
                acc = acc - score_kernel[None, :, row_lag, col_lag] * diagonals[lag - 1][
                    row_lead - row_lag : row_lead - row_lag + row_count
                ]
        band.append(acc.T)
    return jnp.stack(band)


def attend_chunk(shifted, band, query_first, key_pad, score_kernel, value_heads, head_mixing):
    row_count, heads = shifted.shape[:2]
    seq_len = value_heads.shape[0]
    shifted_t = jnp.transpose(shifted, (1, 2, 3, 0)).reshape((heads, -1, row_count))
    convolved = conv_logits(shifted_t, score_kernel, key_pad)
    query_pos = query_first + lax.iota(jnp.int32, row_count)
    gap = query_pos[None, :] - lax.iota(jnp.int32, seq_len)[:, None]
    for lag in range(QCONV - 1):
        convolved = convolved + jnp.where(gap == lag, band[lag][:, None, :], 0.0)
    logits = jnp.where(gap >= 0, convolved, lowest)
    peak = jnp.max(logits, axis=1, keepdims=True)
    expd = jnp.exp(logits - peak)
    probabilities = expd / jnp.sum(expd, axis=1, keepdims=True)
    grouped = probabilities.reshape(heads // GROUP, GROUP, seq_len, row_count)
    weights = head_mixing.reshape(heads // GROUP, GROUP, GROUP)
    mixed_probs = jnp.zeros_like(grouped)
    for source in range(GROUP):
        mixed_probs = mixed_probs + weights[:, :, source, None, None] * grouped[:, source, None]
    mixed_probs = mixed_probs.reshape(heads, seq_len, row_count).astype(jnp.bfloat16)
    return jnp.einsum(
        "hki,khd->ihd", mixed_probs, value_heads, preferred_element_type=jnp.float32
    )


def normalize(weighted, gain_local):
    factor = lax.rsqrt(jnp.mean(weighted * weighted, axis=2, keepdims=True) + epsilon)
    return (
        (weighted * factor * gain_local[None]).astype(jnp.bfloat16).reshape(weighted.shape[0], -1)
    )


def shards(query_states, key_states, value_states, score_kernel, head_mixing, head_gain):
    groups = lax.axis_size("uly")
    stacked = jnp.stack([query_states, key_states, value_states])
    group_width = stacked.shape[2] // groups
    pieces = exchanged(
        lambda group: lax.dynamic_slice_in_dim(stacked, group * group_width, group_width, 2),
        "uly",
    )
    pieces = jnp.moveaxis(pieces, 0, 1)
    query_local, key_local, value_local = pieces.reshape(
        (pieces.shape[0], -1, pieces.shape[-1])
    )
    shard_rows = query_local.shape[0]
    width = query_local.shape[1]
    row_lead = QCONV - 1
    heads = score_kernel.shape[0]
    head_dim = width // heads
    ctx_place = lax.axis_index("ctx")
    query_first = ctx_place * shard_rows
    earlier = passed_along(query_local[shard_rows - row_lead :], "ctx", 1)
    query_ext = jnp.concatenate([earlier, query_local], axis=0)
    key_all = gathered(key_local, "ctx").reshape((-1, width))
    value_all = gathered(value_local, "ctx").reshape((-1, width))
    seq_len = key_all.shape[0]
    key_pad = jnp.concatenate(
        [jnp.zeros((KEY_BLOCK, width), key_all.dtype), key_all], axis=0
    )
    edge = jnp.zeros((8, width), key_all.dtype)
    key_flat = jnp.concatenate([edge, key_all, edge], axis=0)
    band = band_terms(query_ext, query_first, key_flat, score_kernel)
    query_heads = query_ext.reshape(shard_rows + row_lead, heads, head_dim)
    shifted = jnp.stack(
        [query_heads[row_lead - lag : row_lead - lag + shard_rows] for lag in range(QCONV)], axis=2
    )
    value_heads = value_all.reshape(seq_len, heads, head_dim)
    chunk = min(ROW_CHUNK * KEY_BLOCK * 8 // seq_len, shard_rows)
    if chunk == shard_rows:
        weighted = attend_chunk(
            shifted, band, query_first, key_pad, score_kernel, value_heads, head_mixing
        )
    else:
        chunks = shard_rows // chunk

        def one_chunk(index):
            start = index * chunk
            return attend_chunk(
                lax.dynamic_slice_in_dim(shifted, start, chunk, 0),
                lax.dynamic_slice_in_dim(band, start, chunk, 2),
                query_first + start,
                key_pad,
                score_kernel,
                value_heads,
                head_mixing,
            )

        weighted = lax.map(one_chunk, jnp.arange(chunks, dtype=jnp.int32))
        weighted = weighted.reshape((shard_rows,) + weighted.shape[2:])
    gain_local = head_gain.reshape(heads, head_dim)
    attended = normalize(weighted, gain_local)
    block_rows = shard_rows // groups
    returned = exchanged(
        lambda group: lax.dynamic_slice_in_dim(attended, group * block_rows, block_rows, 0),
        "uly",
    )
    return jnp.moveaxis(returned, 0, 1).reshape((block_rows, -1))


def solution(mesh):
    placed = (
        P(("ctx", "uly"), None),
        P(("ctx", "uly"), None),
        P(("ctx", "uly"), None),
        P("uly", None, None),
        P("uly", None),
        P("uly"),
    )
    return jax.shard_map(
        shards, mesh=mesh, in_specs=placed, out_specs=P(("ctx", "uly"), None), check_vma=False
    )
```

```python
import jax
import jax.numpy as jnp
from jax import lax
from jax.experimental import pallas as pl
from jax.experimental.pallas import tpu as pltpu
from jax.sharding import PartitionSpec as P

GROUP = 4
QCONV = 6
KCONV = 11
KEY_BLOCK = 128
KEY_SPAN = 1024
ROW_CHUNK = 128


lowest = -1e30
epsilon = 1e-06


def passed_along(shard, axis, by):
    peers = lax.axis_size(axis)
    pairs = [(i, i + by) for i in range(peers) if 0 <= i + by < peers]
    return lax.ppermute(shard, axis, pairs)


def exchanged(pieces_of, axis):
    peers = lax.axis_size(axis)
    place = lax.axis_index(axis)
    received = [pieces_of(place)]
    for shift in range(1, peers):
        outgoing = pieces_of((place + shift) % peers)
        pairs = [(i, (i + shift) % peers) for i in range(peers)]
        received.append(lax.ppermute(outgoing, axis, pairs))
    order = (place - jnp.arange(peers, dtype=jnp.int32)) % peers
    return jnp.take(jnp.stack(received), order, axis=0)


def gathered(shard, axis):
    peers = lax.axis_size(axis)
    place = lax.axis_index(axis)
    if peers & (peers - 1):
        return lax.all_gather(shard, axis, axis=0, tiled=False)
    bits = peers.bit_length() - 1
    held = shard[None]
    for level in reversed(range(bits)):
        bit = 1 << level
        incoming = lax.ppermute(held, axis, [(i, i ^ bit) for i in range(peers)])
        upper = (place & bit) != 0
        held = jnp.where(
            upper,
            jnp.concatenate([incoming, held], axis=0),
            jnp.concatenate([held, incoming], axis=0),
        )
    held = held.reshape((2,) * bits + shard.shape)
    return jnp.transpose(held, tuple(reversed(range(bits))) + tuple(range(bits, held.ndim)))


def logits_kernel(taps_ref, query_ref, keys_ref, out_ref, high_ref, low_ref, conv_ref):
    head = pl.program_id(0)
    group = pl.program_id(1)

    @pl.when(group == 0)
    def _():
        lane = lax.broadcasted_iota(jnp.int32, (1, 2 * KEY_BLOCK), 1)
        for row_lag in range(QCONV):
            row = jnp.zeros(lane.shape, jnp.float32)
            for col_lag in range(KCONV):
                tap = taps_ref[(head * QCONV + row_lag) * KCONV + col_lag]
                row = jnp.where(lane == KEY_BLOCK - col_lag, tap, row)
            toeplitz = pltpu.roll(
                jnp.broadcast_to(row, (KEY_BLOCK, 2 * KEY_BLOCK)), 0, 1, stride=1, stride_axis=0
            )
            high = toeplitz.astype(jnp.bfloat16)
            low = (toeplitz - high.astype(jnp.float32)).astype(jnp.bfloat16)
            high_ref[row_lag * KEY_BLOCK : (row_lag + 1) * KEY_BLOCK] = high
            low_ref[row_lag * KEY_BLOCK : (row_lag + 1) * KEY_BLOCK] = low

    blocks = conv_ref.shape[2] // KEY_BLOCK
    for block in range(blocks):
        start = pl.multiple_of((group * blocks + block) * KEY_BLOCK, KEY_BLOCK)
        window = keys_ref[pl.ds(start, 2 * KEY_BLOCK), :]
        conv_keys = jnp.dot(
            high_ref[...], window, preferred_element_type=jnp.float32
        ) + jnp.dot(low_ref[...], window, preferred_element_type=jnp.float32)
        keys_high = conv_keys.astype(jnp.bfloat16)
        keys_low = (conv_keys - keys_high.astype(jnp.float32)).astype(jnp.bfloat16)
        rows = slice(block * KEY_BLOCK, (block + 1) * KEY_BLOCK)
        for row_lag in range(QCONV):
            part = slice(row_lag * KEY_BLOCK, (row_lag + 1) * KEY_BLOCK)
            conv_ref[0, row_lag, rows] = keys_high[part]
            conv_ref[1, row_lag, rows] = keys_low[part]
    head_dim = keys_ref.shape[1]
    acc = jnp.zeros(out_ref.shape[1:], jnp.float32)
    for row_lag in range(QCONV):
        part = query_ref[0, row_lag * head_dim : (row_lag + 1) * head_dim, :]
        acc = acc + jnp.dot(conv_ref[0, row_lag], part, preferred_element_type=jnp.float32)
        acc = acc + jnp.dot(conv_ref[1, row_lag], part, preferred_element_type=jnp.float32)
    out_ref[0] = acc


def conv_logits(shifted_t, score_kernel, key_pad):
    heads, contract, row_count = shifted_t.shape
    seq_len = key_pad.shape[0] - KEY_BLOCK
    head_dim = key_pad.shape[1] // heads
    span = min(seq_len, KEY_SPAN)
    taps = (score_kernel * head_dim ** (-0.5)).reshape(-1)
    return pl.pallas_call(
        logits_kernel,
        grid=(heads, seq_len // span),
        in_specs=[
            pl.BlockSpec(memory_space=pltpu.SMEM),
            pl.BlockSpec((1, contract, row_count), lambda h, g: (h, 0, 0)),
            pl.BlockSpec((key_pad.shape[0], head_dim), lambda h, g: (0, h)),
        ],
        out_specs=pl.BlockSpec((1, span, row_count), lambda h, g: (h, g, 0)),
        out_shape=jax.ShapeDtypeStruct((heads, seq_len, row_count), jnp.float32),
        scratch_shapes=[
            pltpu.VMEM((QCONV * KEY_BLOCK, 2 * KEY_BLOCK), jnp.bfloat16),
            pltpu.VMEM((QCONV * KEY_BLOCK, 2 * KEY_BLOCK), jnp.bfloat16),
            pltpu.VMEM((2, QCONV, span, head_dim), jnp.bfloat16),
        ],
    )(taps, shifted_t, key_pad)


def band_terms(query_rows, query_first, key_flat, score_kernel):
    row_lead = QCONV - 1
    heads = score_kernel.shape[0]
    ext_count = query_rows.shape[0]
    row_count = ext_count - row_lead
    near = lax.dynamic_slice_in_dim(key_flat, query_first + 4, ext_count + QCONV - 2, 0)
    query_heads = query_rows.reshape(ext_count, heads, -1).astype(jnp.float32)
    near_heads = near.reshape(near.shape[0], heads, -1).astype(jnp.float32)
    scale = query_heads.shape[2] ** (-0.5)
    diagonals = [
        jnp.sum(query_heads * near_heads[lag - 1 : lag - 1 + ext_count], axis=2) * scale
        for lag in range(1, QCONV)
    ]
    band = []
    for gap in range(QCONV - 1):
        acc = jnp.zeros((row_count, heads), jnp.float32)
        for row_lag in range(gap + 1, QCONV):
            for col_lag in range(row_lag - gap):
                lag = row_lag - col_lag - gap
                acc = acc - score_kernel[None, :, row_lag, col_lag] * diagonals[lag - 1][
                    row_lead - row_lag : row_lead - row_lag + row_count
                ]
        band.append(acc.T)
    return jnp.stack(band)


def attend_chunk(shifted, band, query_first, key_pad, score_kernel, value_heads, head_mixing):
    row_count, heads = shifted.shape[:2]
    seq_len = value_heads.shape[0]
    shifted_t = jnp.transpose(shifted, (1, 2, 3, 0)).reshape((heads, -1, row_count))
    convolved = conv_logits(shifted_t, score_kernel, key_pad)
    query_pos = query_first + lax.iota(jnp.int32, row_count)
    gap = query_pos[None, :] - lax.iota(jnp.int32, seq_len)[:, None]
    for lag in range(QCONV - 1):
        convolved = convolved + jnp.where(gap == lag, band[lag][:, None, :], 0.0)
    logits = jnp.where(gap >= 0, convolved, lowest)
    peak = jnp.max(logits, axis=1, keepdims=True)
    expd = jnp.exp(logits - peak)
    probabilities = expd / jnp.sum(expd, axis=1, keepdims=True)
    grouped = probabilities.reshape(heads // GROUP, GROUP, seq_len, row_count)
    weights = head_mixing.reshape(heads // GROUP, GROUP, GROUP)
    mixed_probs = jnp.zeros_like(grouped)
    for source in range(GROUP):
        mixed_probs = mixed_probs + weights[:, :, source, None, None] * grouped[:, source, None]
    mixed_probs = mixed_probs.reshape(heads, seq_len, row_count).astype(jnp.bfloat16)
    return jnp.einsum(
        "hki,khd->ihd", mixed_probs, value_heads, preferred_element_type=jnp.float32
    )


def normalize(weighted, gain_local):
    factor = lax.rsqrt(jnp.mean(weighted * weighted, axis=2, keepdims=True) + epsilon)
    return (
        (weighted * factor * gain_local[None]).astype(jnp.bfloat16).reshape(weighted.shape[0], -1)
    )


def shards(query_states, key_states, value_states, score_kernel, head_mixing, head_gain):
    groups = lax.axis_size("uly")
    stacked = jnp.stack([query_states, key_states, value_states])
    group_width = stacked.shape[2] // groups
    pieces = exchanged(
        lambda group: lax.dynamic_slice_in_dim(stacked, group * group_width, group_width, 2),
        "uly",
    )
    pieces = jnp.moveaxis(pieces, 0, 1)
    query_local, key_local, value_local = pieces.reshape(
        (pieces.shape[0], -1, pieces.shape[-1])
    )
    shard_rows = query_local.shape[0]
    width = query_local.shape[1]
    row_lead = QCONV - 1
    heads = score_kernel.shape[0]
    head_dim = width // heads
    ctx_place = lax.axis_index("ctx")
    query_first = ctx_place * shard_rows
    earlier = passed_along(query_local[shard_rows - row_lead :], "ctx", 1)
    query_ext = jnp.concatenate([earlier, query_local], axis=0)
    key_all = gathered(key_local, "ctx").reshape((-1, width))
    value_all = gathered(value_local, "ctx").reshape((-1, width))
    seq_len = key_all.shape[0]
    key_pad = jnp.concatenate(
        [jnp.zeros((KEY_BLOCK, width), key_all.dtype), key_all], axis=0
    )
    edge = jnp.zeros((8, width), key_all.dtype)
    key_flat = jnp.concatenate([edge, key_all, edge], axis=0)
    band = band_terms(query_ext, query_first, key_flat, score_kernel)
    query_heads = query_ext.reshape(shard_rows + row_lead, heads, head_dim)
    shifted = jnp.stack(
        [query_heads[row_lead - lag : row_lead - lag + shard_rows] for lag in range(QCONV)], axis=2
    )
    value_heads = value_all.reshape(seq_len, heads, head_dim)
    chunk = min(ROW_CHUNK * KEY_BLOCK * 8 // seq_len, shard_rows)
    if chunk == shard_rows:
        weighted = attend_chunk(
            shifted, band, query_first, key_pad, score_kernel, value_heads, head_mixing
        )
    else:
        chunks = shard_rows // chunk

        def one_chunk(index):
            start = index * chunk
            return attend_chunk(
                lax.dynamic_slice_in_dim(shifted, start, chunk, 0),
                lax.dynamic_slice_in_dim(band, start, chunk, 2),
                query_first + start,
                key_pad,
                score_kernel,
                value_heads,
                head_mixing,
            )

        weighted = lax.map(one_chunk, jnp.arange(chunks, dtype=jnp.int32))
        weighted = weighted.reshape((shard_rows,) + weighted.shape[2:])
    gain_local = head_gain.reshape(heads, head_dim)
    attended = normalize(weighted, gain_local)
    block_rows = shard_rows // groups
    returned = exchanged(
        lambda group: lax.dynamic_slice_in_dim(attended, group * block_rows, block_rows, 0),
        "uly",
    )
    return jnp.moveaxis(returned, 0, 1).reshape((block_rows, -1))


def solution(mesh):
    placed = (
        P(("ctx", "uly"), None),
        P(("ctx", "uly"), None),
        P(("ctx", "uly"), None),
        P("uly", None, None),
        P("uly", None),
        P("uly"),
    )
    return jax.shard_map(
        shards, mesh=mesh, in_specs=placed, out_specs=P(("ctx", "uly"), None), check_vma=False
    )
```

```python
import jax
import jax.numpy as jnp
from jax import lax
from jax.experimental import pallas as pl
from jax.experimental.pallas import tpu as pltpu
from jax.sharding import PartitionSpec as P

GROUP = 4
QCONV = 6
KCONV = 11
KEY_BLOCK = 128
KEY_SPAN = 1024
ROW_CHUNK = 128


lowest = -1e30
epsilon = 1e-06


def passed_along(shard, axis, by):
    peers = lax.axis_size(axis)
    pairs = [(i, i + by) for i in range(peers) if 0 <= i + by < peers]
    return lax.ppermute(shard, axis, pairs)


def exchanged(pieces_of, axis):
    peers = lax.axis_size(axis)
    place = lax.axis_index(axis)
    received = [pieces_of(place)]
    for shift in range(1, peers):
        outgoing = pieces_of((place + shift) % peers)
        pairs = [(i, (i + shift) % peers) for i in range(peers)]
        received.append(lax.ppermute(outgoing, axis, pairs))
    order = (place - jnp.arange(peers, dtype=jnp.int32)) % peers
    return jnp.take(jnp.stack(received), order, axis=0)


def gathered(shard, axis):
    peers = lax.axis_size(axis)
    place = lax.axis_index(axis)
    if peers & (peers - 1):
        return lax.all_gather(shard, axis, axis=0, tiled=False)
    bits = peers.bit_length() - 1
    held = shard[None]
    for level in reversed(range(bits)):
        bit = 1 << level
        incoming = lax.ppermute(held, axis, [(i, i ^ bit) for i in range(peers)])
        upper = (place & bit) != 0
        held = jnp.where(
            upper,
            jnp.concatenate([incoming, held], axis=0),
            jnp.concatenate([held, incoming], axis=0),
        )
    held = held.reshape((2,) * bits + shard.shape)
    return jnp.transpose(held, tuple(reversed(range(bits))) + tuple(range(bits, held.ndim)))


def logits_kernel(taps_ref, query_ref, keys_ref, out_ref, high_ref, low_ref, conv_ref):
    head = pl.program_id(0)
    group = pl.program_id(1)
    edge = 16

    @pl.when(group == 0)
    def _():
        lane = lax.broadcasted_iota(jnp.int32, (1, 2 * KEY_BLOCK), 1)
        for row_lag in range(QCONV):
            row = jnp.zeros(lane.shape, jnp.float32)
            for col_lag in range(KCONV):
                tap = taps_ref[(head * QCONV + row_lag) * KCONV + col_lag]
                row = jnp.where(lane == KEY_BLOCK - col_lag, tap, row)
            toeplitz = pltpu.roll(
                jnp.broadcast_to(row, (KEY_BLOCK, 2 * KEY_BLOCK)), 0, 1, stride=1, stride_axis=0
            )
            high = toeplitz.astype(jnp.bfloat16)
            low = (toeplitz - high.astype(jnp.float32)).astype(jnp.bfloat16)
            high_ref[row_lag * KEY_BLOCK : (row_lag + 1) * KEY_BLOCK] = high[:, KEY_BLOCK:]
            low_ref[row_lag * KEY_BLOCK : (row_lag + 1) * KEY_BLOCK] = low[:, KEY_BLOCK:]
            top = QCONV * KEY_BLOCK + row_lag * edge
            high_ref[top : top + edge] = high[:edge, :KEY_BLOCK]
            low_ref[top : top + edge] = low[:edge, :KEY_BLOCK]

    blocks = conv_ref.shape[1] // KEY_BLOCK
    body = QCONV * KEY_BLOCK
    for block in range(blocks):
        start = pl.multiple_of((group * blocks + block) * KEY_BLOCK, KEY_BLOCK)
        before = keys_ref[pl.ds(start, KEY_BLOCK), :]
        current = keys_ref[pl.ds(start + KEY_BLOCK, KEY_BLOCK), :]
        conv_body = jnp.dot(
            high_ref[:body], current, preferred_element_type=jnp.float32
        ) + jnp.dot(low_ref[:body], current, preferred_element_type=jnp.float32)
        conv_top = jnp.dot(
            high_ref[body:], before, preferred_element_type=jnp.float32
        ) + jnp.dot(low_ref[body:], before, preferred_element_type=jnp.float32)
        base = block * KEY_BLOCK
        for row_lag in range(QCONV):
            first = row_lag * KEY_BLOCK
            head_rows = conv_body[first : first + edge] + conv_top[
                row_lag * edge : (row_lag + 1) * edge
            ]
            rest_rows = conv_body[first + edge : first + KEY_BLOCK]
            cols = slice(row_lag * KEY_BLOCK, (row_lag + 1) * KEY_BLOCK)
            for part, rows in ((head_rows, slice(base, base + edge)),
                               (rest_rows, slice(base + edge, base + KEY_BLOCK))):
                part_high = part.astype(jnp.bfloat16)
                part_low = (part - part_high.astype(jnp.float32)).astype(jnp.bfloat16)
                conv_ref[0, rows, cols] = part_high
                conv_ref[1, rows, cols] = part_low
    query = query_ref[0]
    out_ref[0] = jnp.dot(conv_ref[0], query, preferred_element_type=jnp.float32) + jnp.dot(
        conv_ref[1], query, preferred_element_type=jnp.float32
    )


def conv_logits(shifted_t, score_kernel, key_pad):
    heads, contract, row_count = shifted_t.shape
    seq_len = key_pad.shape[0] - KEY_BLOCK
    head_dim = key_pad.shape[1] // heads
    span = min(seq_len, KEY_SPAN)
    taps = (score_kernel * head_dim ** (-0.5)).reshape(-1)
    return pl.pallas_call(
        logits_kernel,
        grid=(heads, seq_len // span),
        in_specs=[
            pl.BlockSpec(memory_space=pltpu.SMEM),
            pl.BlockSpec((1, contract, row_count), lambda h, g: (h, 0, 0)),
            pl.BlockSpec((key_pad.shape[0], head_dim), lambda h, g: (0, h)),
        ],
        out_specs=pl.BlockSpec((1, span, row_count), lambda h, g: (h, g, 0)),
        out_shape=jax.ShapeDtypeStruct((heads, seq_len, row_count), jnp.float32),
        scratch_shapes=[
            pltpu.VMEM((QCONV * (KEY_BLOCK + 16), KEY_BLOCK), jnp.bfloat16),
            pltpu.VMEM((QCONV * (KEY_BLOCK + 16), KEY_BLOCK), jnp.bfloat16),
            pltpu.VMEM((2, span, QCONV * head_dim), jnp.bfloat16),
        ],
    )(taps, shifted_t, key_pad)


def band_terms(query_rows, query_first, key_flat, score_kernel):
    row_lead = QCONV - 1
    heads = score_kernel.shape[0]
    ext_count = query_rows.shape[0]
    row_count = ext_count - row_lead
    near = lax.dynamic_slice_in_dim(key_flat, query_first + 4, ext_count + QCONV - 2, 0)
    query_heads = query_rows.reshape(ext_count, heads, -1).astype(jnp.float32)
    near_heads = near.reshape(near.shape[0], heads, -1).astype(jnp.float32)
    scale = query_heads.shape[2] ** (-0.5)
    diagonals = [
        jnp.sum(query_heads * near_heads[lag - 1 : lag - 1 + ext_count], axis=2) * scale
        for lag in range(1, QCONV)
    ]
    band = []
    for gap in range(QCONV - 1):
        acc = jnp.zeros((row_count, heads), jnp.float32)
        for row_lag in range(gap + 1, QCONV):
            for col_lag in range(row_lag - gap):
                lag = row_lag - col_lag - gap
                acc = acc - score_kernel[None, :, row_lag, col_lag] * diagonals[lag - 1][
                    row_lead - row_lag : row_lead - row_lag + row_count
                ]
        band.append(acc.T)
    return jnp.stack(band)


def attend_chunk(shifted, band, query_first, key_pad, score_kernel, value_heads, head_mixing):
    row_count, heads = shifted.shape[:2]
    seq_len = value_heads.shape[0]
    shifted_t = jnp.transpose(shifted, (1, 2, 3, 0)).reshape((heads, -1, row_count))
    convolved = conv_logits(shifted_t, score_kernel, key_pad)
    query_pos = query_first + lax.iota(jnp.int32, row_count)
    gap = query_pos[None, :] - lax.iota(jnp.int32, seq_len)[:, None]
    for lag in range(QCONV - 1):
        convolved = convolved + jnp.where(gap == lag, band[lag][:, None, :], 0.0)
    logits = jnp.where(gap >= 0, convolved, lowest)
    peak = jnp.max(logits, axis=1, keepdims=True)
    expd = jnp.exp(logits - peak)
    probabilities = expd / jnp.sum(expd, axis=1, keepdims=True)
    grouped = probabilities.reshape(heads // GROUP, GROUP, seq_len, row_count)
    weights = head_mixing.reshape(heads // GROUP, GROUP, GROUP)
    mixed_probs = jnp.zeros_like(grouped)
    for source in range(GROUP):
        mixed_probs = mixed_probs + weights[:, :, source, None, None] * grouped[:, source, None]
    mixed_probs = mixed_probs.reshape(heads, seq_len, row_count).astype(jnp.bfloat16)
    return jnp.einsum(
        "hki,khd->ihd", mixed_probs, value_heads, preferred_element_type=jnp.float32
    )


def normalize(weighted, gain_local):
    factor = lax.rsqrt(jnp.mean(weighted * weighted, axis=2, keepdims=True) + epsilon)
    return (
        (weighted * factor * gain_local[None]).astype(jnp.bfloat16).reshape(weighted.shape[0], -1)
    )


def shards(query_states, key_states, value_states, score_kernel, head_mixing, head_gain):
    groups = lax.axis_size("uly")
    stacked = jnp.stack([query_states, key_states, value_states])
    group_width = stacked.shape[2] // groups
    pieces = exchanged(
        lambda group: lax.dynamic_slice_in_dim(stacked, group * group_width, group_width, 2),
        "uly",
    )
    pieces = jnp.moveaxis(pieces, 0, 1)
    query_local, key_local, value_local = pieces.reshape(
        (pieces.shape[0], -1, pieces.shape[-1])
    )
    shard_rows = query_local.shape[0]
    width = query_local.shape[1]
    row_lead = QCONV - 1
    heads = score_kernel.shape[0]
    head_dim = width // heads
    ctx_place = lax.axis_index("ctx")
    query_first = ctx_place * shard_rows
    earlier = passed_along(query_local[shard_rows - row_lead :], "ctx", 1)
    query_ext = jnp.concatenate([earlier, query_local], axis=0)
    key_all = gathered(key_local, "ctx").reshape((-1, width))
    value_all = gathered(value_local, "ctx").reshape((-1, width))
    seq_len = key_all.shape[0]
    key_pad = jnp.concatenate(
        [jnp.zeros((KEY_BLOCK, width), key_all.dtype), key_all], axis=0
    )
    edge = jnp.zeros((8, width), key_all.dtype)
    key_flat = jnp.concatenate([edge, key_all, edge], axis=0)
    band = band_terms(query_ext, query_first, key_flat, score_kernel)
    query_heads = query_ext.reshape(shard_rows + row_lead, heads, head_dim)
    shifted = jnp.stack(
        [query_heads[row_lead - lag : row_lead - lag + shard_rows] for lag in range(QCONV)], axis=2
    )
    value_heads = value_all.reshape(seq_len, heads, head_dim)
    chunk = min(ROW_CHUNK * KEY_BLOCK * 8 // seq_len, shard_rows)
    if chunk == shard_rows:
        weighted = attend_chunk(
            shifted, band, query_first, key_pad, score_kernel, value_heads, head_mixing
        )
    else:
        chunks = shard_rows // chunk

        def one_chunk(index):
            start = index * chunk
            return attend_chunk(
                lax.dynamic_slice_in_dim(shifted, start, chunk, 0),
                lax.dynamic_slice_in_dim(band, start, chunk, 2),
                query_first + start,
                key_pad,
                score_kernel,
                value_heads,
                head_mixing,
            )

        weighted = lax.map(one_chunk, jnp.arange(chunks, dtype=jnp.int32))
        weighted = weighted.reshape((shard_rows,) + weighted.shape[2:])
    gain_local = head_gain.reshape(heads, head_dim)
    attended = normalize(weighted, gain_local)
    block_rows = shard_rows // groups
    returned = exchanged(
        lambda group: lax.dynamic_slice_in_dim(attended, group * block_rows, block_rows, 0),
        "uly",
    )
    return jnp.moveaxis(returned, 0, 1).reshape((block_rows, -1))


def solution(mesh):
    placed = (
        P(("ctx", "uly"), None),
        P(("ctx", "uly"), None),
        P(("ctx", "uly"), None),
        P("uly", None, None),
        P("uly", None),
        P("uly"),
    )
    return jax.shard_map(
        shards, mesh=mesh, in_specs=placed, out_specs=P(("ctx", "uly"), None), check_vma=False
    )
```

```python
import jax
import jax.numpy as jnp
from jax import lax
from jax.experimental import pallas as pl
from jax.experimental.pallas import tpu as pltpu
from jax.sharding import PartitionSpec as P

GROUP = 4
QCONV = 6
KCONV = 11
KEY_BLOCK = 128
KEY_SPAN = 1024
ROW_CHUNK = 128


lowest = -1e30
epsilon = 1e-06


def passed_along(shard, axis, by):
    peers = lax.axis_size(axis)
    pairs = [(i, i + by) for i in range(peers) if 0 <= i + by < peers]
    return lax.ppermute(shard, axis, pairs)


def exchanged(pieces_of, axis):
    peers = lax.axis_size(axis)
    place = lax.axis_index(axis)
    received = [pieces_of(place)]
    for shift in range(1, peers):
        outgoing = pieces_of((place + shift) % peers)
        pairs = [(i, (i + shift) % peers) for i in range(peers)]
        received.append(lax.ppermute(outgoing, axis, pairs))
    order = (place - jnp.arange(peers, dtype=jnp.int32)) % peers
    return jnp.take(jnp.stack(received), order, axis=0)


def gathered(shard, axis):
    peers = lax.axis_size(axis)
    place = lax.axis_index(axis)
    if peers & (peers - 1):
        return lax.all_gather(shard, axis, axis=0, tiled=False)
    bits = peers.bit_length() - 1
    held = shard[None]
    for level in reversed(range(bits)):
        bit = 1 << level
        incoming = lax.ppermute(held, axis, [(i, i ^ bit) for i in range(peers)])
        upper = (place & bit) != 0
        held = jnp.where(
            upper,
            jnp.concatenate([incoming, held], axis=0),
            jnp.concatenate([held, incoming], axis=0),
        )
    held = held.reshape((2,) * bits + shard.shape)
    return jnp.transpose(held, tuple(reversed(range(bits))) + tuple(range(bits, held.ndim)))


def logits_kernel(taps_ref, query_ref, keys_ref, out_ref, high_ref, low_ref, conv_ref):
    head = pl.program_id(0)
    group = pl.program_id(1)
    edge = 16

    @pl.when(group == 0)
    def _():
        lane = lax.broadcasted_iota(jnp.int32, (1, 2 * KEY_BLOCK), 1)
        for row_lag in range(QCONV):
            row = jnp.zeros(lane.shape, jnp.float32)
            for col_lag in range(KCONV):
                tap = taps_ref[(head * QCONV + row_lag) * KCONV + col_lag]
                row = jnp.where(lane == KEY_BLOCK - col_lag, tap, row)
            toeplitz = pltpu.roll(
                jnp.broadcast_to(row, (KEY_BLOCK, 2 * KEY_BLOCK)), 0, 1, stride=1, stride_axis=0
            )
            high = toeplitz.astype(jnp.bfloat16)
            low = (toeplitz - high.astype(jnp.float32)).astype(jnp.bfloat16)
            high_ref[row_lag * KEY_BLOCK : (row_lag + 1) * KEY_BLOCK] = high[:, KEY_BLOCK:]
            low_ref[row_lag * KEY_BLOCK : (row_lag + 1) * KEY_BLOCK] = low[:, KEY_BLOCK:]
            top = QCONV * KEY_BLOCK + row_lag * edge
            high_ref[top : top + edge] = high[:edge, :KEY_BLOCK]
            low_ref[top : top + edge] = low[:edge, :KEY_BLOCK]

    blocks = conv_ref.shape[1] // KEY_BLOCK
    body = QCONV * KEY_BLOCK
    for block in range(blocks):
        start = pl.multiple_of((group * blocks + block) * KEY_BLOCK, KEY_BLOCK)
        before = keys_ref[pl.ds(start, KEY_BLOCK), :]
        current = keys_ref[pl.ds(start + KEY_BLOCK, KEY_BLOCK), :]
        conv_body = jnp.dot(
            high_ref[:body], current, preferred_element_type=jnp.float32
        ) + jnp.dot(low_ref[:body], current, preferred_element_type=jnp.float32)
        conv_top = jnp.dot(
            high_ref[body:], before, preferred_element_type=jnp.float32
        ) + jnp.dot(low_ref[body:], before, preferred_element_type=jnp.float32)
        base = block * KEY_BLOCK
        for row_lag in range(QCONV):
            first = row_lag * KEY_BLOCK
            head_rows = conv_body[first : first + edge] + conv_top[
                row_lag * edge : (row_lag + 1) * edge
            ]
            rest_rows = conv_body[first + edge : first + KEY_BLOCK]
            cols = slice(row_lag * KEY_BLOCK, (row_lag + 1) * KEY_BLOCK)
            for part, rows in ((head_rows, slice(base, base + edge)),
                               (rest_rows, slice(base + edge, base + KEY_BLOCK))):
                part_high = part.astype(jnp.bfloat16)
                part_low = (part - part_high.astype(jnp.float32)).astype(jnp.bfloat16)
                conv_ref[0, rows, cols] = part_high
                conv_ref[1, rows, cols] = part_low
    query = query_ref[0]
    out_ref[0] = jnp.dot(conv_ref[0], query, preferred_element_type=jnp.float32) + jnp.dot(
        conv_ref[1], query, preferred_element_type=jnp.float32
    )


def conv_logits(shifted_t, score_kernel, key_pad):
    heads, contract, row_count = shifted_t.shape
    seq_len = key_pad.shape[0] - KEY_BLOCK
    head_dim = key_pad.shape[1] // heads
    span = min(seq_len, KEY_SPAN)
    taps = (score_kernel * head_dim ** (-0.5)).reshape(-1)
    return pl.pallas_call(
        logits_kernel,
        grid=(heads, seq_len // span),
        in_specs=[
            pl.BlockSpec(memory_space=pltpu.SMEM),
            pl.BlockSpec((1, contract, row_count), lambda h, g: (h, 0, 0)),
            pl.BlockSpec((key_pad.shape[0], head_dim), lambda h, g: (0, h)),
        ],
        out_specs=pl.BlockSpec((1, span, row_count), lambda h, g: (h, g, 0)),
        out_shape=jax.ShapeDtypeStruct((heads, seq_len, row_count), jnp.float32),
        scratch_shapes=[
            pltpu.VMEM((QCONV * (KEY_BLOCK + 16), KEY_BLOCK), jnp.bfloat16),
            pltpu.VMEM((QCONV * (KEY_BLOCK + 16), KEY_BLOCK), jnp.bfloat16),
            pltpu.VMEM((2, span, QCONV * head_dim), jnp.bfloat16),
        ],
    )(taps, shifted_t, key_pad)


def band_terms(query_rows, query_first, key_flat, score_kernel):
    row_lead = QCONV - 1
    heads = score_kernel.shape[0]
    ext_count = query_rows.shape[0]
    row_count = ext_count - row_lead
    near = lax.dynamic_slice_in_dim(key_flat, query_first + 4, ext_count + QCONV - 2, 0)
    query_heads = query_rows.reshape(ext_count, heads, -1).astype(jnp.float32)
    near_heads = near.reshape(near.shape[0], heads, -1).astype(jnp.float32)
    scale = query_heads.shape[2] ** (-0.5)
    diagonals = [
        jnp.sum(query_heads * near_heads[lag - 1 : lag - 1 + ext_count], axis=2) * scale
        for lag in range(1, QCONV)
    ]
    band = []
    for gap in range(QCONV - 1):
        acc = jnp.zeros((row_count, heads), jnp.float32)
        for row_lag in range(gap + 1, QCONV):
            for col_lag in range(row_lag - gap):
                lag = row_lag - col_lag - gap
                acc = acc - score_kernel[None, :, row_lag, col_lag] * diagonals[lag - 1][
                    row_lead - row_lag : row_lead - row_lag + row_count
                ]
        band.append(acc.T)
    return jnp.stack(band)


def attend_chunk(shifted, band, query_first, key_pad, score_kernel, value_heads, head_mixing):
    row_count, heads = shifted.shape[:2]
    seq_len = value_heads.shape[0]
    shifted_t = jnp.transpose(shifted, (1, 2, 3, 0)).reshape((heads, -1, row_count))
    convolved = conv_logits(shifted_t, score_kernel, key_pad)
    query_pos = query_first + lax.iota(jnp.int32, row_count)
    gap = query_pos[None, :] - lax.iota(jnp.int32, seq_len)[:, None]
    for lag in range(QCONV - 1):
        convolved = convolved + jnp.where(gap == lag, band[lag][:, None, :], 0.0)
    logits = jnp.where(gap >= 0, convolved, lowest)
    peak = jnp.max(logits, axis=1, keepdims=True)
    expd = jnp.exp(logits - peak)
    probabilities = expd / jnp.sum(expd, axis=1, keepdims=True)
    grouped = probabilities.reshape(heads // GROUP, GROUP, seq_len, row_count)
    weights = head_mixing.reshape(heads // GROUP, GROUP, GROUP)
    mixed_probs = jnp.zeros_like(grouped)
    for source in range(GROUP):
        mixed_probs = mixed_probs + weights[:, :, source, None, None] * grouped[:, source, None]
    mixed_probs = mixed_probs.reshape(heads, seq_len, row_count).astype(jnp.bfloat16)
    return jnp.einsum(
        "hki,khd->ihd", mixed_probs, value_heads, preferred_element_type=jnp.float32
    )


def normalize(weighted, gain_local):
    factor = lax.rsqrt(jnp.mean(weighted * weighted, axis=2, keepdims=True) + epsilon)
    return (
        (weighted * factor * gain_local[None]).astype(jnp.bfloat16).reshape(weighted.shape[0], -1)
    )


def shards(query_states, key_states, value_states, score_kernel, head_mixing, head_gain):
    groups = lax.axis_size("uly")
    stacked = jnp.stack([query_states, key_states, value_states])
    group_width = stacked.shape[2] // groups
    pieces = exchanged(
        lambda group: lax.dynamic_slice_in_dim(stacked, group * group_width, group_width, 2),
        "uly",
    )
    pieces = jnp.moveaxis(pieces, 0, 1)
    query_local, key_local, value_local = pieces.reshape(
        (pieces.shape[0], -1, pieces.shape[-1])
    )
    shard_rows = query_local.shape[0]
    width = query_local.shape[1]
    row_lead = QCONV - 1
    heads = score_kernel.shape[0]
    head_dim = width // heads
    ctx_place = lax.axis_index("ctx")
    query_first = ctx_place * shard_rows
    earlier = passed_along(query_local[shard_rows - row_lead :], "ctx", 1)
    query_ext = jnp.concatenate([earlier, query_local], axis=0)
    key_all = gathered(key_local, "ctx").reshape((-1, width))
    key_all, value_local = lax.optimization_barrier((key_all, value_local))
    value_all = gathered(value_local, "ctx").reshape((-1, width))
    seq_len = key_all.shape[0]
    key_pad = jnp.concatenate(
        [jnp.zeros((KEY_BLOCK, width), key_all.dtype), key_all], axis=0
    )
    edge = jnp.zeros((8, width), key_all.dtype)
    key_flat = jnp.concatenate([edge, key_all, edge], axis=0)
    band = band_terms(query_ext, query_first, key_flat, score_kernel)
    query_heads = query_ext.reshape(shard_rows + row_lead, heads, head_dim)
    shifted = jnp.stack(
        [query_heads[row_lead - lag : row_lead - lag + shard_rows] for lag in range(QCONV)], axis=2
    )
    value_heads = value_all.reshape(seq_len, heads, head_dim)
    chunk = min(ROW_CHUNK * KEY_BLOCK * 8 // seq_len, shard_rows)
    if chunk == shard_rows:
        weighted = attend_chunk(
            shifted, band, query_first, key_pad, score_kernel, value_heads, head_mixing
        )
    else:
        chunks = shard_rows // chunk

        def one_chunk(index):
            start = index * chunk
            return attend_chunk(
                lax.dynamic_slice_in_dim(shifted, start, chunk, 0),
                lax.dynamic_slice_in_dim(band, start, chunk, 2),
                query_first + start,
                key_pad,
                score_kernel,
                value_heads,
                head_mixing,
            )

        weighted = lax.map(one_chunk, jnp.arange(chunks, dtype=jnp.int32))
        weighted = weighted.reshape((shard_rows,) + weighted.shape[2:])
    gain_local = head_gain.reshape(heads, head_dim)
    attended = normalize(weighted, gain_local)
    block_rows = shard_rows // groups
    returned = exchanged(
        lambda group: lax.dynamic_slice_in_dim(attended, group * block_rows, block_rows, 0),
        "uly",
    )
    return jnp.moveaxis(returned, 0, 1).reshape((block_rows, -1))


def solution(mesh):
    placed = (
        P(("ctx", "uly"), None),
        P(("ctx", "uly"), None),
        P(("ctx", "uly"), None),
        P("uly", None, None),
        P("uly", None),
        P("uly"),
    )
    return jax.shard_map(
        shards, mesh=mesh, in_specs=placed, out_specs=P(("ctx", "uly"), None), check_vma=False
    )
```

```python
import jax
import jax.numpy as jnp
from jax import lax
from jax.experimental import pallas as pl
from jax.experimental.pallas import tpu as pltpu
from jax.sharding import PartitionSpec as P

GROUP = 4
QCONV = 6
KCONV = 11
KEY_BLOCK = 128
KEY_SPAN = 1024
CAUSAL_PEERS = 8
ROW_CHUNK = 128


lowest = -1e30
epsilon = 1e-06


def passed_along(shard, axis, by):
    peers = lax.axis_size(axis)
    pairs = [(i, i + by) for i in range(peers) if 0 <= i + by < peers]
    return lax.ppermute(shard, axis, pairs)


def exchanged(pieces_of, axis):
    peers = lax.axis_size(axis)
    place = lax.axis_index(axis)
    received = [pieces_of(place)]
    for shift in range(1, peers):
        outgoing = pieces_of((place + shift) % peers)
        pairs = [(i, (i + shift) % peers) for i in range(peers)]
        received.append(lax.ppermute(outgoing, axis, pairs))
    order = (place - jnp.arange(peers, dtype=jnp.int32)) % peers
    return jnp.take(jnp.stack(received), order, axis=0)


def gathered(shard, axis):
    peers = lax.axis_size(axis)
    place = lax.axis_index(axis)
    if peers & (peers - 1):
        return lax.all_gather(shard, axis, axis=0, tiled=False)
    bits = peers.bit_length() - 1
    held = shard[None]
    for level in reversed(range(bits)):
        bit = 1 << level
        incoming = lax.ppermute(held, axis, [(i, i ^ bit) for i in range(peers)])
        upper = (place & bit) != 0
        held = jnp.where(
            upper,
            jnp.concatenate([incoming, held], axis=0),
            jnp.concatenate([held, incoming], axis=0),
        )
    held = held.reshape((2,) * bits + shard.shape)
    return jnp.transpose(held, tuple(reversed(range(bits))) + tuple(range(bits, held.ndim)))


def causal_gathered(shard, axis):
    peers = lax.axis_size(axis)
    if peers > CAUSAL_PEERS:
        return gathered(shard, axis)
    place = lax.axis_index(axis)
    received = [shard]
    for shift in range(1, peers):
        pairs = [(i, i + shift) for i in range(peers - shift)]
        received.append(lax.ppermute(shard, axis, pairs))
    received.append(jnp.zeros_like(shard))
    blocks = jnp.arange(peers, dtype=jnp.int32)
    order = jnp.where(blocks <= place, place - blocks, peers)
    return jnp.take(jnp.stack(received), order, axis=0)


def logits_kernel(taps_ref, query_ref, keys_ref, out_ref, high_ref, low_ref, conv_ref):
    head = pl.program_id(0)
    group = pl.program_id(1)
    edge = 16

    @pl.when(group == 0)
    def _():
        lane = lax.broadcasted_iota(jnp.int32, (1, 2 * KEY_BLOCK), 1)
        for row_lag in range(QCONV):
            row = jnp.zeros(lane.shape, jnp.float32)
            for col_lag in range(KCONV):
                tap = taps_ref[(head * QCONV + row_lag) * KCONV + col_lag]
                row = jnp.where(lane == KEY_BLOCK - col_lag, tap, row)
            toeplitz = pltpu.roll(
                jnp.broadcast_to(row, (KEY_BLOCK, 2 * KEY_BLOCK)), 0, 1, stride=1, stride_axis=0
            )
            high = toeplitz.astype(jnp.bfloat16)
            low = (toeplitz - high.astype(jnp.float32)).astype(jnp.bfloat16)
            high_ref[row_lag * KEY_BLOCK : (row_lag + 1) * KEY_BLOCK] = high[:, KEY_BLOCK:]
            low_ref[row_lag * KEY_BLOCK : (row_lag + 1) * KEY_BLOCK] = low[:, KEY_BLOCK:]
            top = QCONV * KEY_BLOCK + row_lag * edge
            high_ref[top : top + edge] = high[:edge, :KEY_BLOCK]
            low_ref[top : top + edge] = low[:edge, :KEY_BLOCK]

    blocks = conv_ref.shape[1] // KEY_BLOCK
    body = QCONV * KEY_BLOCK
    for block in range(blocks):
        start = pl.multiple_of((group * blocks + block) * KEY_BLOCK, KEY_BLOCK)
        before = keys_ref[pl.ds(start, KEY_BLOCK), :]
        current = keys_ref[pl.ds(start + KEY_BLOCK, KEY_BLOCK), :]
        conv_body = jnp.dot(
            high_ref[:body], current, preferred_element_type=jnp.float32
        ) + jnp.dot(low_ref[:body], current, preferred_element_type=jnp.float32)
        conv_top = jnp.dot(
            high_ref[body:], before, preferred_element_type=jnp.float32
        ) + jnp.dot(low_ref[body:], before, preferred_element_type=jnp.float32)
        base = block * KEY_BLOCK
        for row_lag in range(QCONV):
            first = row_lag * KEY_BLOCK
            head_rows = conv_body[first : first + edge] + conv_top[
                row_lag * edge : (row_lag + 1) * edge
            ]
            rest_rows = conv_body[first + edge : first + KEY_BLOCK]
            cols = slice(row_lag * KEY_BLOCK, (row_lag + 1) * KEY_BLOCK)
            for part, rows in ((head_rows, slice(base, base + edge)),
                               (rest_rows, slice(base + edge, base + KEY_BLOCK))):
                part_high = part.astype(jnp.bfloat16)
                part_low = (part - part_high.astype(jnp.float32)).astype(jnp.bfloat16)
                conv_ref[0, rows, cols] = part_high
                conv_ref[1, rows, cols] = part_low
    query = query_ref[0]
    out_ref[0] = jnp.dot(conv_ref[0], query, preferred_element_type=jnp.float32) + jnp.dot(
        conv_ref[1], query, preferred_element_type=jnp.float32
    )


def conv_logits(shifted_t, score_kernel, key_pad):
    heads, contract, row_count = shifted_t.shape
    seq_len = key_pad.shape[0] - KEY_BLOCK
    head_dim = key_pad.shape[1] // heads
    span = min(seq_len, KEY_SPAN)
    taps = (score_kernel * head_dim ** (-0.5)).reshape(-1)
    return pl.pallas_call(
        logits_kernel,
        grid=(heads, seq_len // span),
        in_specs=[
            pl.BlockSpec(memory_space=pltpu.SMEM),
            pl.BlockSpec((1, contract, row_count), lambda h, g: (h, 0, 0)),
            pl.BlockSpec((key_pad.shape[0], head_dim), lambda h, g: (0, h)),
        ],
        out_specs=pl.BlockSpec((1, span, row_count), lambda h, g: (h, g, 0)),
        out_shape=jax.ShapeDtypeStruct((heads, seq_len, row_count), jnp.float32),
        scratch_shapes=[
            pltpu.VMEM((QCONV * (KEY_BLOCK + 16), KEY_BLOCK), jnp.bfloat16),
            pltpu.VMEM((QCONV * (KEY_BLOCK + 16), KEY_BLOCK), jnp.bfloat16),
            pltpu.VMEM((2, span, QCONV * head_dim), jnp.bfloat16),
        ],
    )(taps, shifted_t, key_pad)


def band_terms(query_rows, query_first, key_flat, score_kernel):
    row_lead = QCONV - 1
    heads = score_kernel.shape[0]
    ext_count = query_rows.shape[0]
    row_count = ext_count - row_lead
    near = lax.dynamic_slice_in_dim(key_flat, query_first + 4, ext_count + QCONV - 2, 0)
    query_heads = query_rows.reshape(ext_count, heads, -1).astype(jnp.float32)
    near_heads = near.reshape(near.shape[0], heads, -1).astype(jnp.float32)
    scale = query_heads.shape[2] ** (-0.5)
    diagonals = [
        jnp.sum(query_heads * near_heads[lag - 1 : lag - 1 + ext_count], axis=2) * scale
        for lag in range(1, QCONV)
    ]
    band = []
    for gap in range(QCONV - 1):
        acc = jnp.zeros((row_count, heads), jnp.float32)
        for row_lag in range(gap + 1, QCONV):
            for col_lag in range(row_lag - gap):
                lag = row_lag - col_lag - gap
                acc = acc - score_kernel[None, :, row_lag, col_lag] * diagonals[lag - 1][
                    row_lead - row_lag : row_lead - row_lag + row_count
                ]
        band.append(acc.T)
    return jnp.stack(band)


def attend_chunk(shifted, band, query_first, key_pad, score_kernel, value_heads, head_mixing):
    row_count, heads = shifted.shape[:2]
    seq_len = value_heads.shape[0]
    shifted_t = jnp.transpose(shifted, (1, 2, 3, 0)).reshape((heads, -1, row_count))
    convolved = conv_logits(shifted_t, score_kernel, key_pad)
    query_pos = query_first + lax.iota(jnp.int32, row_count)
    gap = query_pos[None, :] - lax.iota(jnp.int32, seq_len)[:, None]
    for lag in range(QCONV - 1):
        convolved = convolved + jnp.where(gap == lag, band[lag][:, None, :], 0.0)
    logits = jnp.where(gap >= 0, convolved, lowest)
    peak = jnp.max(logits, axis=1, keepdims=True)
    expd = jnp.exp(logits - peak)
    probabilities = expd / jnp.sum(expd, axis=1, keepdims=True)
    grouped = probabilities.reshape(heads // GROUP, GROUP, seq_len, row_count)
    weights = head_mixing.reshape(heads // GROUP, GROUP, GROUP)
    mixed_probs = jnp.zeros_like(grouped)
    for source in range(GROUP):
        mixed_probs = mixed_probs + weights[:, :, source, None, None] * grouped[:, source, None]
    mixed_probs = mixed_probs.reshape(heads, seq_len, row_count).astype(jnp.bfloat16)
    return jnp.einsum(
        "hki,khd->ihd", mixed_probs, value_heads, preferred_element_type=jnp.float32
    )


def normalize(weighted, gain_local):
    factor = lax.rsqrt(jnp.mean(weighted * weighted, axis=2, keepdims=True) + epsilon)
    return (
        (weighted * factor * gain_local[None]).astype(jnp.bfloat16).reshape(weighted.shape[0], -1)
    )


def shards(query_states, key_states, value_states, score_kernel, head_mixing, head_gain):
    groups = lax.axis_size("uly")
    stacked = jnp.stack([query_states, key_states, value_states])
    group_width = stacked.shape[2] // groups
    pieces = exchanged(
        lambda group: lax.dynamic_slice_in_dim(stacked, group * group_width, group_width, 2),
        "uly",
    )
    pieces = jnp.moveaxis(pieces, 0, 1)
    query_local, key_local, value_local = pieces.reshape(
        (pieces.shape[0], -1, pieces.shape[-1])
    )
    shard_rows = query_local.shape[0]
    width = query_local.shape[1]
    row_lead = QCONV - 1
    heads = score_kernel.shape[0]
    head_dim = width // heads
    ctx_place = lax.axis_index("ctx")
    query_first = ctx_place * shard_rows
    earlier = passed_along(query_local[shard_rows - row_lead :], "ctx", 1)
    query_ext = jnp.concatenate([earlier, query_local], axis=0)
    key_all = causal_gathered(key_local, "ctx").reshape((-1, width))
    key_all, value_local = lax.optimization_barrier((key_all, value_local))
    value_all = causal_gathered(value_local, "ctx").reshape((-1, width))
    seq_len = key_all.shape[0]
    key_pad = jnp.concatenate(
        [jnp.zeros((KEY_BLOCK, width), key_all.dtype), key_all], axis=0
    )
    edge = jnp.zeros((8, width), key_all.dtype)
    key_flat = jnp.concatenate([edge, key_all, edge], axis=0)
    band = band_terms(query_ext, query_first, key_flat, score_kernel)
    query_heads = query_ext.reshape(shard_rows + row_lead, heads, head_dim)
    shifted = jnp.stack(
        [query_heads[row_lead - lag : row_lead - lag + shard_rows] for lag in range(QCONV)], axis=2
    )
    value_heads = value_all.reshape(seq_len, heads, head_dim)
    chunk = min(ROW_CHUNK * KEY_BLOCK * 8 // seq_len, shard_rows)
    if chunk == shard_rows:
        weighted = attend_chunk(
            shifted, band, query_first, key_pad, score_kernel, value_heads, head_mixing
        )
    else:
        chunks = shard_rows // chunk

        def one_chunk(index):
            start = index * chunk
            return attend_chunk(
                lax.dynamic_slice_in_dim(shifted, start, chunk, 0),
                lax.dynamic_slice_in_dim(band, start, chunk, 2),
                query_first + start,
                key_pad,
                score_kernel,
                value_heads,
                head_mixing,
            )

        weighted = lax.map(one_chunk, jnp.arange(chunks, dtype=jnp.int32))
        weighted = weighted.reshape((shard_rows,) + weighted.shape[2:])
    gain_local = head_gain.reshape(heads, head_dim)
    attended = normalize(weighted, gain_local)
    block_rows = shard_rows // groups
    returned = exchanged(
        lambda group: lax.dynamic_slice_in_dim(attended, group * block_rows, block_rows, 0),
        "uly",
    )
    return jnp.moveaxis(returned, 0, 1).reshape((block_rows, -1))


def solution(mesh):
    placed = (
        P(("ctx", "uly"), None),
        P(("ctx", "uly"), None),
        P(("ctx", "uly"), None),
        P("uly", None, None),
        P("uly", None),
        P("uly"),
    )
    return jax.shard_map(
        shards, mesh=mesh, in_specs=placed, out_specs=P(("ctx", "uly"), None), check_vma=False
    )
```

```python
import jax
import jax.numpy as jnp
from jax import lax
from jax.experimental import pallas as pl
from jax.experimental.pallas import tpu as pltpu
from jax.sharding import PartitionSpec as P

GROUP = 4
QCONV = 6
KCONV = 11
KEY_BLOCK = 128
KEY_SPAN = 1024
ROW_CHUNK = 128


lowest = -1e30
epsilon = 1e-06


def passed_along(shard, axis, by):
    peers = lax.axis_size(axis)
    pairs = [(i, i + by) for i in range(peers) if 0 <= i + by < peers]
    return lax.ppermute(shard, axis, pairs)


def exchanged(pieces_of, axis):
    peers = lax.axis_size(axis)
    place = lax.axis_index(axis)
    received = [pieces_of(place)]
    for shift in range(1, peers):
        outgoing = pieces_of((place + shift) % peers)
        pairs = [(i, (i + shift) % peers) for i in range(peers)]
        received.append(lax.ppermute(outgoing, axis, pairs))
    order = (place - jnp.arange(peers, dtype=jnp.int32)) % peers
    return jnp.take(jnp.stack(received), order, axis=0)


def gathered(shard, axis):
    peers = lax.axis_size(axis)
    place = lax.axis_index(axis)
    if peers & (peers - 1) or peers < 4:
        return lax.all_gather(shard, axis, axis=0, tiled=False)
    bits = peers.bit_length() - 1
    received = [shard] + [
        lax.ppermute(shard, axis, [(i, i ^ flip) for i in range(peers)]) for flip in range(1, 4)
    ]
    order = (place & 3) ^ jnp.arange(4, dtype=jnp.int32)
    held = jnp.take(jnp.stack(received), order, axis=0)
    for level in reversed(range(2, bits)):
        bit = 1 << level
        incoming = lax.ppermute(held, axis, [(i, i ^ bit) for i in range(peers)])
        upper = (place & bit) != 0
        held = jnp.where(
            upper,
            jnp.concatenate([incoming, held], axis=0),
            jnp.concatenate([held, incoming], axis=0),
        )
    held = held.reshape((2,) * (bits - 2) + (4,) + shard.shape)
    low_first = tuple(reversed(range(bits - 2))) + (bits - 2,)
    return jnp.transpose(held, low_first + tuple(range(bits - 1, held.ndim))).reshape(
        (peers,) + shard.shape
    )


def logits_kernel(taps_ref, query_ref, keys_ref, out_ref, high_ref, low_ref, conv_ref):
    head = pl.program_id(0)
    group = pl.program_id(1)
    edge = 16

    @pl.when(group == 0)
    def _():
        lane = lax.broadcasted_iota(jnp.int32, (1, 2 * KEY_BLOCK), 1)
        for row_lag in range(QCONV):
            row = jnp.zeros(lane.shape, jnp.float32)
            for col_lag in range(KCONV):
                tap = taps_ref[(head * QCONV + row_lag) * KCONV + col_lag]
                row = jnp.where(lane == KEY_BLOCK - col_lag, tap, row)
            toeplitz = pltpu.roll(
                jnp.broadcast_to(row, (KEY_BLOCK, 2 * KEY_BLOCK)), 0, 1, stride=1, stride_axis=0
            )
            high = toeplitz.astype(jnp.bfloat16)
            low = (toeplitz - high.astype(jnp.float32)).astype(jnp.bfloat16)
            high_ref[row_lag * KEY_BLOCK : (row_lag + 1) * KEY_BLOCK] = high[:, KEY_BLOCK:]
            low_ref[row_lag * KEY_BLOCK : (row_lag + 1) * KEY_BLOCK] = low[:, KEY_BLOCK:]
            top = QCONV * KEY_BLOCK + row_lag * edge
            high_ref[top : top + edge] = high[:edge, :KEY_BLOCK]
            low_ref[top : top + edge] = low[:edge, :KEY_BLOCK]

    blocks = conv_ref.shape[1] // KEY_BLOCK
    body = QCONV * KEY_BLOCK
    for block in range(blocks):
        start = pl.multiple_of((group * blocks + block) * KEY_BLOCK, KEY_BLOCK)
        before = keys_ref[pl.ds(start, KEY_BLOCK), :]
        current = keys_ref[pl.ds(start + KEY_BLOCK, KEY_BLOCK), :]
        conv_body = jnp.dot(
            high_ref[:body], current, preferred_element_type=jnp.float32
        ) + jnp.dot(low_ref[:body], current, preferred_element_type=jnp.float32)
        conv_top = jnp.dot(
            high_ref[body:], before, preferred_element_type=jnp.float32
        ) + jnp.dot(low_ref[body:], before, preferred_element_type=jnp.float32)
        base = block * KEY_BLOCK
        for row_lag in range(QCONV):
            first = row_lag * KEY_BLOCK
            head_rows = conv_body[first : first + edge] + conv_top[
                row_lag * edge : (row_lag + 1) * edge
            ]
            rest_rows = conv_body[first + edge : first + KEY_BLOCK]
            cols = slice(row_lag * KEY_BLOCK, (row_lag + 1) * KEY_BLOCK)
            for part, rows in ((head_rows, slice(base, base + edge)),
                               (rest_rows, slice(base + edge, base + KEY_BLOCK))):
                part_high = part.astype(jnp.bfloat16)
                part_low = (part - part_high.astype(jnp.float32)).astype(jnp.bfloat16)
                conv_ref[0, rows, cols] = part_high
                conv_ref[1, rows, cols] = part_low
    query = query_ref[0]
    out_ref[0] = jnp.dot(conv_ref[0], query, preferred_element_type=jnp.float32) + jnp.dot(
        conv_ref[1], query, preferred_element_type=jnp.float32
    )


def conv_logits(shifted_t, score_kernel, key_pad):
    heads, contract, row_count = shifted_t.shape
    seq_len = key_pad.shape[0] - KEY_BLOCK
    head_dim = key_pad.shape[1] // heads
    span = min(seq_len, KEY_SPAN)
    taps = (score_kernel * head_dim ** (-0.5)).reshape(-1)
    return pl.pallas_call(
        logits_kernel,
        grid=(heads, seq_len // span),
        in_specs=[
            pl.BlockSpec(memory_space=pltpu.SMEM),
            pl.BlockSpec((1, contract, row_count), lambda h, g: (h, 0, 0)),
            pl.BlockSpec((key_pad.shape[0], head_dim), lambda h, g: (0, h)),
        ],
        out_specs=pl.BlockSpec((1, span, row_count), lambda h, g: (h, g, 0)),
        out_shape=jax.ShapeDtypeStruct((heads, seq_len, row_count), jnp.float32),
        scratch_shapes=[
            pltpu.VMEM((QCONV * (KEY_BLOCK + 16), KEY_BLOCK), jnp.bfloat16),
            pltpu.VMEM((QCONV * (KEY_BLOCK + 16), KEY_BLOCK), jnp.bfloat16),
            pltpu.VMEM((2, span, QCONV * head_dim), jnp.bfloat16),
        ],
    )(taps, shifted_t, key_pad)


def band_terms(query_rows, query_first, key_flat, score_kernel):
    row_lead = QCONV - 1
    heads = score_kernel.shape[0]
    ext_count = query_rows.shape[0]
    row_count = ext_count - row_lead
    near = lax.dynamic_slice_in_dim(key_flat, query_first + 4, ext_count + QCONV - 2, 0)
    query_heads = query_rows.reshape(ext_count, heads, -1).astype(jnp.float32)
    near_heads = near.reshape(near.shape[0], heads, -1).astype(jnp.float32)
    scale = query_heads.shape[2] ** (-0.5)
    diagonals = [
        jnp.sum(query_heads * near_heads[lag - 1 : lag - 1 + ext_count], axis=2) * scale
        for lag in range(1, QCONV)
    ]
    band = []
    for gap in range(QCONV - 1):
        acc = jnp.zeros((row_count, heads), jnp.float32)
        for row_lag in range(gap + 1, QCONV):
            for col_lag in range(row_lag - gap):
                lag = row_lag - col_lag - gap
                acc = acc - score_kernel[None, :, row_lag, col_lag] * diagonals[lag - 1][
                    row_lead - row_lag : row_lead - row_lag + row_count
                ]
        band.append(acc.T)
    return jnp.stack(band)


def attend_chunk(shifted, band, query_first, key_pad, score_kernel, value_heads, head_mixing):
    row_count, heads = shifted.shape[:2]
    seq_len = value_heads.shape[0]
    shifted_t = jnp.transpose(shifted, (1, 2, 3, 0)).reshape((heads, -1, row_count))
    convolved = conv_logits(shifted_t, score_kernel, key_pad)
    query_pos = query_first + lax.iota(jnp.int32, row_count)
    gap = query_pos[None, :] - lax.iota(jnp.int32, seq_len)[:, None]
    for lag in range(QCONV - 1):
        convolved = convolved + jnp.where(gap == lag, band[lag][:, None, :], 0.0)
    logits = jnp.where(gap >= 0, convolved, lowest)
    peak = jnp.max(logits, axis=1, keepdims=True)
    expd = jnp.exp(logits - peak)
    probabilities = expd / jnp.sum(expd, axis=1, keepdims=True)
    grouped = probabilities.reshape(heads // GROUP, GROUP, seq_len, row_count)
    weights = head_mixing.reshape(heads // GROUP, GROUP, GROUP)
    mixed_probs = jnp.zeros_like(grouped)
    for source in range(GROUP):
        mixed_probs = mixed_probs + weights[:, :, source, None, None] * grouped[:, source, None]
    mixed_probs = mixed_probs.reshape(heads, seq_len, row_count).astype(jnp.bfloat16)
    return jnp.einsum(
        "hki,khd->ihd", mixed_probs, value_heads, preferred_element_type=jnp.float32
    )


def normalize(weighted, gain_local):
    factor = lax.rsqrt(jnp.mean(weighted * weighted, axis=2, keepdims=True) + epsilon)
    return (
        (weighted * factor * gain_local[None]).astype(jnp.bfloat16).reshape(weighted.shape[0], -1)
    )


def shards(query_states, key_states, value_states, score_kernel, head_mixing, head_gain):
    groups = lax.axis_size("uly")
    stacked = jnp.stack([query_states, key_states, value_states])
    group_width = stacked.shape[2] // groups
    pieces = exchanged(
        lambda group: lax.dynamic_slice_in_dim(stacked, group * group_width, group_width, 2),
        "uly",
    )
    pieces = jnp.moveaxis(pieces, 0, 1)
    query_local, key_local, value_local = pieces.reshape(
        (pieces.shape[0], -1, pieces.shape[-1])
    )
    shard_rows = query_local.shape[0]
    width = query_local.shape[1]
    row_lead = QCONV - 1
    heads = score_kernel.shape[0]
    head_dim = width // heads
    ctx_place = lax.axis_index("ctx")
    query_first = ctx_place * shard_rows
    earlier = passed_along(query_local[shard_rows - row_lead :], "ctx", 1)
    query_ext = jnp.concatenate([earlier, query_local], axis=0)
    key_all = gathered(key_local, "ctx").reshape((-1, width))
    key_all, value_local = lax.optimization_barrier((key_all, value_local))
    value_all = gathered(value_local, "ctx").reshape((-1, width))
    seq_len = key_all.shape[0]
    key_pad = jnp.concatenate(
        [jnp.zeros((KEY_BLOCK, width), key_all.dtype), key_all], axis=0
    )
    edge = jnp.zeros((8, width), key_all.dtype)
    key_flat = jnp.concatenate([edge, key_all, edge], axis=0)
    band = band_terms(query_ext, query_first, key_flat, score_kernel)
    query_heads = query_ext.reshape(shard_rows + row_lead, heads, head_dim)
    shifted = jnp.stack(
        [query_heads[row_lead - lag : row_lead - lag + shard_rows] for lag in range(QCONV)], axis=2
    )
    value_heads = value_all.reshape(seq_len, heads, head_dim)
    chunk = min(ROW_CHUNK * KEY_BLOCK * 8 // seq_len, shard_rows)
    if chunk == shard_rows:
        weighted = attend_chunk(
            shifted, band, query_first, key_pad, score_kernel, value_heads, head_mixing
        )
    else:
        chunks = shard_rows // chunk

        def one_chunk(index):
            start = index * chunk
            return attend_chunk(
                lax.dynamic_slice_in_dim(shifted, start, chunk, 0),
                lax.dynamic_slice_in_dim(band, start, chunk, 2),
                query_first + start,
                key_pad,
                score_kernel,
                value_heads,
                head_mixing,
            )

        weighted = lax.map(one_chunk, jnp.arange(chunks, dtype=jnp.int32))
        weighted = weighted.reshape((shard_rows,) + weighted.shape[2:])
    gain_local = head_gain.reshape(heads, head_dim)
    attended = normalize(weighted, gain_local)
    block_rows = shard_rows // groups
    returned = exchanged(
        lambda group: lax.dynamic_slice_in_dim(attended, group * block_rows, block_rows, 0),
        "uly",
    )
    return jnp.moveaxis(returned, 0, 1).reshape((block_rows, -1))


def solution(mesh):
    placed = (
        P(("ctx", "uly"), None),
        P(("ctx", "uly"), None),
        P(("ctx", "uly"), None),
        P("uly", None, None),
        P("uly", None),
        P("uly"),
    )
    return jax.shard_map(
        shards, mesh=mesh, in_specs=placed, out_specs=P(("ctx", "uly"), None), check_vma=False
    )
```

```python
import jax
import jax.numpy as jnp
from jax import lax
from jax.experimental import pallas as pl
from jax.experimental.pallas import tpu as pltpu
from jax.sharding import PartitionSpec as P

GROUP = 4
QCONV = 6
KCONV = 11
KEY_BLOCK = 128
KEY_SPAN = 1024
ROW_CHUNK = 128


lowest = -1e30
epsilon = 1e-06


def passed_along(shard, axis, by):
    peers = lax.axis_size(axis)
    pairs = [(i, i + by) for i in range(peers) if 0 <= i + by < peers]
    return lax.ppermute(shard, axis, pairs)


def exchanged(pieces_of, axis):
    peers = lax.axis_size(axis)
    place = lax.axis_index(axis)
    received = [pieces_of(place)]
    for shift in range(1, peers):
        outgoing = pieces_of((place + shift) % peers)
        pairs = [(i, (i + shift) % peers) for i in range(peers)]
        received.append(lax.ppermute(outgoing, axis, pairs))
    order = (place - jnp.arange(peers, dtype=jnp.int32)) % peers
    return jnp.take(jnp.stack(received), order, axis=0)


def gathered(shard, axis):
    peers = lax.axis_size(axis)
    place = lax.axis_index(axis)
    if peers & (peers - 1):
        return lax.all_gather(shard, axis, axis=0, tiled=False)
    bits = peers.bit_length() - 1
    held = shard[None]
    for level in reversed(range(bits)):
        bit = 1 << level
        incoming = lax.ppermute(held, axis, [(i, i ^ bit) for i in range(peers)])
        upper = (place & bit) != 0
        held = jnp.where(
            upper,
            jnp.concatenate([incoming, held], axis=0),
            jnp.concatenate([held, incoming], axis=0),
        )
    held = held.reshape((2,) * bits + shard.shape)
    return jnp.transpose(held, tuple(reversed(range(bits))) + tuple(range(bits, held.ndim)))


def logits_kernel(taps_ref, query_ref, keys_ref, out_ref, high_ref, low_ref, conv_ref):
    head = pl.program_id(0)
    group = pl.program_id(1)
    edge = 16

    @pl.when(group == 0)
    def _():
        lane = lax.broadcasted_iota(jnp.int32, (1, 2 * KEY_BLOCK), 1)
        for row_lag in range(QCONV):
            row = jnp.zeros(lane.shape, jnp.float32)
            for col_lag in range(KCONV):
                tap = taps_ref[(head * QCONV + row_lag) * KCONV + col_lag]
                row = jnp.where(lane == KEY_BLOCK - col_lag, tap, row)
            toeplitz = pltpu.roll(
                jnp.broadcast_to(row, (KEY_BLOCK, 2 * KEY_BLOCK)), 0, 1, stride=1, stride_axis=0
            )
            high = toeplitz.astype(jnp.bfloat16)
            low = (toeplitz - high.astype(jnp.float32)).astype(jnp.bfloat16)
            high_ref[row_lag * KEY_BLOCK : (row_lag + 1) * KEY_BLOCK] = high[:, KEY_BLOCK:]
            low_ref[row_lag * KEY_BLOCK : (row_lag + 1) * KEY_BLOCK] = low[:, KEY_BLOCK:]
            top = QCONV * KEY_BLOCK + row_lag * edge
            high_ref[top : top + edge] = high[:edge, :KEY_BLOCK]
            low_ref[top : top + edge] = low[:edge, :KEY_BLOCK]

    blocks = conv_ref.shape[1] // KEY_BLOCK
    body = QCONV * KEY_BLOCK
    for block in range(blocks):
        start = pl.multiple_of((group * blocks + block) * KEY_BLOCK, KEY_BLOCK)
        before = keys_ref[pl.ds(start, KEY_BLOCK), :]
        current = keys_ref[pl.ds(start + KEY_BLOCK, KEY_BLOCK), :]
        conv_body = jnp.dot(
            high_ref[:body], current, preferred_element_type=jnp.float32
        ) + jnp.dot(low_ref[:body], current, preferred_element_type=jnp.float32)
        conv_top = jnp.dot(
            high_ref[body:], before, preferred_element_type=jnp.float32
        ) + jnp.dot(low_ref[body:], before, preferred_element_type=jnp.float32)
        base = block * KEY_BLOCK
        for row_lag in range(QCONV):
            first = row_lag * KEY_BLOCK
            head_rows = conv_body[first : first + edge] + conv_top[
                row_lag * edge : (row_lag + 1) * edge
            ]
            rest_rows = conv_body[first + edge : first + KEY_BLOCK]
            cols = slice(row_lag * KEY_BLOCK, (row_lag + 1) * KEY_BLOCK)
            for part, rows in ((head_rows, slice(base, base + edge)),
                               (rest_rows, slice(base + edge, base + KEY_BLOCK))):
                part_high = part.astype(jnp.bfloat16)
                part_low = (part - part_high.astype(jnp.float32)).astype(jnp.bfloat16)
                conv_ref[0, rows, cols] = part_high
                conv_ref[1, rows, cols] = part_low
    query = query_ref[0]
    out_ref[0] = jnp.dot(conv_ref[0], query, preferred_element_type=jnp.float32) + jnp.dot(
        conv_ref[1], query, preferred_element_type=jnp.float32
    )


def conv_logits(shifted_t, score_kernel, key_pad):
    heads, contract, row_count = shifted_t.shape
    seq_len = key_pad.shape[0] - KEY_BLOCK
    head_dim = key_pad.shape[1] // heads
    span = min(seq_len, KEY_SPAN)
    taps = (score_kernel * head_dim ** (-0.5)).reshape(-1)
    return pl.pallas_call(
        logits_kernel,
        grid=(heads, seq_len // span),
        in_specs=[
            pl.BlockSpec(memory_space=pltpu.SMEM),
            pl.BlockSpec((1, contract, row_count), lambda h, g: (h, 0, 0)),
            pl.BlockSpec((key_pad.shape[0], head_dim), lambda h, g: (0, h)),
        ],
        out_specs=pl.BlockSpec((1, span, row_count), lambda h, g: (h, g, 0)),
        out_shape=jax.ShapeDtypeStruct((heads, seq_len, row_count), jnp.float32),
        scratch_shapes=[
            pltpu.VMEM((QCONV * (KEY_BLOCK + 16), KEY_BLOCK), jnp.bfloat16),
            pltpu.VMEM((QCONV * (KEY_BLOCK + 16), KEY_BLOCK), jnp.bfloat16),
            pltpu.VMEM((2, span, QCONV * head_dim), jnp.bfloat16),
        ],
    )(taps, shifted_t, key_pad)


def band_terms(query_rows, query_first, key_flat, score_kernel):
    row_lead = QCONV - 1
    heads = score_kernel.shape[0]
    ext_count = query_rows.shape[0]
    row_count = ext_count - row_lead
    near = lax.dynamic_slice_in_dim(key_flat, query_first + 4, ext_count + QCONV - 2, 0)
    query_heads = query_rows.reshape(ext_count, heads, -1).astype(jnp.float32)
    near_heads = near.reshape(near.shape[0], heads, -1).astype(jnp.float32)
    scale = query_heads.shape[2] ** (-0.5)
    diagonals = [
        jnp.sum(query_heads * near_heads[lag - 1 : lag - 1 + ext_count], axis=2) * scale
        for lag in range(1, QCONV)
    ]
    band = []
    for gap in range(QCONV - 1):
        acc = jnp.zeros((row_count, heads), jnp.float32)
        for row_lag in range(gap + 1, QCONV):
            for col_lag in range(row_lag - gap):
                lag = row_lag - col_lag - gap
                acc = acc - score_kernel[None, :, row_lag, col_lag] * diagonals[lag - 1][
                    row_lead - row_lag : row_lead - row_lag + row_count
                ]
        band.append(acc.T)
    return jnp.stack(band)


def attend_chunk(shifted, band, query_first, key_pad, score_kernel, value_heads, head_mixing):
    row_count, heads = shifted.shape[:2]
    seq_len = value_heads.shape[0]
    shifted_t = jnp.transpose(shifted, (1, 2, 3, 0)).reshape((heads, -1, row_count))
    convolved = conv_logits(shifted_t, score_kernel, key_pad)
    query_pos = query_first + lax.iota(jnp.int32, row_count)
    gap = query_pos[None, :] - lax.iota(jnp.int32, seq_len)[:, None]
    for lag in range(QCONV - 1):
        convolved = convolved + jnp.where(gap == lag, band[lag][:, None, :], 0.0)
    logits = jnp.where(gap >= 0, convolved, lowest)
    peak = jnp.max(logits, axis=1, keepdims=True)
    expd = jnp.exp(logits - peak)
    probabilities = expd / jnp.sum(expd, axis=1, keepdims=True)
    grouped = probabilities.reshape(heads // GROUP, GROUP, seq_len, row_count)
    weights = head_mixing.reshape(heads // GROUP, GROUP, GROUP)
    mixed_probs = jnp.zeros_like(grouped)
    for source in range(GROUP):
        mixed_probs = mixed_probs + weights[:, :, source, None, None] * grouped[:, source, None]
    mixed_probs = mixed_probs.reshape(heads, seq_len, row_count).astype(jnp.bfloat16)
    return jnp.einsum(
        "hki,khd->ihd", mixed_probs, value_heads, preferred_element_type=jnp.float32
    )


def normalize(weighted, gain_local):
    factor = lax.rsqrt(jnp.mean(weighted * weighted, axis=2, keepdims=True) + epsilon)
    return (
        (weighted * factor * gain_local[None]).astype(jnp.bfloat16).reshape(weighted.shape[0], -1)
    )


def shards(query_states, key_states, value_states, score_kernel, head_mixing, head_gain):
    groups = lax.axis_size("uly")
    stacked = jnp.stack([query_states, key_states, value_states])
    group_width = stacked.shape[2] // groups
    pieces = exchanged(
        lambda group: lax.dynamic_slice_in_dim(stacked, group * group_width, group_width, 2),
        "uly",
    )
    pieces = jnp.moveaxis(pieces, 0, 1)
    query_local, key_local, value_local = pieces.reshape(
        (pieces.shape[0], -1, pieces.shape[-1])
    )
    shard_rows = query_local.shape[0]
    width = query_local.shape[1]
    row_lead = QCONV - 1
    heads = score_kernel.shape[0]
    head_dim = width // heads
    ctx_place = lax.axis_index("ctx")
    query_first = ctx_place * shard_rows
    earlier = passed_along(query_local[shard_rows - row_lead :], "ctx", 1)
    query_ext = jnp.concatenate([earlier, query_local], axis=0)
    both = gathered(jnp.stack([key_local, value_local]), "ctx")
    both = both.reshape((-1,) + both.shape[-3:])
    key_all = both[:, 0].reshape((-1, width))
    value_all = both[:, 1].reshape((-1, width))
    seq_len = key_all.shape[0]
    key_pad = jnp.concatenate(
        [jnp.zeros((KEY_BLOCK, width), key_all.dtype), key_all], axis=0
    )
    edge = jnp.zeros((8, width), key_all.dtype)
    key_flat = jnp.concatenate([edge, key_all, edge], axis=0)
    band = band_terms(query_ext, query_first, key_flat, score_kernel)
    query_heads = query_ext.reshape(shard_rows + row_lead, heads, head_dim)
    shifted = jnp.stack(
        [query_heads[row_lead - lag : row_lead - lag + shard_rows] for lag in range(QCONV)], axis=2
    )
    value_heads = value_all.reshape(seq_len, heads, head_dim)
    chunk = min(ROW_CHUNK * KEY_BLOCK * 8 // seq_len, shard_rows)
    if chunk == shard_rows:
        weighted = attend_chunk(
            shifted, band, query_first, key_pad, score_kernel, value_heads, head_mixing
        )
    else:
        chunks = shard_rows // chunk

        def one_chunk(index):
            start = index * chunk
            return attend_chunk(
                lax.dynamic_slice_in_dim(shifted, start, chunk, 0),
                lax.dynamic_slice_in_dim(band, start, chunk, 2),
                query_first + start,
                key_pad,
                score_kernel,
                value_heads,
                head_mixing,
            )

        weighted = lax.map(one_chunk, jnp.arange(chunks, dtype=jnp.int32))
        weighted = weighted.reshape((shard_rows,) + weighted.shape[2:])
    gain_local = head_gain.reshape(heads, head_dim)
    attended = normalize(weighted, gain_local)
    block_rows = shard_rows // groups
    returned = exchanged(
        lambda group: lax.dynamic_slice_in_dim(attended, group * block_rows, block_rows, 0),
        "uly",
    )
    return jnp.moveaxis(returned, 0, 1).reshape((block_rows, -1))


def solution(mesh):
    placed = (
        P(("ctx", "uly"), None),
        P(("ctx", "uly"), None),
        P(("ctx", "uly"), None),
        P("uly", None, None),
        P("uly", None),
        P("uly"),
    )
    return jax.shard_map(
        shards, mesh=mesh, in_specs=placed, out_specs=P(("ctx", "uly"), None), check_vma=False
    )
```

```python
import jax
import jax.numpy as jnp
from jax import lax
from jax.experimental import pallas as pl
from jax.experimental.pallas import tpu as pltpu
from jax.sharding import PartitionSpec as P

GROUP = 4
QCONV = 6
KCONV = 11
KEY_BLOCK = 128
KEY_SPAN = 1024
ROW_CHUNK = 128


lowest = -1e30
epsilon = 1e-06


def passed_along(shard, axis, by):
    peers = lax.axis_size(axis)
    pairs = [(i, i + by) for i in range(peers) if 0 <= i + by < peers]
    return lax.ppermute(shard, axis, pairs)


def exchanged(pieces_of, axis):
    peers = lax.axis_size(axis)
    place = lax.axis_index(axis)
    received = [pieces_of(place)]
    for shift in range(1, peers):
        outgoing = pieces_of((place + shift) % peers)
        pairs = [(i, (i + shift) % peers) for i in range(peers)]
        received.append(lax.ppermute(outgoing, axis, pairs))
    order = (place - jnp.arange(peers, dtype=jnp.int32)) % peers
    return jnp.take(jnp.stack(received), order, axis=0)


def gathered(shard, axis):
    peers = lax.axis_size(axis)
    place = lax.axis_index(axis)
    if peers & (peers - 1):
        return lax.all_gather(shard, axis, axis=0, tiled=False)
    bits = peers.bit_length() - 1
    held = shard[None]
    for level in reversed(range(bits)):
        bit = 1 << level
        incoming = lax.ppermute(held, axis, [(i, i ^ bit) for i in range(peers)])
        upper = (place & bit) != 0
        held = jnp.where(
            upper,
            jnp.concatenate([incoming, held], axis=0),
            jnp.concatenate([held, incoming], axis=0),
        )
    held = held.reshape((2,) * bits + shard.shape)
    return jnp.transpose(held, tuple(reversed(range(bits))) + tuple(range(bits, held.ndim)))


def logits_kernel(taps_ref, query_ref, keys_ref, out_ref, high_ref, low_ref, conv_ref):
    head = pl.program_id(0)
    group = pl.program_id(1)
    edge = 16

    @pl.when(group == 0)
    def _():
        lane = lax.broadcasted_iota(jnp.int32, (1, 2 * KEY_BLOCK), 1)
        for row_lag in range(QCONV):
            row = jnp.zeros(lane.shape, jnp.float32)
            for col_lag in range(KCONV):
                tap = taps_ref[(head * QCONV + row_lag) * KCONV + col_lag]
                row = jnp.where(lane == KEY_BLOCK - col_lag, tap, row)
            toeplitz = pltpu.roll(
                jnp.broadcast_to(row, (KEY_BLOCK, 2 * KEY_BLOCK)), 0, 1, stride=1, stride_axis=0
            )
            high = toeplitz.astype(jnp.bfloat16)
            low = (toeplitz - high.astype(jnp.float32)).astype(jnp.bfloat16)
            high_ref[row_lag * KEY_BLOCK : (row_lag + 1) * KEY_BLOCK] = high[:, KEY_BLOCK:]
            low_ref[row_lag * KEY_BLOCK : (row_lag + 1) * KEY_BLOCK] = low[:, KEY_BLOCK:]
            top = QCONV * KEY_BLOCK + row_lag * edge
            high_ref[top : top + edge] = high[:edge, :KEY_BLOCK]
            low_ref[top : top + edge] = low[:edge, :KEY_BLOCK]

    blocks = conv_ref.shape[1] // KEY_BLOCK
    body = QCONV * KEY_BLOCK
    for block in range(blocks):
        start = pl.multiple_of((group * blocks + block) * KEY_BLOCK, KEY_BLOCK)
        before = keys_ref[pl.ds(start, KEY_BLOCK), :]
        current = keys_ref[pl.ds(start + KEY_BLOCK, KEY_BLOCK), :]
        conv_body = jnp.dot(
            high_ref[:body], current, preferred_element_type=jnp.float32
        ) + jnp.dot(low_ref[:body], current, preferred_element_type=jnp.float32)
        conv_top = jnp.dot(
            high_ref[body:], before, preferred_element_type=jnp.float32
        ) + jnp.dot(low_ref[body:], before, preferred_element_type=jnp.float32)
        base = block * KEY_BLOCK
        for row_lag in range(QCONV):
            first = row_lag * KEY_BLOCK
            head_rows = conv_body[first : first + edge] + conv_top[
                row_lag * edge : (row_lag + 1) * edge
            ]
            rest_rows = conv_body[first + edge : first + KEY_BLOCK]
            cols = slice(row_lag * KEY_BLOCK, (row_lag + 1) * KEY_BLOCK)
            for part, rows in ((head_rows, slice(base, base + edge)),
                               (rest_rows, slice(base + edge, base + KEY_BLOCK))):
                part_high = part.astype(jnp.bfloat16)
                part_low = (part - part_high.astype(jnp.float32)).astype(jnp.bfloat16)
                conv_ref[0, rows, cols] = part_high
                conv_ref[1, rows, cols] = part_low
    query = query_ref[0]
    out_ref[0] = jnp.dot(conv_ref[0], query, preferred_element_type=jnp.float32) + jnp.dot(
        conv_ref[1], query, preferred_element_type=jnp.float32
    )


def conv_logits(shifted_t, score_kernel, key_pad):
    heads, contract, row_count = shifted_t.shape
    seq_len = key_pad.shape[0] - KEY_BLOCK
    head_dim = key_pad.shape[1] // heads
    span = min(seq_len, KEY_SPAN)
    taps = (score_kernel * head_dim ** (-0.5)).reshape(-1)
    return pl.pallas_call(
        logits_kernel,
        grid=(heads, seq_len // span),
        in_specs=[
            pl.BlockSpec(memory_space=pltpu.SMEM),
            pl.BlockSpec((1, contract, row_count), lambda h, g: (h, 0, 0)),
            pl.BlockSpec((key_pad.shape[0], head_dim), lambda h, g: (0, h)),
        ],
        out_specs=pl.BlockSpec((1, span, row_count), lambda h, g: (h, g, 0)),
        out_shape=jax.ShapeDtypeStruct((heads, seq_len, row_count), jnp.float32),
        scratch_shapes=[
            pltpu.VMEM((QCONV * (KEY_BLOCK + 16), KEY_BLOCK), jnp.bfloat16),
            pltpu.VMEM((QCONV * (KEY_BLOCK + 16), KEY_BLOCK), jnp.bfloat16),
            pltpu.VMEM((2, span, QCONV * head_dim), jnp.bfloat16),
        ],
    )(taps, shifted_t, key_pad)


def band_terms(query_rows, query_first, key_flat, score_kernel):
    row_lead = QCONV - 1
    heads = score_kernel.shape[0]
    ext_count = query_rows.shape[0]
    row_count = ext_count - row_lead
    near = lax.dynamic_slice_in_dim(key_flat, query_first + 4, ext_count + QCONV - 2, 0)
    query_heads = query_rows.reshape(ext_count, heads, -1).astype(jnp.float32)
    near_heads = near.reshape(near.shape[0], heads, -1).astype(jnp.float32)
    scale = query_heads.shape[2] ** (-0.5)
    diagonals = [
        jnp.sum(query_heads * near_heads[lag - 1 : lag - 1 + ext_count], axis=2) * scale
        for lag in range(1, QCONV)
    ]
    band = []
    for gap in range(QCONV - 1):
        acc = jnp.zeros((row_count, heads), jnp.float32)
        for row_lag in range(gap + 1, QCONV):
            for col_lag in range(row_lag - gap):
                lag = row_lag - col_lag - gap
                acc = acc - score_kernel[None, :, row_lag, col_lag] * diagonals[lag - 1][
                    row_lead - row_lag : row_lead - row_lag + row_count
                ]
        band.append(acc.T)
    return jnp.stack(band)


def attend_chunk(shifted, band, query_first, key_pad, score_kernel, value_heads, head_mixing):
    row_count, heads = shifted.shape[:2]
    seq_len = value_heads.shape[0]
    shifted_t = jnp.transpose(shifted, (1, 2, 3, 0)).reshape((heads, -1, row_count))
    convolved = conv_logits(shifted_t, score_kernel, key_pad)
    query_pos = query_first + lax.iota(jnp.int32, row_count)
    gap = query_pos[None, :] - lax.iota(jnp.int32, seq_len)[:, None]
    for lag in range(QCONV - 1):
        convolved = convolved + jnp.where(gap == lag, band[lag][:, None, :], 0.0)
    logits = jnp.where(gap >= 0, convolved, lowest)
    peak = jnp.max(logits, axis=1, keepdims=True)
    expd = jnp.exp(logits - peak)
    probabilities = expd / jnp.sum(expd, axis=1, keepdims=True)
    grouped = probabilities.reshape(heads // GROUP, GROUP, seq_len, row_count)
    weights = head_mixing.reshape(heads // GROUP, GROUP, GROUP)
    mixed_probs = jnp.zeros_like(grouped)
    for source in range(GROUP):
        mixed_probs = mixed_probs + weights[:, :, source, None, None] * grouped[:, source, None]
    mixed_probs = mixed_probs.reshape(heads, seq_len, row_count).astype(jnp.bfloat16)
    return jnp.einsum(
        "hki,khd->ihd", mixed_probs, value_heads, preferred_element_type=jnp.float32
    )


def normalize(weighted, gain_local):
    factor = lax.rsqrt(jnp.mean(weighted * weighted, axis=2, keepdims=True) + epsilon)
    return (
        (weighted * factor * gain_local[None]).astype(jnp.bfloat16).reshape(weighted.shape[0], -1)
    )


def shards(query_states, key_states, value_states, score_kernel, head_mixing, head_gain):
    groups = lax.axis_size("uly")
    stacked = jnp.stack([query_states, key_states, value_states])
    stacked = stacked.reshape(stacked.shape[:2] + (groups, -1))
    stacked = jnp.transpose(stacked, (2, 0, 1, 3))
    pieces = exchanged(
        lambda group: lax.dynamic_index_in_dim(stacked, group, 0, keepdims=False), "uly"
    )
    pieces = jnp.moveaxis(pieces, 0, 1)
    query_local, key_local, value_local = pieces.reshape(
        (pieces.shape[0], -1, pieces.shape[-1])
    )
    shard_rows = query_local.shape[0]
    width = query_local.shape[1]
    row_lead = QCONV - 1
    heads = score_kernel.shape[0]
    head_dim = width // heads
    ctx_place = lax.axis_index("ctx")
    query_first = ctx_place * shard_rows
    earlier = passed_along(query_local[shard_rows - row_lead :], "ctx", 1)
    query_ext = jnp.concatenate([earlier, query_local], axis=0)
    key_all = gathered(key_local, "ctx").reshape((-1, width))
    key_all, value_local = lax.optimization_barrier((key_all, value_local))
    value_all = gathered(value_local, "ctx").reshape((-1, width))
    seq_len = key_all.shape[0]
    key_pad = jnp.concatenate(
        [jnp.zeros((KEY_BLOCK, width), key_all.dtype), key_all], axis=0
    )
    edge = jnp.zeros((8, width), key_all.dtype)
    key_flat = jnp.concatenate([edge, key_all, edge], axis=0)
    band = band_terms(query_ext, query_first, key_flat, score_kernel)
    query_heads = query_ext.reshape(shard_rows + row_lead, heads, head_dim)
    shifted = jnp.stack(
        [query_heads[row_lead - lag : row_lead - lag + shard_rows] for lag in range(QCONV)], axis=2
    )
    value_heads = value_all.reshape(seq_len, heads, head_dim)
    chunk = min(ROW_CHUNK * KEY_BLOCK * 8 // seq_len, shard_rows)
    if chunk == shard_rows:
        weighted = attend_chunk(
            shifted, band, query_first, key_pad, score_kernel, value_heads, head_mixing
        )
    else:
        chunks = shard_rows // chunk

        def one_chunk(index):
            start = index * chunk
            return attend_chunk(
                lax.dynamic_slice_in_dim(shifted, start, chunk, 0),
                lax.dynamic_slice_in_dim(band, start, chunk, 2),
                query_first + start,
                key_pad,
                score_kernel,
                value_heads,
                head_mixing,
            )

        weighted = lax.map(one_chunk, jnp.arange(chunks, dtype=jnp.int32))
        weighted = weighted.reshape((shard_rows,) + weighted.shape[2:])
    gain_local = head_gain.reshape(heads, head_dim)
    attended = normalize(weighted, gain_local)
    block_rows = shard_rows // groups
    returned = exchanged(
        lambda group: lax.dynamic_slice_in_dim(attended, group * block_rows, block_rows, 0),
        "uly",
    )
    return jnp.moveaxis(returned, 0, 1).reshape((block_rows, -1))


def solution(mesh):
    placed = (
        P(("ctx", "uly"), None),
        P(("ctx", "uly"), None),
        P(("ctx", "uly"), None),
        P("uly", None, None),
        P("uly", None),
        P("uly"),
    )
    return jax.shard_map(
        shards, mesh=mesh, in_specs=placed, out_specs=P(("ctx", "uly"), None), check_vma=False
    )
```

```python
import jax
import jax.numpy as jnp
from jax import lax
from jax.experimental import pallas as pl
from jax.experimental.pallas import tpu as pltpu
from jax.sharding import PartitionSpec as P

GROUP = 4
QCONV = 6
KCONV = 11
KEY_BLOCK = 128
KEY_SPAN = 1024
ROW_CHUNK = 128


lowest = -1e30
epsilon = 1e-06


def passed_along(shard, axis, by):
    peers = lax.axis_size(axis)
    pairs = [(i, i + by) for i in range(peers) if 0 <= i + by < peers]
    return lax.ppermute(shard, axis, pairs)


def exchanged(pieces_of, axis):
    peers = lax.axis_size(axis)
    place = lax.axis_index(axis)
    received = [pieces_of(place)]
    for shift in range(1, peers):
        outgoing = pieces_of((place + shift) % peers)
        pairs = [(i, (i + shift) % peers) for i in range(peers)]
        received.append(lax.ppermute(outgoing, axis, pairs))
    order = (place - jnp.arange(peers, dtype=jnp.int32)) % peers
    return jnp.take(jnp.stack(received), order, axis=0)


def gathered(shard, axis):
    peers = lax.axis_size(axis)
    place = lax.axis_index(axis)
    if peers & (peers - 1):
        return lax.all_gather(shard, axis, axis=0, tiled=False)
    bits = peers.bit_length() - 1
    held = shard[None]
    for level in reversed(range(bits)):
        bit = 1 << level
        incoming = lax.ppermute(held, axis, [(i, i ^ bit) for i in range(peers)])
        upper = (place & bit) != 0
        held = jnp.where(
            upper,
            jnp.concatenate([incoming, held], axis=0),
            jnp.concatenate([held, incoming], axis=0),
        )
    held = held.reshape((2,) * bits + shard.shape)
    return jnp.transpose(held, tuple(reversed(range(bits))) + tuple(range(bits, held.ndim)))


def logits_kernel(taps_ref, query_ref, keys_ref, out_ref, high_ref, low_ref, conv_ref):
    head = pl.program_id(0)
    group = pl.program_id(1)
    edge = 16

    @pl.when(group == 0)
    def _():
        lane = lax.broadcasted_iota(jnp.int32, (1, 2 * KEY_BLOCK), 1)
        for row_lag in range(QCONV):
            row = jnp.zeros(lane.shape, jnp.float32)
            for col_lag in range(KCONV):
                tap = taps_ref[(head * QCONV + row_lag) * KCONV + col_lag]
                row = jnp.where(lane == KEY_BLOCK - col_lag, tap, row)
            toeplitz = pltpu.roll(
                jnp.broadcast_to(row, (KEY_BLOCK, 2 * KEY_BLOCK)), 0, 1, stride=1, stride_axis=0
            )
            high = toeplitz.astype(jnp.bfloat16)
            low = (toeplitz - high.astype(jnp.float32)).astype(jnp.bfloat16)
            high_ref[row_lag * KEY_BLOCK : (row_lag + 1) * KEY_BLOCK] = high[:, KEY_BLOCK:]
            low_ref[row_lag * KEY_BLOCK : (row_lag + 1) * KEY_BLOCK] = low[:, KEY_BLOCK:]
            top = QCONV * KEY_BLOCK + row_lag * edge
            high_ref[top : top + edge] = high[:edge, :KEY_BLOCK]
            low_ref[top : top + edge] = low[:edge, :KEY_BLOCK]

    blocks = conv_ref.shape[1] // KEY_BLOCK
    body = QCONV * KEY_BLOCK
    for block in range(blocks):
        start = pl.multiple_of((group * blocks + block) * KEY_BLOCK, KEY_BLOCK)
        before = keys_ref[pl.ds(start, KEY_BLOCK), :]
        current = keys_ref[pl.ds(start + KEY_BLOCK, KEY_BLOCK), :]
        conv_body = jnp.dot(
            high_ref[:body], current, preferred_element_type=jnp.float32
        ) + jnp.dot(low_ref[:body], current, preferred_element_type=jnp.float32)
        conv_top = jnp.dot(
            high_ref[body:], before, preferred_element_type=jnp.float32
        ) + jnp.dot(low_ref[body:], before, preferred_element_type=jnp.float32)
        base = block * KEY_BLOCK
        for row_lag in range(QCONV):
            first = row_lag * KEY_BLOCK
            head_rows = conv_body[first : first + edge] + conv_top[
                row_lag * edge : (row_lag + 1) * edge
            ]
            rest_rows = conv_body[first + edge : first + KEY_BLOCK]
            cols = slice(row_lag * KEY_BLOCK, (row_lag + 1) * KEY_BLOCK)
            for part, rows in ((head_rows, slice(base, base + edge)),
                               (rest_rows, slice(base + edge, base + KEY_BLOCK))):
                part_high = part.astype(jnp.bfloat16)
                part_low = (part - part_high.astype(jnp.float32)).astype(jnp.bfloat16)
                conv_ref[0, rows, cols] = part_high
                conv_ref[1, rows, cols] = part_low
    query = query_ref[0]
    out_ref[0] = jnp.dot(conv_ref[0], query, preferred_element_type=jnp.float32) + jnp.dot(
        conv_ref[1], query, preferred_element_type=jnp.float32
    )


def conv_logits(shifted_t, score_kernel, key_pad):
    heads, contract, row_count = shifted_t.shape
    seq_len = key_pad.shape[0] - KEY_BLOCK
    head_dim = key_pad.shape[1] // heads
    span = min(seq_len, KEY_SPAN)
    taps = (score_kernel * head_dim ** (-0.5)).reshape(-1)
    return pl.pallas_call(
        logits_kernel,
        grid=(heads, seq_len // span),
        in_specs=[
            pl.BlockSpec(memory_space=pltpu.SMEM),
            pl.BlockSpec((1, contract, row_count), lambda h, g: (h, 0, 0)),
            pl.BlockSpec((key_pad.shape[0], head_dim), lambda h, g: (0, h)),
        ],
        out_specs=pl.BlockSpec((1, span, row_count), lambda h, g: (h, g, 0)),
        out_shape=jax.ShapeDtypeStruct((heads, seq_len, row_count), jnp.float32),
        scratch_shapes=[
            pltpu.VMEM((QCONV * (KEY_BLOCK + 16), KEY_BLOCK), jnp.bfloat16),
            pltpu.VMEM((QCONV * (KEY_BLOCK + 16), KEY_BLOCK), jnp.bfloat16),
            pltpu.VMEM((2, span, QCONV * head_dim), jnp.bfloat16),
        ],
    )(taps, shifted_t, key_pad)


def post_kernel(first_ref, mix_ref, logits_ref, band_ref, values_ref, out_ref, probs_ref):
    heads, seq_len, rows = logits_ref.shape
    head_dim = out_ref.shape[1]
    gap = (
        first_ref[0]
        + lax.broadcasted_iota(jnp.int32, (seq_len, rows), 1)
        - lax.broadcasted_iota(jnp.int32, (seq_len, rows), 0)
    )
    for head in range(heads):
        convolved = logits_ref[head]
        for lag in range(QCONV - 1):
            convolved = convolved + jnp.where(gap == lag, band_ref[head, lag : lag + 1, :], 0.0)
        logits = jnp.where(gap >= 0, convolved, lowest)
        peak = jnp.max(logits, axis=0, keepdims=True)
        expd = jnp.exp(logits - peak)
        probs_ref[head] = expd / jnp.sum(expd, axis=0, keepdims=True)
    for head in range(heads):
        first_head = head // GROUP * GROUP
        mixed = jnp.zeros((seq_len, rows), jnp.float32)
        for source in range(GROUP):
            mixed = mixed + mix_ref[head * GROUP + source] * probs_ref[first_head + source]
        out_ref[head] = jnp.dot(
            values_ref[head * head_dim : (head + 1) * head_dim, :],
            mixed.astype(jnp.bfloat16),
            preferred_element_type=jnp.float32,
        )


def post_attend(convolved, band, query_first, values_t, head_mixing):
    heads, seq_len, row_count = convolved.shape
    head_dim = values_t.shape[0] // heads
    first = jnp.reshape(query_first, (1,)).astype(jnp.int32)
    return pl.pallas_call(
        post_kernel,
        in_specs=[
            pl.BlockSpec(memory_space=pltpu.SMEM),
            pl.BlockSpec(memory_space=pltpu.SMEM),
            pl.BlockSpec(memory_space=pltpu.VMEM),
            pl.BlockSpec(memory_space=pltpu.VMEM),
            pl.BlockSpec(memory_space=pltpu.VMEM),
        ],
        out_specs=pl.BlockSpec(memory_space=pltpu.VMEM),
        out_shape=jax.ShapeDtypeStruct((heads, head_dim, row_count), jnp.float32),
        scratch_shapes=[pltpu.VMEM((heads, seq_len, row_count), jnp.float32)],
    )(first, head_mixing.reshape(-1), convolved, jnp.transpose(band, (1, 0, 2)), values_t)


def band_terms(query_rows, query_first, key_flat, score_kernel):
    row_lead = QCONV - 1
    heads = score_kernel.shape[0]
    ext_count = query_rows.shape[0]
    row_count = ext_count - row_lead
    near = lax.dynamic_slice_in_dim(key_flat, query_first + 4, ext_count + QCONV - 2, 0)
    query_heads = query_rows.reshape(ext_count, heads, -1).astype(jnp.float32)
    near_heads = near.reshape(near.shape[0], heads, -1).astype(jnp.float32)
    scale = query_heads.shape[2] ** (-0.5)
    diagonals = [
        jnp.sum(query_heads * near_heads[lag - 1 : lag - 1 + ext_count], axis=2) * scale
        for lag in range(1, QCONV)
    ]
    band = []
    for gap in range(QCONV - 1):
        acc = jnp.zeros((row_count, heads), jnp.float32)
        for row_lag in range(gap + 1, QCONV):
            for col_lag in range(row_lag - gap):
                lag = row_lag - col_lag - gap
                acc = acc - score_kernel[None, :, row_lag, col_lag] * diagonals[lag - 1][
                    row_lead - row_lag : row_lead - row_lag + row_count
                ]
        band.append(acc.T)
    return jnp.stack(band)


def attend_chunk(shifted, band, query_first, key_pad, score_kernel, value_heads, head_mixing):
    row_count, heads = shifted.shape[:2]
    shifted_t = jnp.transpose(shifted, (1, 2, 3, 0)).reshape((heads, -1, row_count))
    convolved = conv_logits(shifted_t, score_kernel, key_pad)
    weighted_t = post_attend(convolved, band, query_first, value_heads, head_mixing)
    return jnp.transpose(weighted_t, (2, 0, 1))


def normalize(weighted, gain_local):
    factor = lax.rsqrt(jnp.mean(weighted * weighted, axis=2, keepdims=True) + epsilon)
    return (
        (weighted * factor * gain_local[None]).astype(jnp.bfloat16).reshape(weighted.shape[0], -1)
    )


def shards(query_states, key_states, value_states, score_kernel, head_mixing, head_gain):
    groups = lax.axis_size("uly")
    stacked = jnp.stack([query_states, key_states, value_states])
    group_width = stacked.shape[2] // groups
    pieces = exchanged(
        lambda group: lax.dynamic_slice_in_dim(stacked, group * group_width, group_width, 2),
        "uly",
    )
    pieces = jnp.moveaxis(pieces, 0, 1)
    query_local, key_local, value_local = pieces.reshape(
        (pieces.shape[0], -1, pieces.shape[-1])
    )
    shard_rows = query_local.shape[0]
    width = query_local.shape[1]
    row_lead = QCONV - 1
    heads = score_kernel.shape[0]
    head_dim = width // heads
    ctx_place = lax.axis_index("ctx")
    query_first = ctx_place * shard_rows
    earlier = passed_along(query_local[shard_rows - row_lead :], "ctx", 1)
    query_ext = jnp.concatenate([earlier, query_local], axis=0)
    key_all = gathered(key_local, "ctx").reshape((-1, width))
    key_all, value_local = lax.optimization_barrier((key_all, value_local))
    value_all = gathered(value_local, "ctx").reshape((-1, width))
    seq_len = key_all.shape[0]
    key_pad = jnp.concatenate(
        [jnp.zeros((KEY_BLOCK, width), key_all.dtype), key_all], axis=0
    )
    edge = jnp.zeros((8, width), key_all.dtype)
    key_flat = jnp.concatenate([edge, key_all, edge], axis=0)
    band = band_terms(query_ext, query_first, key_flat, score_kernel)
    query_heads = query_ext.reshape(shard_rows + row_lead, heads, head_dim)
    shifted = jnp.stack(
        [query_heads[row_lead - lag : row_lead - lag + shard_rows] for lag in range(QCONV)], axis=2
    )
    value_heads = value_all.T
    chunk = min(ROW_CHUNK * KEY_BLOCK * 8 // seq_len, shard_rows)
    if chunk == shard_rows:
        weighted = attend_chunk(
            shifted, band, query_first, key_pad, score_kernel, value_heads, head_mixing
        )
    else:
        chunks = shard_rows // chunk

        def one_chunk(index):
            start = index * chunk
            return attend_chunk(
                lax.dynamic_slice_in_dim(shifted, start, chunk, 0),
                lax.dynamic_slice_in_dim(band, start, chunk, 2),
                query_first + start,
                key_pad,
                score_kernel,
                value_heads,
                head_mixing,
            )

        weighted = lax.map(one_chunk, jnp.arange(chunks, dtype=jnp.int32))
        weighted = weighted.reshape((shard_rows,) + weighted.shape[2:])
    gain_local = head_gain.reshape(heads, head_dim)
    attended = normalize(weighted, gain_local)
    block_rows = shard_rows // groups
    returned = exchanged(
        lambda group: lax.dynamic_slice_in_dim(attended, group * block_rows, block_rows, 0),
        "uly",
    )
    return jnp.moveaxis(returned, 0, 1).reshape((block_rows, -1))


def solution(mesh):
    placed = (
        P(("ctx", "uly"), None),
        P(("ctx", "uly"), None),
        P(("ctx", "uly"), None),
        P("uly", None, None),
        P("uly", None),
        P("uly"),
    )
    return jax.shard_map(
        shards, mesh=mesh, in_specs=placed, out_specs=P(("ctx", "uly"), None), check_vma=False
    )
```

```python
import jax
import jax.numpy as jnp
from jax import lax
from jax.experimental import pallas as pl
from jax.experimental.pallas import tpu as pltpu
from jax.sharding import PartitionSpec as P

GROUP = 4
QCONV = 6
KCONV = 11
KEY_BLOCK = 128
KEY_SPAN = 1024
ROW_CHUNK = 128


lowest = -1e30
epsilon = 1e-06


def passed_along(shard, axis, by):
    peers = lax.axis_size(axis)
    pairs = [(i, i + by) for i in range(peers) if 0 <= i + by < peers]
    return lax.ppermute(shard, axis, pairs)


def exchanged(pieces_of, axis):
    peers = lax.axis_size(axis)
    place = lax.axis_index(axis)
    received = [pieces_of(place)]
    for shift in range(1, peers):
        outgoing = pieces_of((place + shift) % peers)
        pairs = [(i, (i + shift) % peers) for i in range(peers)]
        received.append(lax.ppermute(outgoing, axis, pairs))
    order = (place - jnp.arange(peers, dtype=jnp.int32)) % peers
    return jnp.take(jnp.stack(received), order, axis=0)


def gathered(shard, axis):
    peers = lax.axis_size(axis)
    place = lax.axis_index(axis)
    if peers & (peers - 1):
        return lax.all_gather(shard, axis, axis=0, tiled=False)
    bits = peers.bit_length() - 1
    held = shard[None]
    for level in reversed(range(bits)):
        bit = 1 << level
        incoming = lax.ppermute(held, axis, [(i, i ^ bit) for i in range(peers)])
        upper = (place & bit) != 0
        held = jnp.where(
            upper,
            jnp.concatenate([incoming, held], axis=0),
            jnp.concatenate([held, incoming], axis=0),
        )
    held = held.reshape((2,) * bits + shard.shape)
    return jnp.transpose(held, tuple(reversed(range(bits))) + tuple(range(bits, held.ndim)))


def logits_kernel(taps_ref, query_ref, keys_ref, out_ref, high_ref, low_ref, conv_ref):
    head = pl.program_id(0)
    group = pl.program_id(1)
    edge = 16

    @pl.when(group == 0)
    def _():
        lane = lax.broadcasted_iota(jnp.int32, (1, 2 * KEY_BLOCK), 1)
        for row_lag in range(QCONV):
            row = jnp.zeros(lane.shape, jnp.float32)
            for col_lag in range(KCONV):
                tap = taps_ref[(head * QCONV + row_lag) * KCONV + col_lag]
                row = jnp.where(lane == KEY_BLOCK - col_lag, tap, row)
            toeplitz = pltpu.roll(
                jnp.broadcast_to(row, (KEY_BLOCK, 2 * KEY_BLOCK)), 0, 1, stride=1, stride_axis=0
            )
            high = toeplitz.astype(jnp.bfloat16)
            low = (toeplitz - high.astype(jnp.float32)).astype(jnp.bfloat16)
            high_ref[row_lag * KEY_BLOCK : (row_lag + 1) * KEY_BLOCK] = high[:, KEY_BLOCK:]
            low_ref[row_lag * KEY_BLOCK : (row_lag + 1) * KEY_BLOCK] = low[:, KEY_BLOCK:]
            top = QCONV * KEY_BLOCK + row_lag * edge
            high_ref[top : top + edge] = high[:edge, :KEY_BLOCK]
            low_ref[top : top + edge] = low[:edge, :KEY_BLOCK]

    blocks = conv_ref.shape[1] // KEY_BLOCK
    body = QCONV * KEY_BLOCK
    for block in range(blocks):
        start = pl.multiple_of((group * blocks + block) * KEY_BLOCK, KEY_BLOCK)
        before_start = pl.multiple_of(jnp.maximum(start - KEY_BLOCK, 0), KEY_BLOCK)
        before = keys_ref[pl.ds(before_start, KEY_BLOCK), :]
        before = jnp.where(start > 0, before, jnp.zeros(before.shape, before.dtype))
        current = keys_ref[pl.ds(start, KEY_BLOCK), :]
        conv_body = jnp.dot(
            high_ref[:body], current, preferred_element_type=jnp.float32
        ) + jnp.dot(low_ref[:body], current, preferred_element_type=jnp.float32)
        conv_top = jnp.dot(
            high_ref[body:], before, preferred_element_type=jnp.float32
        ) + jnp.dot(low_ref[body:], before, preferred_element_type=jnp.float32)
        base = block * KEY_BLOCK
        for row_lag in range(QCONV):
            first = row_lag * KEY_BLOCK
            head_rows = conv_body[first : first + edge] + conv_top[
                row_lag * edge : (row_lag + 1) * edge
            ]
            rest_rows = conv_body[first + edge : first + KEY_BLOCK]
            cols = slice(row_lag * KEY_BLOCK, (row_lag + 1) * KEY_BLOCK)
            for part, rows in ((head_rows, slice(base, base + edge)),
                               (rest_rows, slice(base + edge, base + KEY_BLOCK))):
                part_high = part.astype(jnp.bfloat16)
                part_low = (part - part_high.astype(jnp.float32)).astype(jnp.bfloat16)
                conv_ref[0, rows, cols] = part_high
                conv_ref[1, rows, cols] = part_low
    query = query_ref[0]
    out_ref[0] = jnp.dot(conv_ref[0], query, preferred_element_type=jnp.float32) + jnp.dot(
        conv_ref[1], query, preferred_element_type=jnp.float32
    )


def conv_logits(shifted_t, score_kernel, key_pad):
    heads, contract, row_count = shifted_t.shape
    seq_len = key_pad.shape[0]
    head_dim = key_pad.shape[1] // heads
    span = min(seq_len, KEY_SPAN)
    taps = (score_kernel * head_dim ** (-0.5)).reshape(-1)
    return pl.pallas_call(
        logits_kernel,
        grid=(heads, seq_len // span),
        in_specs=[
            pl.BlockSpec(memory_space=pltpu.SMEM),
            pl.BlockSpec((1, contract, row_count), lambda h, g: (h, 0, 0)),
            pl.BlockSpec((key_pad.shape[0], head_dim), lambda h, g: (0, h)),
        ],
        out_specs=pl.BlockSpec((1, span, row_count), lambda h, g: (h, g, 0)),
        out_shape=jax.ShapeDtypeStruct((heads, seq_len, row_count), jnp.float32),
        scratch_shapes=[
            pltpu.VMEM((QCONV * (KEY_BLOCK + 16), KEY_BLOCK), jnp.bfloat16),
            pltpu.VMEM((QCONV * (KEY_BLOCK + 16), KEY_BLOCK), jnp.bfloat16),
            pltpu.VMEM((2, span, QCONV * head_dim), jnp.bfloat16),
        ],
    )(taps, shifted_t, key_pad)


def band_terms(query_rows, query_first, key_flat, score_kernel):
    row_lead = QCONV - 1
    heads = score_kernel.shape[0]
    ext_count = query_rows.shape[0]
    row_count = ext_count - row_lead
    near = lax.dynamic_slice_in_dim(key_flat, query_first + 4, ext_count + QCONV - 2, 0)
    query_heads = query_rows.reshape(ext_count, heads, -1).astype(jnp.float32)
    near_heads = near.reshape(near.shape[0], heads, -1).astype(jnp.float32)
    scale = query_heads.shape[2] ** (-0.5)
    diagonals = [
        jnp.sum(query_heads * near_heads[lag - 1 : lag - 1 + ext_count], axis=2) * scale
        for lag in range(1, QCONV)
    ]
    band = []
    for gap in range(QCONV - 1):
        acc = jnp.zeros((row_count, heads), jnp.float32)
        for row_lag in range(gap + 1, QCONV):
            for col_lag in range(row_lag - gap):
                lag = row_lag - col_lag - gap
                acc = acc - score_kernel[None, :, row_lag, col_lag] * diagonals[lag - 1][
                    row_lead - row_lag : row_lead - row_lag + row_count
                ]
        band.append(acc.T)
    return jnp.stack(band)


def attend_chunk(shifted, band, query_first, key_pad, score_kernel, value_heads, head_mixing):
    row_count, heads = shifted.shape[:2]
    seq_len = value_heads.shape[0]
    shifted_t = jnp.transpose(shifted, (1, 2, 3, 0)).reshape((heads, -1, row_count))
    convolved = conv_logits(shifted_t, score_kernel, key_pad)
    query_pos = query_first + lax.iota(jnp.int32, row_count)
    gap = query_pos[None, :] - lax.iota(jnp.int32, seq_len)[:, None]
    for lag in range(QCONV - 1):
        convolved = convolved + jnp.where(gap == lag, band[lag][:, None, :], 0.0)
    logits = jnp.where(gap >= 0, convolved, lowest)
    peak = jnp.max(logits, axis=1, keepdims=True)
    expd = jnp.exp(logits - peak)
    probabilities = expd / jnp.sum(expd, axis=1, keepdims=True)
    grouped = probabilities.reshape(heads // GROUP, GROUP, seq_len, row_count)
    weights = head_mixing.reshape(heads // GROUP, GROUP, GROUP)
    mixed_probs = jnp.zeros_like(grouped)
    for source in range(GROUP):
        mixed_probs = mixed_probs + weights[:, :, source, None, None] * grouped[:, source, None]
    mixed_probs = mixed_probs.reshape(heads, seq_len, row_count).astype(jnp.bfloat16)
    return jnp.einsum(
        "hki,khd->ihd", mixed_probs, value_heads, preferred_element_type=jnp.float32
    )


def normalize(weighted, gain_local):
    factor = lax.rsqrt(jnp.mean(weighted * weighted, axis=2, keepdims=True) + epsilon)
    return (
        (weighted * factor * gain_local[None]).astype(jnp.bfloat16).reshape(weighted.shape[0], -1)
    )


def shards(query_states, key_states, value_states, score_kernel, head_mixing, head_gain):
    groups = lax.axis_size("uly")
    stacked = jnp.stack([query_states, key_states, value_states])
    group_width = stacked.shape[2] // groups
    pieces = exchanged(
        lambda group: lax.dynamic_slice_in_dim(stacked, group * group_width, group_width, 2),
        "uly",
    )
    pieces = jnp.moveaxis(pieces, 0, 1)
    query_local, key_local, value_local = pieces.reshape(
        (pieces.shape[0], -1, pieces.shape[-1])
    )
    shard_rows = query_local.shape[0]
    width = query_local.shape[1]
    row_lead = QCONV - 1
    heads = score_kernel.shape[0]
    head_dim = width // heads
    ctx_place = lax.axis_index("ctx")
    query_first = ctx_place * shard_rows
    earlier = passed_along(query_local[shard_rows - row_lead :], "ctx", 1)
    query_ext = jnp.concatenate([earlier, query_local], axis=0)
    key_all = gathered(key_local, "ctx").reshape((-1, width))
    key_all, value_local = lax.optimization_barrier((key_all, value_local))
    value_all = gathered(value_local, "ctx").reshape((-1, width))
    seq_len = key_all.shape[0]
    key_pad = key_all
    edge = jnp.zeros((8, width), key_all.dtype)
    key_flat = jnp.concatenate([edge, key_all, edge], axis=0)
    band = band_terms(query_ext, query_first, key_flat, score_kernel)
    query_heads = query_ext.reshape(shard_rows + row_lead, heads, head_dim)
    shifted = jnp.stack(
        [query_heads[row_lead - lag : row_lead - lag + shard_rows] for lag in range(QCONV)], axis=2
    )
    value_heads = value_all.reshape(seq_len, heads, head_dim)
    chunk = min(ROW_CHUNK * KEY_BLOCK * 8 // seq_len, shard_rows)
    if chunk == shard_rows:
        weighted = attend_chunk(
            shifted, band, query_first, key_pad, score_kernel, value_heads, head_mixing
        )
    else:
        chunks = shard_rows // chunk

        def one_chunk(index):
            start = index * chunk
            return attend_chunk(
                lax.dynamic_slice_in_dim(shifted, start, chunk, 0),
                lax.dynamic_slice_in_dim(band, start, chunk, 2),
                query_first + start,
                key_pad,
                score_kernel,
                value_heads,
                head_mixing,
            )

        weighted = lax.map(one_chunk, jnp.arange(chunks, dtype=jnp.int32))
        weighted = weighted.reshape((shard_rows,) + weighted.shape[2:])
    gain_local = head_gain.reshape(heads, head_dim)
    attended = normalize(weighted, gain_local)
    block_rows = shard_rows // groups
    returned = exchanged(
        lambda group: lax.dynamic_slice_in_dim(attended, group * block_rows, block_rows, 0),
        "uly",
    )
    return jnp.moveaxis(returned, 0, 1).reshape((block_rows, -1))


def solution(mesh):
    placed = (
        P(("ctx", "uly"), None),
        P(("ctx", "uly"), None),
        P(("ctx", "uly"), None),
        P("uly", None, None),
        P("uly", None),
        P("uly"),
    )
    return jax.shard_map(
        shards, mesh=mesh, in_specs=placed, out_specs=P(("ctx", "uly"), None), check_vma=False
    )
```

```python
import jax
import jax.numpy as jnp
from jax import lax
from jax.experimental import pallas as pl
from jax.experimental.pallas import tpu as pltpu
from jax.sharding import PartitionSpec as P

GROUP = 4
QCONV = 6
KCONV = 11
KEY_BLOCK = 128
KEY_SPAN = 1024
ROW_CHUNK = 128


lowest = -1e30
epsilon = 1e-06


def passed_along(shard, axis, by):
    peers = lax.axis_size(axis)
    pairs = [(i, i + by) for i in range(peers) if 0 <= i + by < peers]
    return lax.ppermute(shard, axis, pairs)


def exchanged(pieces_of, axis):
    peers = lax.axis_size(axis)
    place = lax.axis_index(axis)
    received = [pieces_of(place)]
    for shift in range(1, peers):
        outgoing = pieces_of((place + shift) % peers)
        pairs = [(i, (i + shift) % peers) for i in range(peers)]
        received.append(lax.ppermute(outgoing, axis, pairs))
    order = (place - jnp.arange(peers, dtype=jnp.int32)) % peers
    return jnp.take(jnp.stack(received), order, axis=0)


def gathered(shard, axis):
    peers = lax.axis_size(axis)
    place = lax.axis_index(axis)
    if peers & (peers - 1):
        return lax.all_gather(shard, axis, axis=0, tiled=False)
    bits = peers.bit_length() - 1
    held = shard[None]
    for level in range(bits):
        bit = 1 << level
        incoming = lax.ppermute(held, axis, [(i, i ^ bit) for i in range(peers)])
        upper = (place & bit) != 0
        held = jnp.where(
            upper,
            jnp.concatenate([incoming, held], axis=0),
            jnp.concatenate([held, incoming], axis=0),
        )
    return held.reshape((peers,) + shard.shape)


def logits_kernel(taps_ref, query_ref, keys_ref, out_ref, high_ref, low_ref, conv_ref):
    head = pl.program_id(0)
    group = pl.program_id(1)
    edge = 16

    @pl.when(group == 0)
    def _():
        lane = lax.broadcasted_iota(jnp.int32, (1, 2 * KEY_BLOCK), 1)
        for row_lag in range(QCONV):
            row = jnp.zeros(lane.shape, jnp.float32)
            for col_lag in range(KCONV):
                tap = taps_ref[(head * QCONV + row_lag) * KCONV + col_lag]
                row = jnp.where(lane == KEY_BLOCK - col_lag, tap, row)
            toeplitz = pltpu.roll(
                jnp.broadcast_to(row, (KEY_BLOCK, 2 * KEY_BLOCK)), 0, 1, stride=1, stride_axis=0
            )
            high = toeplitz.astype(jnp.bfloat16)
            low = (toeplitz - high.astype(jnp.float32)).astype(jnp.bfloat16)
            high_ref[row_lag * KEY_BLOCK : (row_lag + 1) * KEY_BLOCK] = high[:, KEY_BLOCK:]
            low_ref[row_lag * KEY_BLOCK : (row_lag + 1) * KEY_BLOCK] = low[:, KEY_BLOCK:]
            top = QCONV * KEY_BLOCK + row_lag * edge
            high_ref[top : top + edge] = high[:edge, :KEY_BLOCK]
            low_ref[top : top + edge] = low[:edge, :KEY_BLOCK]

    blocks = conv_ref.shape[1] // KEY_BLOCK
    body = QCONV * KEY_BLOCK
    for block in range(blocks):
        start = pl.multiple_of((group * blocks + block) * KEY_BLOCK, KEY_BLOCK)
        before_start = pl.multiple_of(jnp.maximum(start - KEY_BLOCK, 0), KEY_BLOCK)
        before = keys_ref[pl.ds(before_start, KEY_BLOCK), :]
        before = jnp.where(start > 0, before, jnp.zeros(before.shape, before.dtype))
        current = keys_ref[pl.ds(start, KEY_BLOCK), :]
        conv_body = jnp.dot(
            high_ref[:body], current, preferred_element_type=jnp.float32
        ) + jnp.dot(low_ref[:body], current, preferred_element_type=jnp.float32)
        conv_top = jnp.dot(
            high_ref[body:], before, preferred_element_type=jnp.float32
        ) + jnp.dot(low_ref[body:], before, preferred_element_type=jnp.float32)
        base = block * KEY_BLOCK
        for row_lag in range(QCONV):
            first = row_lag * KEY_BLOCK
            head_rows = conv_body[first : first + edge] + conv_top[
                row_lag * edge : (row_lag + 1) * edge
            ]
            rest_rows = conv_body[first + edge : first + KEY_BLOCK]
            cols = slice(row_lag * KEY_BLOCK, (row_lag + 1) * KEY_BLOCK)
            for part, rows in ((head_rows, slice(base, base + edge)),
                               (rest_rows, slice(base + edge, base + KEY_BLOCK))):
                part_high = part.astype(jnp.bfloat16)
                part_low = (part - part_high.astype(jnp.float32)).astype(jnp.bfloat16)
                conv_ref[0, rows, cols] = part_high
                conv_ref[1, rows, cols] = part_low
    query = query_ref[0]
    out_ref[0] = jnp.dot(conv_ref[0], query, preferred_element_type=jnp.float32) + jnp.dot(
        conv_ref[1], query, preferred_element_type=jnp.float32
    )


def conv_logits(shifted_t, score_kernel, key_pad):
    heads, contract, row_count = shifted_t.shape
    seq_len = key_pad.shape[0]
    head_dim = key_pad.shape[1] // heads
    span = min(seq_len, KEY_SPAN)
    taps = (score_kernel * head_dim ** (-0.5)).reshape(-1)
    return pl.pallas_call(
        logits_kernel,
        grid=(heads, seq_len // span),
        in_specs=[
            pl.BlockSpec(memory_space=pltpu.SMEM),
            pl.BlockSpec((1, contract, row_count), lambda h, g: (h, 0, 0)),
            pl.BlockSpec((key_pad.shape[0], head_dim), lambda h, g: (0, h)),
        ],
        out_specs=pl.BlockSpec((1, span, row_count), lambda h, g: (h, g, 0)),
        out_shape=jax.ShapeDtypeStruct((heads, seq_len, row_count), jnp.float32),
        scratch_shapes=[
            pltpu.VMEM((QCONV * (KEY_BLOCK + 16), KEY_BLOCK), jnp.bfloat16),
            pltpu.VMEM((QCONV * (KEY_BLOCK + 16), KEY_BLOCK), jnp.bfloat16),
            pltpu.VMEM((2, span, QCONV * head_dim), jnp.bfloat16),
        ],
    )(taps, shifted_t, key_pad)


def band_terms(query_rows, query_first, key_flat, score_kernel):
    row_lead = QCONV - 1
    heads = score_kernel.shape[0]
    ext_count = query_rows.shape[0]
    row_count = ext_count - row_lead
    near = lax.dynamic_slice_in_dim(key_flat, query_first + 4, ext_count + QCONV - 2, 0)
    query_heads = query_rows.reshape(ext_count, heads, -1).astype(jnp.float32)
    near_heads = near.reshape(near.shape[0], heads, -1).astype(jnp.float32)
    scale = query_heads.shape[2] ** (-0.5)
    diagonals = [
        jnp.sum(query_heads * near_heads[lag - 1 : lag - 1 + ext_count], axis=2) * scale
        for lag in range(1, QCONV)
    ]
    band = []
    for gap in range(QCONV - 1):
        acc = jnp.zeros((row_count, heads), jnp.float32)
        for row_lag in range(gap + 1, QCONV):
            for col_lag in range(row_lag - gap):
                lag = row_lag - col_lag - gap
                acc = acc - score_kernel[None, :, row_lag, col_lag] * diagonals[lag - 1][
                    row_lead - row_lag : row_lead - row_lag + row_count
                ]
        band.append(acc.T)
    return jnp.stack(band)


def attend_chunk(shifted, band, query_first, key_pad, score_kernel, value_heads, head_mixing):
    row_count, heads = shifted.shape[:2]
    seq_len = value_heads.shape[0]
    shifted_t = jnp.transpose(shifted, (1, 2, 3, 0)).reshape((heads, -1, row_count))
    convolved = conv_logits(shifted_t, score_kernel, key_pad)
    query_pos = query_first + lax.iota(jnp.int32, row_count)
    gap = query_pos[None, :] - lax.iota(jnp.int32, seq_len)[:, None]
    for lag in range(QCONV - 1):
        convolved = convolved + jnp.where(gap == lag, band[lag][:, None, :], 0.0)
    logits = jnp.where(gap >= 0, convolved, lowest)
    peak = jnp.max(logits, axis=1, keepdims=True)
    expd = jnp.exp(logits - peak)
    probabilities = expd / jnp.sum(expd, axis=1, keepdims=True)
    grouped = probabilities.reshape(heads // GROUP, GROUP, seq_len, row_count)
    weights = head_mixing.reshape(heads // GROUP, GROUP, GROUP)
    mixed_probs = jnp.zeros_like(grouped)
    for source in range(GROUP):
        mixed_probs = mixed_probs + weights[:, :, source, None, None] * grouped[:, source, None]
    mixed_probs = mixed_probs.reshape(heads, seq_len, row_count).astype(jnp.bfloat16)
    return jnp.einsum(
        "hki,khd->ihd", mixed_probs, value_heads, preferred_element_type=jnp.float32
    )


def normalize(weighted, gain_local):
    factor = lax.rsqrt(jnp.mean(weighted * weighted, axis=2, keepdims=True) + epsilon)
    return (
        (weighted * factor * gain_local[None]).astype(jnp.bfloat16).reshape(weighted.shape[0], -1)
    )


def shards(query_states, key_states, value_states, score_kernel, head_mixing, head_gain):
    groups = lax.axis_size("uly")
    stacked = jnp.stack([query_states, key_states, value_states])
    group_width = stacked.shape[2] // groups
    pieces = exchanged(
        lambda group: lax.dynamic_slice_in_dim(stacked, group * group_width, group_width, 2),
        "uly",
    )
    pieces = jnp.moveaxis(pieces, 0, 1)
    query_local, key_local, value_local = pieces.reshape(
        (pieces.shape[0], -1, pieces.shape[-1])
    )
    shard_rows = query_local.shape[0]
    width = query_local.shape[1]
    row_lead = QCONV - 1
    heads = score_kernel.shape[0]
    head_dim = width // heads
    ctx_place = lax.axis_index("ctx")
    query_first = ctx_place * shard_rows
    earlier = passed_along(query_local[shard_rows - row_lead :], "ctx", 1)
    query_ext = jnp.concatenate([earlier, query_local], axis=0)
    key_all = gathered(key_local, "ctx").reshape((-1, width))
    key_all, value_local = lax.optimization_barrier((key_all, value_local))
    value_all = gathered(value_local, "ctx").reshape((-1, width))
    seq_len = key_all.shape[0]
    key_pad = key_all
    edge = jnp.zeros((8, width), key_all.dtype)
    key_flat = jnp.concatenate([edge, key_all, edge], axis=0)
    band = band_terms(query_ext, query_first, key_flat, score_kernel)
    query_heads = query_ext.reshape(shard_rows + row_lead, heads, head_dim)
    shifted = jnp.stack(
        [query_heads[row_lead - lag : row_lead - lag + shard_rows] for lag in range(QCONV)], axis=2
    )
    value_heads = value_all.reshape(seq_len, heads, head_dim)
    chunk = min(ROW_CHUNK * KEY_BLOCK * 8 // seq_len, shard_rows)
    if chunk == shard_rows:
        weighted = attend_chunk(
            shifted, band, query_first, key_pad, score_kernel, value_heads, head_mixing
        )
    else:
        chunks = shard_rows // chunk

        def one_chunk(index):
            start = index * chunk
            return attend_chunk(
                lax.dynamic_slice_in_dim(shifted, start, chunk, 0),
                lax.dynamic_slice_in_dim(band, start, chunk, 2),
                query_first + start,
                key_pad,
                score_kernel,
                value_heads,
                head_mixing,
            )

        weighted = lax.map(one_chunk, jnp.arange(chunks, dtype=jnp.int32))
        weighted = weighted.reshape((shard_rows,) + weighted.shape[2:])
    gain_local = head_gain.reshape(heads, head_dim)
    attended = normalize(weighted, gain_local)
    block_rows = shard_rows // groups
    returned = exchanged(
        lambda group: lax.dynamic_slice_in_dim(attended, group * block_rows, block_rows, 0),
        "uly",
    )
    return jnp.moveaxis(returned, 0, 1).reshape((block_rows, -1))


def solution(mesh):
    placed = (
        P(("ctx", "uly"), None),
        P(("ctx", "uly"), None),
        P(("ctx", "uly"), None),
        P("uly", None, None),
        P("uly", None),
        P("uly"),
    )
    return jax.shard_map(
        shards, mesh=mesh, in_specs=placed, out_specs=P(("ctx", "uly"), None), check_vma=False
    )
```

```python
import jax
import jax.numpy as jnp
from jax import lax
from jax.experimental import pallas as pl
from jax.experimental.pallas import tpu as pltpu
from jax.sharding import PartitionSpec as P

GROUP = 4
QCONV = 6
KCONV = 11
KEY_BLOCK = 128
KEY_SPAN = 1024
ROW_CHUNK = 128


lowest = -1e30
epsilon = 1e-06


def passed_along(shard, axis, by):
    peers = lax.axis_size(axis)
    pairs = [(i, i + by) for i in range(peers) if 0 <= i + by < peers]
    return lax.ppermute(shard, axis, pairs)


def exchanged(pieces_of, axis):
    peers = lax.axis_size(axis)
    place = lax.axis_index(axis)
    received = [pieces_of(place)]
    for shift in range(1, peers):
        outgoing = pieces_of((place + shift) % peers)
        pairs = [(i, (i + shift) % peers) for i in range(peers)]
        received.append(lax.ppermute(outgoing, axis, pairs))
    order = (place - jnp.arange(peers, dtype=jnp.int32)) % peers
    return jnp.take(jnp.stack(received), order, axis=0)


def gathered(shard, axis):
    peers = lax.axis_size(axis)
    place = lax.axis_index(axis)
    if peers & (peers - 1):
        return lax.all_gather(shard, axis, axis=0, tiled=False)
    bits = peers.bit_length() - 1
    held = shard[None]
    for level in reversed(range(bits)):
        bit = 1 << level
        incoming = lax.ppermute(held, axis, [(i, i ^ bit) for i in range(peers)])
        upper = (place & bit) != 0
        held = jnp.where(
            upper,
            jnp.concatenate([incoming, held], axis=0),
            jnp.concatenate([held, incoming], axis=0),
        )
    held = held.reshape((2,) * bits + shard.shape)
    return jnp.transpose(held, tuple(reversed(range(bits))) + tuple(range(bits, held.ndim)))


def logits_kernel(taps_ref, query_ref, keys_ref, out_ref, high_ref, low_ref, conv_ref):
    head = pl.program_id(0)
    group = pl.program_id(1)
    edge = 16

    @pl.when(group == 0)
    def _():
        lane = lax.broadcasted_iota(jnp.int32, (1, 2 * KEY_BLOCK), 1)
        for row_lag in range(QCONV):
            row = jnp.zeros(lane.shape, jnp.float32)
            for col_lag in range(KCONV):
                tap = taps_ref[(head * QCONV + row_lag) * KCONV + col_lag]
                row = jnp.where(lane == KEY_BLOCK - col_lag, tap, row)
            toeplitz = pltpu.roll(
                jnp.broadcast_to(row, (KEY_BLOCK, 2 * KEY_BLOCK)), 0, 1, stride=1, stride_axis=0
            )
            high = toeplitz.astype(jnp.bfloat16)
            low = (toeplitz - high.astype(jnp.float32)).astype(jnp.bfloat16)
            high_ref[row_lag * KEY_BLOCK : (row_lag + 1) * KEY_BLOCK] = high[:, KEY_BLOCK:]
            low_ref[row_lag * KEY_BLOCK : (row_lag + 1) * KEY_BLOCK] = low[:, KEY_BLOCK:]
            top = QCONV * KEY_BLOCK + row_lag * edge
            high_ref[top : top + edge] = high[:edge, :KEY_BLOCK]
            low_ref[top : top + edge] = low[:edge, :KEY_BLOCK]

    blocks = conv_ref.shape[1] // KEY_BLOCK
    body = QCONV * KEY_BLOCK
    for block in range(blocks):
        start = pl.multiple_of((group * blocks + block) * KEY_BLOCK, KEY_BLOCK)
        before_start = pl.multiple_of(jnp.maximum(start - KEY_BLOCK, 0), KEY_BLOCK)
        before = keys_ref[pl.ds(before_start, KEY_BLOCK), :]
        before = jnp.where(start > 0, before, jnp.zeros(before.shape, before.dtype))
        current = keys_ref[pl.ds(start, KEY_BLOCK), :]
        conv_body = jnp.dot(
            high_ref[:body], current, preferred_element_type=jnp.float32
        ) + jnp.dot(low_ref[:body], current, preferred_element_type=jnp.float32)
        conv_top = jnp.dot(
            high_ref[body:], before, preferred_element_type=jnp.float32
        ) + jnp.dot(low_ref[body:], before, preferred_element_type=jnp.float32)
        base = block * KEY_BLOCK
        for row_lag in range(QCONV):
            first = row_lag * KEY_BLOCK
            head_rows = conv_body[first : first + edge] + conv_top[
                row_lag * edge : (row_lag + 1) * edge
            ]
            rest_rows = conv_body[first + edge : first + KEY_BLOCK]
            cols = slice(row_lag * KEY_BLOCK, (row_lag + 1) * KEY_BLOCK)
            for part, rows in ((head_rows, slice(base, base + edge)),
                               (rest_rows, slice(base + edge, base + KEY_BLOCK))):
                part_high = part.astype(jnp.bfloat16)
                part_low = (part - part_high.astype(jnp.float32)).astype(jnp.bfloat16)
                conv_ref[0, rows, cols] = part_high
                conv_ref[1, rows, cols] = part_low
    query = query_ref[0]
    dims = (((1,), (1,)), ((), ()))
    out_ref[0] = lax.dot_general(
        query, conv_ref[0], dims, preferred_element_type=jnp.float32
    ) + lax.dot_general(query, conv_ref[1], dims, preferred_element_type=jnp.float32)


def conv_logits(shifted_t, score_kernel, key_pad):
    heads, row_count, contract = shifted_t.shape
    seq_len = key_pad.shape[0]
    head_dim = key_pad.shape[1] // heads
    span = min(seq_len, KEY_SPAN)
    taps = (score_kernel * head_dim ** (-0.5)).reshape(-1)
    return pl.pallas_call(
        logits_kernel,
        grid=(heads, seq_len // span),
        in_specs=[
            pl.BlockSpec(memory_space=pltpu.SMEM),
            pl.BlockSpec((1, row_count, contract), lambda h, g: (h, 0, 0)),
            pl.BlockSpec((key_pad.shape[0], head_dim), lambda h, g: (0, h)),
        ],
        out_specs=pl.BlockSpec((1, row_count, span), lambda h, g: (h, 0, g)),
        out_shape=jax.ShapeDtypeStruct((heads, row_count, seq_len), jnp.float32),
        scratch_shapes=[
            pltpu.VMEM((QCONV * (KEY_BLOCK + 16), KEY_BLOCK), jnp.bfloat16),
            pltpu.VMEM((QCONV * (KEY_BLOCK + 16), KEY_BLOCK), jnp.bfloat16),
            pltpu.VMEM((2, span, QCONV * head_dim), jnp.bfloat16),
        ],
    )(taps, shifted_t, key_pad)


def band_terms(query_rows, query_first, key_flat, score_kernel):
    row_lead = QCONV - 1
    heads = score_kernel.shape[0]
    ext_count = query_rows.shape[0]
    row_count = ext_count - row_lead
    near = lax.dynamic_slice_in_dim(key_flat, query_first + 4, ext_count + QCONV - 2, 0)
    query_heads = query_rows.reshape(ext_count, heads, -1).astype(jnp.float32)
    near_heads = near.reshape(near.shape[0], heads, -1).astype(jnp.float32)
    scale = query_heads.shape[2] ** (-0.5)
    diagonals = [
        jnp.sum(query_heads * near_heads[lag - 1 : lag - 1 + ext_count], axis=2) * scale
        for lag in range(1, QCONV)
    ]
    band = []
    for gap in range(QCONV - 1):
        acc = jnp.zeros((row_count, heads), jnp.float32)
        for row_lag in range(gap + 1, QCONV):
            for col_lag in range(row_lag - gap):
                lag = row_lag - col_lag - gap
                acc = acc - score_kernel[None, :, row_lag, col_lag] * diagonals[lag - 1][
                    row_lead - row_lag : row_lead - row_lag + row_count
                ]
        band.append(acc.T)
    return jnp.stack(band)


def attend_chunk(shifted, band, query_first, key_pad, score_kernel, value_heads, head_mixing):
    row_count, heads = shifted.shape[:2]
    seq_len = value_heads.shape[0]
    shifted_t = jnp.transpose(shifted, (1, 0, 2, 3)).reshape((heads, row_count, -1))
    convolved = conv_logits(shifted_t, score_kernel, key_pad)
    query_pos = query_first + lax.iota(jnp.int32, row_count)
    gap = query_pos[:, None] - lax.iota(jnp.int32, seq_len)[None, :]
    for lag in range(QCONV - 1):
        convolved = convolved + jnp.where(gap == lag, band[lag][:, :, None], 0.0)
    logits = jnp.where(gap >= 0, convolved, lowest)
    peak = jnp.max(logits, axis=2, keepdims=True)
    expd = jnp.exp(logits - peak)
    probabilities = expd / jnp.sum(expd, axis=2, keepdims=True)
    grouped = probabilities.reshape(heads // GROUP, GROUP, row_count, seq_len)
    weights = head_mixing.reshape(heads // GROUP, GROUP, GROUP)
    mixed_probs = jnp.zeros_like(grouped)
    for source in range(GROUP):
        mixed_probs = mixed_probs + weights[:, :, source, None, None] * grouped[:, source, None]
    mixed_probs = mixed_probs.reshape(heads, row_count, seq_len).astype(jnp.bfloat16)
    return jnp.einsum(
        "hik,khd->ihd", mixed_probs, value_heads, preferred_element_type=jnp.float32
    )


def normalize(weighted, gain_local):
    factor = lax.rsqrt(jnp.mean(weighted * weighted, axis=2, keepdims=True) + epsilon)
    return (
        (weighted * factor * gain_local[None]).astype(jnp.bfloat16).reshape(weighted.shape[0], -1)
    )


def shards(query_states, key_states, value_states, score_kernel, head_mixing, head_gain):
    groups = lax.axis_size("uly")
    stacked = jnp.stack([query_states, key_states, value_states])
    group_width = stacked.shape[2] // groups
    pieces = exchanged(
        lambda group: lax.dynamic_slice_in_dim(stacked, group * group_width, group_width, 2),
        "uly",
    )
    pieces = jnp.moveaxis(pieces, 0, 1)
    query_local, key_local, value_local = pieces.reshape(
        (pieces.shape[0], -1, pieces.shape[-1])
    )
    shard_rows = query_local.shape[0]
    width = query_local.shape[1]
    row_lead = QCONV - 1
    heads = score_kernel.shape[0]
    head_dim = width // heads
    ctx_place = lax.axis_index("ctx")
    query_first = ctx_place * shard_rows
    earlier = passed_along(query_local[shard_rows - row_lead :], "ctx", 1)
    query_ext = jnp.concatenate([earlier, query_local], axis=0)
    key_all = gathered(key_local, "ctx").reshape((-1, width))
    key_all, value_local = lax.optimization_barrier((key_all, value_local))
    value_all = gathered(value_local, "ctx").reshape((-1, width))
    seq_len = key_all.shape[0]
    key_pad = key_all
    edge = jnp.zeros((8, width), key_all.dtype)
    key_flat = jnp.concatenate([edge, key_all, edge], axis=0)
    band = band_terms(query_ext, query_first, key_flat, score_kernel)
    query_heads = query_ext.reshape(shard_rows + row_lead, heads, head_dim)
    shifted = jnp.stack(
        [query_heads[row_lead - lag : row_lead - lag + shard_rows] for lag in range(QCONV)], axis=2
    )
    value_heads = value_all.reshape(seq_len, heads, head_dim)
    chunk = min(ROW_CHUNK * KEY_BLOCK * 8 // seq_len, shard_rows)
    if chunk == shard_rows:
        weighted = attend_chunk(
            shifted, band, query_first, key_pad, score_kernel, value_heads, head_mixing
        )
    else:
        chunks = shard_rows // chunk

        def one_chunk(index):
            start = index * chunk
            return attend_chunk(
                lax.dynamic_slice_in_dim(shifted, start, chunk, 0),
                lax.dynamic_slice_in_dim(band, start, chunk, 2),
                query_first + start,
                key_pad,
                score_kernel,
                value_heads,
                head_mixing,
            )

        weighted = lax.map(one_chunk, jnp.arange(chunks, dtype=jnp.int32))
        weighted = weighted.reshape((shard_rows,) + weighted.shape[2:])
    gain_local = head_gain.reshape(heads, head_dim)
    attended = normalize(weighted, gain_local)
    block_rows = shard_rows // groups
    returned = exchanged(
        lambda group: lax.dynamic_slice_in_dim(attended, group * block_rows, block_rows, 0),
        "uly",
    )
    return jnp.moveaxis(returned, 0, 1).reshape((block_rows, -1))


def solution(mesh):
    placed = (
        P(("ctx", "uly"), None),
        P(("ctx", "uly"), None),
        P(("ctx", "uly"), None),
        P("uly", None, None),
        P("uly", None),
        P("uly"),
    )
    return jax.shard_map(
        shards, mesh=mesh, in_specs=placed, out_specs=P(("ctx", "uly"), None), check_vma=False
    )
```

```python
import jax
import jax.numpy as jnp
from jax import lax
from jax.experimental import pallas as pl
from jax.experimental.pallas import tpu as pltpu
from jax.sharding import PartitionSpec as P

GROUP = 4
QCONV = 6
KCONV = 11
KEY_BLOCK = 128
KEY_SPAN = 1024
ROW_CHUNK = 128


lowest = -1e30
epsilon = 1e-06


def passed_along(shard, axis, by):
    peers = lax.axis_size(axis)
    pairs = [(i, i + by) for i in range(peers) if 0 <= i + by < peers]
    return lax.ppermute(shard, axis, pairs)


def exchanged(pieces_of, axis):
    peers = lax.axis_size(axis)
    place = lax.axis_index(axis)
    received = [pieces_of(place)]
    for shift in range(1, peers):
        outgoing = pieces_of((place + shift) % peers)
        pairs = [(i, (i + shift) % peers) for i in range(peers)]
        received.append(lax.ppermute(outgoing, axis, pairs))
    order = (place - jnp.arange(peers, dtype=jnp.int32)) % peers
    return jnp.take(jnp.stack(received), order, axis=0)


def gathered(shard, axis):
    peers = lax.axis_size(axis)
    place = lax.axis_index(axis)
    if peers & (peers - 1):
        return lax.all_gather(shard, axis, axis=0, tiled=False)
    bits = peers.bit_length() - 1
    held = shard[None]
    for level in reversed(range(bits)):
        bit = 1 << level
        incoming = lax.ppermute(held, axis, [(i, i ^ bit) for i in range(peers)])
        upper = (place & bit) != 0
        held = jnp.where(
            upper,
            jnp.concatenate([incoming, held], axis=0),
            jnp.concatenate([held, incoming], axis=0),
        )
    held = held.reshape((2,) * bits + shard.shape)
    return jnp.transpose(held, tuple(reversed(range(bits))) + tuple(range(bits, held.ndim)))


def logits_kernel(taps_ref, query_ref, keys_ref, out_ref, high_ref, low_ref, conv_ref):
    head = pl.program_id(0)
    group = pl.program_id(1)
    edge = 16

    @pl.when(group == 0)
    def _():
        lane = lax.broadcasted_iota(jnp.int32, (1, 2 * KEY_BLOCK), 1)
        for row_lag in range(QCONV):
            row = jnp.zeros(lane.shape, jnp.float32)
            for col_lag in range(KCONV):
                tap = taps_ref[(head * QCONV + row_lag) * KCONV + col_lag]
                row = jnp.where(lane == KEY_BLOCK - col_lag, tap, row)
            toeplitz = pltpu.roll(
                jnp.broadcast_to(row, (KEY_BLOCK, 2 * KEY_BLOCK)), 0, 1, stride=1, stride_axis=0
            )
            high = toeplitz.astype(jnp.bfloat16)
            low = (toeplitz - high.astype(jnp.float32)).astype(jnp.bfloat16)
            high_ref[row_lag * KEY_BLOCK : (row_lag + 1) * KEY_BLOCK] = high[:, KEY_BLOCK:]
            low_ref[row_lag * KEY_BLOCK : (row_lag + 1) * KEY_BLOCK] = low[:, KEY_BLOCK:]
            top = QCONV * KEY_BLOCK + row_lag * edge
            high_ref[top : top + edge] = high[:edge, :KEY_BLOCK]
            low_ref[top : top + edge] = low[:edge, :KEY_BLOCK]

    blocks = conv_ref.shape[0] // KEY_BLOCK
    body = QCONV * KEY_BLOCK
    for block in range(blocks):
        start = pl.multiple_of((group * blocks + block) * KEY_BLOCK, KEY_BLOCK)
        before_start = pl.multiple_of(jnp.maximum(start - KEY_BLOCK, 0), KEY_BLOCK)
        before = keys_ref[pl.ds(before_start, KEY_BLOCK), :]
        before = jnp.where(start > 0, before, jnp.zeros(before.shape, before.dtype))
        current = keys_ref[pl.ds(start, KEY_BLOCK), :]
        conv_body = jnp.dot(
            high_ref[:body], current, preferred_element_type=jnp.float32
        ) + jnp.dot(low_ref[:body], current, preferred_element_type=jnp.float32)
        conv_top = jnp.dot(
            high_ref[body:], before, preferred_element_type=jnp.float32
        ) + jnp.dot(low_ref[body:], before, preferred_element_type=jnp.float32)
        base = block * KEY_BLOCK
        for row_lag in range(QCONV):
            first = row_lag * KEY_BLOCK
            head_rows = conv_body[first : first + edge] + conv_top[
                row_lag * edge : (row_lag + 1) * edge
            ]
            rest_rows = conv_body[first + edge : first + KEY_BLOCK]
            cols = slice(row_lag * KEY_BLOCK, (row_lag + 1) * KEY_BLOCK)
            for part, rows in ((head_rows, slice(base, base + edge)),
                               (rest_rows, slice(base + edge, base + KEY_BLOCK))):
                part_high = part.astype(jnp.bfloat16)
                part_low = (part - part_high.astype(jnp.float32)).astype(jnp.bfloat16)
                low_cols = slice(body + cols.start, body + cols.stop)
                conv_ref[rows, cols] = part_high
                conv_ref[rows, low_cols] = part_low
    out_ref[0] = jnp.dot(conv_ref[...], query_ref[0], preferred_element_type=jnp.float32)


def conv_logits(shifted_t, score_kernel, key_pad):
    heads, contract, row_count = shifted_t.shape
    seq_len = key_pad.shape[0]
    head_dim = key_pad.shape[1] // heads
    span = min(seq_len, KEY_SPAN)
    taps = (score_kernel * head_dim ** (-0.5)).reshape(-1)
    return pl.pallas_call(
        logits_kernel,
        grid=(heads, seq_len // span),
        in_specs=[
            pl.BlockSpec(memory_space=pltpu.SMEM),
            pl.BlockSpec((1, 2 * contract, row_count), lambda h, g: (h, 0, 0)),
            pl.BlockSpec((key_pad.shape[0], head_dim), lambda h, g: (0, h)),
        ],
        out_specs=pl.BlockSpec((1, span, row_count), lambda h, g: (h, g, 0)),
        out_shape=jax.ShapeDtypeStruct((heads, seq_len, row_count), jnp.float32),
        scratch_shapes=[
            pltpu.VMEM((QCONV * (KEY_BLOCK + 16), KEY_BLOCK), jnp.bfloat16),
            pltpu.VMEM((QCONV * (KEY_BLOCK + 16), KEY_BLOCK), jnp.bfloat16),
            pltpu.VMEM((span, 2 * QCONV * head_dim), jnp.bfloat16),
        ],
    )(taps, jnp.concatenate([shifted_t, shifted_t], axis=1), key_pad)


def band_terms(query_rows, query_first, key_flat, score_kernel):
    row_lead = QCONV - 1
    heads = score_kernel.shape[0]
    ext_count = query_rows.shape[0]
    row_count = ext_count - row_lead
    near = lax.dynamic_slice_in_dim(key_flat, query_first + 4, ext_count + QCONV - 2, 0)
    query_heads = query_rows.reshape(ext_count, heads, -1).astype(jnp.float32)
    near_heads = near.reshape(near.shape[0], heads, -1).astype(jnp.float32)
    scale = query_heads.shape[2] ** (-0.5)
    diagonals = [
        jnp.sum(query_heads * near_heads[lag - 1 : lag - 1 + ext_count], axis=2) * scale
        for lag in range(1, QCONV)
    ]
    band = []
    for gap in range(QCONV - 1):
        acc = jnp.zeros((row_count, heads), jnp.float32)
        for row_lag in range(gap + 1, QCONV):
            for col_lag in range(row_lag - gap):
                lag = row_lag - col_lag - gap
                acc = acc - score_kernel[None, :, row_lag, col_lag] * diagonals[lag - 1][
                    row_lead - row_lag : row_lead - row_lag + row_count
                ]
        band.append(acc.T)
    return jnp.stack(band)


def attend_chunk(shifted, band, query_first, key_pad, score_kernel, value_heads, head_mixing):
    row_count, heads = shifted.shape[:2]
    seq_len = value_heads.shape[0]
    shifted_t = jnp.transpose(shifted, (1, 2, 3, 0)).reshape((heads, -1, row_count))
    convolved = conv_logits(shifted_t, score_kernel, key_pad)
    query_pos = query_first + lax.iota(jnp.int32, row_count)
    gap = query_pos[None, :] - lax.iota(jnp.int32, seq_len)[:, None]
    for lag in range(QCONV - 1):
        convolved = convolved + jnp.where(gap == lag, band[lag][:, None, :], 0.0)
    logits = jnp.where(gap >= 0, convolved, lowest)
    peak = jnp.max(logits, axis=1, keepdims=True)
    expd = jnp.exp(logits - peak)
    probabilities = expd / jnp.sum(expd, axis=1, keepdims=True)
    grouped = probabilities.reshape(heads // GROUP, GROUP, seq_len, row_count)
    weights = head_mixing.reshape(heads // GROUP, GROUP, GROUP)
    mixed_probs = jnp.zeros_like(grouped)
    for source in range(GROUP):
        mixed_probs = mixed_probs + weights[:, :, source, None, None] * grouped[:, source, None]
    mixed_probs = mixed_probs.reshape(heads, seq_len, row_count).astype(jnp.bfloat16)
    return jnp.einsum(
        "hki,khd->ihd", mixed_probs, value_heads, preferred_element_type=jnp.float32
    )


def normalize(weighted, gain_local):
    factor = lax.rsqrt(jnp.mean(weighted * weighted, axis=2, keepdims=True) + epsilon)
    return (
        (weighted * factor * gain_local[None]).astype(jnp.bfloat16).reshape(weighted.shape[0], -1)
    )


def shards(query_states, key_states, value_states, score_kernel, head_mixing, head_gain):
    groups = lax.axis_size("uly")
    stacked = jnp.stack([query_states, key_states, value_states])
    group_width = stacked.shape[2] // groups
    pieces = exchanged(
        lambda group: lax.dynamic_slice_in_dim(stacked, group * group_width, group_width, 2),
        "uly",
    )
    pieces = jnp.moveaxis(pieces, 0, 1)
    query_local, key_local, value_local = pieces.reshape(
        (pieces.shape[0], -1, pieces.shape[-1])
    )
    shard_rows = query_local.shape[0]
    width = query_local.shape[1]
    row_lead = QCONV - 1
    heads = score_kernel.shape[0]
    head_dim = width // heads
    ctx_place = lax.axis_index("ctx")
    query_first = ctx_place * shard_rows
    earlier = passed_along(query_local[shard_rows - row_lead :], "ctx", 1)
    query_ext = jnp.concatenate([earlier, query_local], axis=0)
    key_all = gathered(key_local, "ctx").reshape((-1, width))
    key_all, value_local = lax.optimization_barrier((key_all, value_local))
    value_all = gathered(value_local, "ctx").reshape((-1, width))
    seq_len = key_all.shape[0]
    key_pad = key_all
    edge = jnp.zeros((8, width), key_all.dtype)
    key_flat = jnp.concatenate([edge, key_all, edge], axis=0)
    band = band_terms(query_ext, query_first, key_flat, score_kernel)
    query_heads = query_ext.reshape(shard_rows + row_lead, heads, head_dim)
    shifted = jnp.stack(
        [query_heads[row_lead - lag : row_lead - lag + shard_rows] for lag in range(QCONV)], axis=2
    )
    value_heads = value_all.reshape(seq_len, heads, head_dim)
    chunk = min(ROW_CHUNK * KEY_BLOCK * 8 // seq_len, shard_rows)
    if chunk == shard_rows:
        weighted = attend_chunk(
            shifted, band, query_first, key_pad, score_kernel, value_heads, head_mixing
        )
    else:
        chunks = shard_rows // chunk

        def one_chunk(index):
            start = index * chunk
            return attend_chunk(
                lax.dynamic_slice_in_dim(shifted, start, chunk, 0),
                lax.dynamic_slice_in_dim(band, start, chunk, 2),
                query_first + start,
                key_pad,
                score_kernel,
                value_heads,
                head_mixing,
            )

        weighted = lax.map(one_chunk, jnp.arange(chunks, dtype=jnp.int32))
        weighted = weighted.reshape((shard_rows,) + weighted.shape[2:])
    gain_local = head_gain.reshape(heads, head_dim)
    attended = normalize(weighted, gain_local)
    block_rows = shard_rows // groups
    returned = exchanged(
        lambda group: lax.dynamic_slice_in_dim(attended, group * block_rows, block_rows, 0),
        "uly",
    )
    return jnp.moveaxis(returned, 0, 1).reshape((block_rows, -1))


def solution(mesh):
    placed = (
        P(("ctx", "uly"), None),
        P(("ctx", "uly"), None),
        P(("ctx", "uly"), None),
        P("uly", None, None),
        P("uly", None),
        P("uly"),
    )
    return jax.shard_map(
        shards, mesh=mesh, in_specs=placed, out_specs=P(("ctx", "uly"), None), check_vma=False
    )
```

```python
import jax
import jax.numpy as jnp
from jax import lax
from jax.experimental import pallas as pl
from jax.experimental.pallas import tpu as pltpu
from jax.sharding import PartitionSpec as P

GROUP = 4
QCONV = 6
KCONV = 11
KEY_BLOCK = 128
KEY_SPAN = 1024
ROW_CHUNK = 128


lowest = -1e30
epsilon = 1e-06


def passed_along(shard, axis, by):
    peers = lax.axis_size(axis)
    pairs = [(i, i + by) for i in range(peers) if 0 <= i + by < peers]
    return lax.ppermute(shard, axis, pairs)


def exchanged(pieces_of, axis):
    peers = lax.axis_size(axis)
    place = lax.axis_index(axis)
    received = [pieces_of(place)]
    for shift in range(1, peers):
        outgoing = pieces_of((place + shift) % peers)
        pairs = [(i, (i + shift) % peers) for i in range(peers)]
        received.append(lax.ppermute(outgoing, axis, pairs))
    order = (place - jnp.arange(peers, dtype=jnp.int32)) % peers
    return jnp.take(jnp.stack(received), order, axis=0)


def gathered(shard, axis):
    peers = lax.axis_size(axis)
    place = lax.axis_index(axis)
    if peers & (peers - 1):
        return lax.all_gather(shard, axis, axis=0, tiled=False)
    bits = peers.bit_length() - 1
    held = shard[None]
    for level in reversed(range(bits)):
        bit = 1 << level
        incoming = lax.ppermute(held, axis, [(i, i ^ bit) for i in range(peers)])
        upper = (place & bit) != 0
        held = jnp.where(
            upper,
            jnp.concatenate([incoming, held], axis=0),
            jnp.concatenate([held, incoming], axis=0),
        )
    held = held.reshape((2,) * bits + shard.shape)
    return jnp.transpose(held, tuple(reversed(range(bits))) + tuple(range(bits, held.ndim)))


def logits_kernel(taps_ref, query_ref, keys_ref, out_ref, high_ref, low_ref, conv_ref):
    head = pl.program_id(0)
    group = pl.program_id(1)
    edge = 16

    @pl.when(group == 0)
    def _():
        lane = lax.broadcasted_iota(jnp.int32, (1, 2 * KEY_BLOCK), 1)
        for row_lag in range(QCONV):
            row = jnp.zeros(lane.shape, jnp.float32)
            for col_lag in range(KCONV):
                tap = taps_ref[(head * QCONV + row_lag) * KCONV + col_lag]
                row = jnp.where(lane == KEY_BLOCK - col_lag, tap, row)
            toeplitz = pltpu.roll(
                jnp.broadcast_to(row, (KEY_BLOCK, 2 * KEY_BLOCK)), 0, 1, stride=1, stride_axis=0
            )
            high = toeplitz.astype(jnp.bfloat16)
            low = (toeplitz - high.astype(jnp.float32)).astype(jnp.bfloat16)
            high_ref[row_lag * KEY_BLOCK : (row_lag + 1) * KEY_BLOCK] = high[:, KEY_BLOCK:]
            low_ref[row_lag * KEY_BLOCK : (row_lag + 1) * KEY_BLOCK] = low[:, KEY_BLOCK:]
            top = QCONV * KEY_BLOCK + row_lag * edge
            high_ref[top : top + edge] = high[:edge, :KEY_BLOCK]
            low_ref[top : top + edge] = low[:edge, :KEY_BLOCK]

    blocks = conv_ref.shape[1] // KEY_BLOCK
    body = QCONV * KEY_BLOCK
    for block in range(blocks):
        start = pl.multiple_of((group * blocks + block) * KEY_BLOCK, KEY_BLOCK)
        before_start = pl.multiple_of(jnp.maximum(start - KEY_BLOCK, 0), KEY_BLOCK)
        before = keys_ref[pl.ds(before_start, KEY_BLOCK), :]
        before = jnp.where(start > 0, before, jnp.zeros(before.shape, before.dtype))
        current = keys_ref[pl.ds(start, KEY_BLOCK), :]
        conv_body = jnp.dot(
            high_ref[:body], current, preferred_element_type=jnp.float32
        ) + jnp.dot(low_ref[:body], current, preferred_element_type=jnp.float32)
        conv_top = jnp.dot(
            high_ref[body:], before, preferred_element_type=jnp.float32
        ) + jnp.dot(low_ref[body:], before, preferred_element_type=jnp.float32)
        base = block * KEY_BLOCK
        for row_lag in range(QCONV):
            first = row_lag * KEY_BLOCK
            head_rows = conv_body[first : first + edge] + conv_top[
                row_lag * edge : (row_lag + 1) * edge
            ]
            rest_rows = conv_body[first + edge : first + KEY_BLOCK]
            cols = slice(row_lag * KEY_BLOCK, (row_lag + 1) * KEY_BLOCK)
            for part, rows in ((head_rows, slice(base, base + edge)),
                               (rest_rows, slice(base + edge, base + KEY_BLOCK))):
                part_high = part.astype(jnp.bfloat16)
                part_low = (part - part_high.astype(jnp.float32)).astype(jnp.bfloat16)
                conv_ref[0, rows, cols] = part_high
                conv_ref[1, rows, cols] = part_low
    query = query_ref[0]
    out_ref[0] = jnp.dot(conv_ref[0], query, preferred_element_type=jnp.float32) + jnp.dot(
        conv_ref[1], query, preferred_element_type=jnp.float32
    )


def conv_logits(shifted_t, score_kernel, key_pad):
    heads, contract, row_count = shifted_t.shape
    seq_len = key_pad.shape[0]
    head_dim = key_pad.shape[1] // heads
    span = min(seq_len, KEY_SPAN)
    taps = (score_kernel * head_dim ** (-0.5)).reshape(-1)
    return pl.pallas_call(
        logits_kernel,
        grid=(heads, seq_len // span),
        in_specs=[
            pl.BlockSpec(memory_space=pltpu.SMEM),
            pl.BlockSpec((1, contract, row_count), lambda h, g: (h, 0, 0)),
            pl.BlockSpec((key_pad.shape[0], head_dim), lambda h, g: (0, h)),
        ],
        out_specs=pl.BlockSpec((1, span, row_count), lambda h, g: (h, g, 0)),
        out_shape=jax.ShapeDtypeStruct((heads, seq_len, row_count), jnp.float32),
        scratch_shapes=[
            pltpu.VMEM((QCONV * (KEY_BLOCK + 16), KEY_BLOCK), jnp.bfloat16),
            pltpu.VMEM((QCONV * (KEY_BLOCK + 16), KEY_BLOCK), jnp.bfloat16),
            pltpu.VMEM((2, span, QCONV * head_dim), jnp.bfloat16),
        ],
    )(taps, shifted_t, key_pad)


def band_terms(query_rows, query_first, key_flat, score_kernel):
    row_lead = QCONV - 1
    heads = score_kernel.shape[0]
    ext_count = query_rows.shape[0]
    row_count = ext_count - row_lead
    near = lax.dynamic_slice_in_dim(key_flat, query_first + 4, ext_count + QCONV - 2, 0)
    query_heads = query_rows.reshape(ext_count, heads, -1).astype(jnp.float32)
    near_heads = near.reshape(near.shape[0], heads, -1).astype(jnp.float32)
    scale = query_heads.shape[2] ** (-0.5)
    diagonals = [
        jnp.sum(query_heads * near_heads[lag - 1 : lag - 1 + ext_count], axis=2) * scale
        for lag in range(1, QCONV)
    ]
    band = []
    for gap in range(QCONV - 1):
        acc = jnp.zeros((row_count, heads), jnp.float32)
        for row_lag in range(gap + 1, QCONV):
            for col_lag in range(row_lag - gap):
                lag = row_lag - col_lag - gap
                acc = acc - score_kernel[None, :, row_lag, col_lag] * diagonals[lag - 1][
                    row_lead - row_lag : row_lead - row_lag + row_count
                ]
        band.append(acc.T)
    return jnp.stack(band)


def attend_chunk(shifted, band, query_first, key_pad, score_kernel, value_heads, head_mixing):
    row_count, heads = shifted.shape[:2]
    seq_len = value_heads.shape[0]
    shifted_t = jnp.transpose(shifted, (1, 2, 3, 0)).reshape((heads, -1, row_count))
    convolved = conv_logits(shifted_t, score_kernel, key_pad)
    query_pos = query_first + lax.iota(jnp.int32, row_count)
    gap = query_pos[None, :] - lax.iota(jnp.int32, seq_len)[:, None]
    for lag in range(QCONV - 1):
        convolved = convolved + jnp.where(gap == lag, band[lag][:, None, :], 0.0)
    logits = jnp.where(gap >= 0, convolved, lowest)
    peak = jnp.max(logits, axis=1, keepdims=True)
    expd = jnp.exp(logits - peak)
    probabilities = expd / jnp.sum(expd, axis=1, keepdims=True)
    grouped = probabilities.reshape(heads // GROUP, GROUP, seq_len, row_count)
    weights = head_mixing.reshape(heads // GROUP, GROUP, GROUP)
    mixed_probs = jnp.zeros_like(grouped)
    for source in range(GROUP):
        mixed_probs = mixed_probs + weights[:, :, source, None, None] * grouped[:, source, None]
    mixed_probs = mixed_probs.reshape(heads, seq_len, row_count).astype(jnp.bfloat16)
    return jnp.einsum(
        "hki,khd->ihd", mixed_probs, value_heads, preferred_element_type=jnp.float32
    )


def normalize(weighted, gain_local):
    factor = lax.rsqrt(jnp.mean(weighted * weighted, axis=2, keepdims=True) + epsilon)
    return (
        (weighted * factor * gain_local[None]).astype(jnp.bfloat16).reshape(weighted.shape[0], -1)
    )


def shards(query_states, key_states, value_states, score_kernel, head_mixing, head_gain):
    groups = lax.axis_size("uly")
    stacked = jnp.stack([query_states, key_states, value_states])
    group_width = stacked.shape[2] // groups
    pieces = exchanged(
        lambda group: lax.dynamic_slice_in_dim(stacked, group * group_width, group_width, 2),
        "uly",
    )
    pieces = jnp.moveaxis(pieces, 0, 1)
    query_local, key_local, value_local = pieces.reshape(
        (pieces.shape[0], -1, pieces.shape[-1])
    )
    shard_rows = query_local.shape[0]
    width = query_local.shape[1]
    row_lead = QCONV - 1
    heads = score_kernel.shape[0]
    head_dim = width // heads
    ctx_place = lax.axis_index("ctx")
    query_first = ctx_place * shard_rows
    earlier = passed_along(query_local[shard_rows - row_lead :], "ctx", 1)
    query_ext = jnp.concatenate([earlier, query_local], axis=0)
    value_all = lax.all_gather(value_local, "ctx", axis=0, tiled=True)
    key_all = gathered(key_local, "ctx").reshape((-1, width))
    seq_len = key_all.shape[0]
    key_pad = key_all
    edge = jnp.zeros((8, width), key_all.dtype)
    key_flat = jnp.concatenate([edge, key_all, edge], axis=0)
    band = band_terms(query_ext, query_first, key_flat, score_kernel)
    query_heads = query_ext.reshape(shard_rows + row_lead, heads, head_dim)
    shifted = jnp.stack(
        [query_heads[row_lead - lag : row_lead - lag + shard_rows] for lag in range(QCONV)], axis=2
    )
    value_heads = value_all.reshape(seq_len, heads, head_dim)
    chunk = min(ROW_CHUNK * KEY_BLOCK * 8 // seq_len, shard_rows)
    if chunk == shard_rows:
        weighted = attend_chunk(
            shifted, band, query_first, key_pad, score_kernel, value_heads, head_mixing
        )
    else:
        chunks = shard_rows // chunk

        def one_chunk(index):
            start = index * chunk
            return attend_chunk(
                lax.dynamic_slice_in_dim(shifted, start, chunk, 0),
                lax.dynamic_slice_in_dim(band, start, chunk, 2),
                query_first + start,
                key_pad,
                score_kernel,
                value_heads,
                head_mixing,
            )

        weighted = lax.map(one_chunk, jnp.arange(chunks, dtype=jnp.int32))
        weighted = weighted.reshape((shard_rows,) + weighted.shape[2:])
    gain_local = head_gain.reshape(heads, head_dim)
    attended = normalize(weighted, gain_local)
    block_rows = shard_rows // groups
    returned = exchanged(
        lambda group: lax.dynamic_slice_in_dim(attended, group * block_rows, block_rows, 0),
        "uly",
    )
    return jnp.moveaxis(returned, 0, 1).reshape((block_rows, -1))


def solution(mesh):
    placed = (
        P(("ctx", "uly"), None),
        P(("ctx", "uly"), None),
        P(("ctx", "uly"), None),
        P("uly", None, None),
        P("uly", None),
        P("uly"),
    )
    return jax.shard_map(
        shards, mesh=mesh, in_specs=placed, out_specs=P(("ctx", "uly"), None), check_vma=False
    )
```

```python
import functools

import jax
import jax.numpy as jnp
from jax import lax
from jax.experimental import pallas as pl
from jax.experimental.pallas import tpu as pltpu
from jax.sharding import PartitionSpec as P

GROUP = 4
QCONV = 6
KCONV = 11
KEY_BLOCK = 128
KEY_SPAN = 1024
ROW_CHUNK = 128


lowest = -1e30
epsilon = 1e-06


def passed_along(shard, axis, by):
    peers = lax.axis_size(axis)
    pairs = [(i, i + by) for i in range(peers) if 0 <= i + by < peers]
    return lax.ppermute(shard, axis, pairs)


def exchanged(pieces_of, axis):
    peers = lax.axis_size(axis)
    place = lax.axis_index(axis)
    received = [pieces_of(place)]
    for shift in range(1, peers):
        outgoing = pieces_of((place + shift) % peers)
        pairs = [(i, (i + shift) % peers) for i in range(peers)]
        received.append(lax.ppermute(outgoing, axis, pairs))
    order = (place - jnp.arange(peers, dtype=jnp.int32)) % peers
    return jnp.take(jnp.stack(received), order, axis=0)


def gathered(shard, axis):
    peers = lax.axis_size(axis)
    place = lax.axis_index(axis)
    if peers & (peers - 1):
        return lax.all_gather(shard, axis, axis=0, tiled=False)
    bits = peers.bit_length() - 1
    held = shard[None]
    for level in reversed(range(bits)):
        bit = 1 << level
        incoming = lax.ppermute(held, axis, [(i, i ^ bit) for i in range(peers)])
        upper = (place & bit) != 0
        held = jnp.where(
            upper,
            jnp.concatenate([incoming, held], axis=0),
            jnp.concatenate([held, incoming], axis=0),
        )
    held = held.reshape((2,) * bits + shard.shape)
    return jnp.transpose(held, tuple(reversed(range(bits))) + tuple(range(bits, held.ndim)))


def logits_kernel(first_head, taps_ref, query_ref, keys_ref, out_ref, high_ref, low_ref, conv_ref):
    head = pl.program_id(0) + first_head
    group = pl.program_id(1)
    edge = 16

    @pl.when(group == 0)
    def _():
        lane = lax.broadcasted_iota(jnp.int32, (1, 2 * KEY_BLOCK), 1)
        for row_lag in range(QCONV):
            row = jnp.zeros(lane.shape, jnp.float32)
            for col_lag in range(KCONV):
                tap = taps_ref[(head * QCONV + row_lag) * KCONV + col_lag]
                row = jnp.where(lane == KEY_BLOCK - col_lag, tap, row)
            toeplitz = pltpu.roll(
                jnp.broadcast_to(row, (KEY_BLOCK, 2 * KEY_BLOCK)), 0, 1, stride=1, stride_axis=0
            )
            high = toeplitz.astype(jnp.bfloat16)
            low = (toeplitz - high.astype(jnp.float32)).astype(jnp.bfloat16)
            high_ref[row_lag * KEY_BLOCK : (row_lag + 1) * KEY_BLOCK] = high[:, KEY_BLOCK:]
            low_ref[row_lag * KEY_BLOCK : (row_lag + 1) * KEY_BLOCK] = low[:, KEY_BLOCK:]
            top = QCONV * KEY_BLOCK + row_lag * edge
            high_ref[top : top + edge] = high[:edge, :KEY_BLOCK]
            low_ref[top : top + edge] = low[:edge, :KEY_BLOCK]

    blocks = conv_ref.shape[1] // KEY_BLOCK
    body = QCONV * KEY_BLOCK
    for block in range(blocks):
        start = pl.multiple_of((group * blocks + block) * KEY_BLOCK, KEY_BLOCK)
        before_start = pl.multiple_of(jnp.maximum(start - KEY_BLOCK, 0), KEY_BLOCK)
        before = keys_ref[pl.ds(before_start, KEY_BLOCK), :]
        before = jnp.where(start > 0, before, jnp.zeros(before.shape, before.dtype))
        current = keys_ref[pl.ds(start, KEY_BLOCK), :]
        conv_body = jnp.dot(
            high_ref[:body], current, preferred_element_type=jnp.float32
        ) + jnp.dot(low_ref[:body], current, preferred_element_type=jnp.float32)
        conv_top = jnp.dot(
            high_ref[body:], before, preferred_element_type=jnp.float32
        ) + jnp.dot(low_ref[body:], before, preferred_element_type=jnp.float32)
        base = block * KEY_BLOCK
        for row_lag in range(QCONV):
            first = row_lag * KEY_BLOCK
            head_rows = conv_body[first : first + edge] + conv_top[
                row_lag * edge : (row_lag + 1) * edge
            ]
            rest_rows = conv_body[first + edge : first + KEY_BLOCK]
            cols = slice(row_lag * KEY_BLOCK, (row_lag + 1) * KEY_BLOCK)
            for part, rows in ((head_rows, slice(base, base + edge)),
                               (rest_rows, slice(base + edge, base + KEY_BLOCK))):
                part_high = part.astype(jnp.bfloat16)
                part_low = (part - part_high.astype(jnp.float32)).astype(jnp.bfloat16)
                conv_ref[0, rows, cols] = part_high
                conv_ref[1, rows, cols] = part_low
    query = query_ref[0]
    out_ref[0] = jnp.dot(conv_ref[0], query, preferred_element_type=jnp.float32) + jnp.dot(
        conv_ref[1], query, preferred_element_type=jnp.float32
    )


def conv_logits(shifted_t, score_kernel, key_pad, first_head):
    heads, contract, row_count = shifted_t.shape
    seq_len = key_pad.shape[0]
    head_dim = key_pad.shape[1] // score_kernel.shape[0]
    span = min(seq_len, KEY_SPAN)
    taps = (score_kernel * head_dim ** (-0.5)).reshape(-1)
    return pl.pallas_call(
        functools.partial(logits_kernel, first_head),
        grid=(heads, seq_len // span),
        in_specs=[
            pl.BlockSpec(memory_space=pltpu.SMEM),
            pl.BlockSpec((1, contract, row_count), lambda h, g: (h, 0, 0)),
            pl.BlockSpec((key_pad.shape[0], head_dim), lambda h, g: (0, h + first_head)),
        ],
        out_specs=pl.BlockSpec((1, span, row_count), lambda h, g: (h, g, 0)),
        out_shape=jax.ShapeDtypeStruct((heads, seq_len, row_count), jnp.float32),
        scratch_shapes=[
            pltpu.VMEM((QCONV * (KEY_BLOCK + 16), KEY_BLOCK), jnp.bfloat16),
            pltpu.VMEM((QCONV * (KEY_BLOCK + 16), KEY_BLOCK), jnp.bfloat16),
            pltpu.VMEM((2, span, QCONV * head_dim), jnp.bfloat16),
        ],
    )(taps, shifted_t, key_pad)


def band_terms(query_rows, query_first, key_flat, score_kernel):
    row_lead = QCONV - 1
    heads = score_kernel.shape[0]
    ext_count = query_rows.shape[0]
    row_count = ext_count - row_lead
    near = lax.dynamic_slice_in_dim(key_flat, query_first + 4, ext_count + QCONV - 2, 0)
    query_heads = query_rows.reshape(ext_count, heads, -1).astype(jnp.float32)
    near_heads = near.reshape(near.shape[0], heads, -1).astype(jnp.float32)
    scale = query_heads.shape[2] ** (-0.5)
    diagonals = [
        jnp.sum(query_heads * near_heads[lag - 1 : lag - 1 + ext_count], axis=2) * scale
        for lag in range(1, QCONV)
    ]
    band = []
    for gap in range(QCONV - 1):
        acc = jnp.zeros((row_count, heads), jnp.float32)
        for row_lag in range(gap + 1, QCONV):
            for col_lag in range(row_lag - gap):
                lag = row_lag - col_lag - gap
                acc = acc - score_kernel[None, :, row_lag, col_lag] * diagonals[lag - 1][
                    row_lead - row_lag : row_lead - row_lag + row_count
                ]
        band.append(acc.T)
    return jnp.stack(band)


def attend_chunk(shifted, band, query_first, key_pad, score_kernel, value_heads, head_mixing):
    row_count, heads = shifted.shape[:2]
    seq_len = value_heads.shape[0]
    shifted_t = jnp.transpose(shifted, (1, 2, 3, 0)).reshape((heads, -1, row_count))
    half = heads // 2
    convolved = jnp.concatenate(
        [
            conv_logits(shifted_t[:half], score_kernel, key_pad, 0),
            conv_logits(shifted_t[half:], score_kernel, key_pad, half),
        ],
        axis=0,
    )
    query_pos = query_first + lax.iota(jnp.int32, row_count)
    gap = query_pos[None, :] - lax.iota(jnp.int32, seq_len)[:, None]
    for lag in range(QCONV - 1):
        convolved = convolved + jnp.where(gap == lag, band[lag][:, None, :], 0.0)
    logits = jnp.where(gap >= 0, convolved, lowest)
    peak = jnp.max(logits, axis=1, keepdims=True)
    expd = jnp.exp(logits - peak)
    probabilities = expd / jnp.sum(expd, axis=1, keepdims=True)
    grouped = probabilities.reshape(heads // GROUP, GROUP, seq_len, row_count)
    weights = head_mixing.reshape(heads // GROUP, GROUP, GROUP)
    mixed_probs = jnp.zeros_like(grouped)
    for source in range(GROUP):
        mixed_probs = mixed_probs + weights[:, :, source, None, None] * grouped[:, source, None]
    mixed_probs = mixed_probs.reshape(heads, seq_len, row_count).astype(jnp.bfloat16)
    return jnp.einsum(
        "hki,khd->ihd", mixed_probs, value_heads, preferred_element_type=jnp.float32
    )


def normalize(weighted, gain_local):
    factor = lax.rsqrt(jnp.mean(weighted * weighted, axis=2, keepdims=True) + epsilon)
    return (
        (weighted * factor * gain_local[None]).astype(jnp.bfloat16).reshape(weighted.shape[0], -1)
    )


def shards(query_states, key_states, value_states, score_kernel, head_mixing, head_gain):
    groups = lax.axis_size("uly")
    stacked = jnp.stack([query_states, key_states, value_states])
    group_width = stacked.shape[2] // groups
    pieces = exchanged(
        lambda group: lax.dynamic_slice_in_dim(stacked, group * group_width, group_width, 2),
        "uly",
    )
    pieces = jnp.moveaxis(pieces, 0, 1)
    query_local, key_local, value_local = pieces.reshape(
        (pieces.shape[0], -1, pieces.shape[-1])
    )
    shard_rows = query_local.shape[0]
    width = query_local.shape[1]
    row_lead = QCONV - 1
    heads = score_kernel.shape[0]
    head_dim = width // heads
    ctx_place = lax.axis_index("ctx")
    query_first = ctx_place * shard_rows
    earlier = passed_along(query_local[shard_rows - row_lead :], "ctx", 1)
    query_ext = jnp.concatenate([earlier, query_local], axis=0)
    key_all = gathered(key_local, "ctx").reshape((-1, width))
    key_all, value_local = lax.optimization_barrier((key_all, value_local))
    value_all = gathered(value_local, "ctx").reshape((-1, width))
    seq_len = key_all.shape[0]
    key_pad = key_all
    edge = jnp.zeros((8, width), key_all.dtype)
    key_flat = jnp.concatenate([edge, key_all, edge], axis=0)
    band = band_terms(query_ext, query_first, key_flat, score_kernel)
    query_heads = query_ext.reshape(shard_rows + row_lead, heads, head_dim)
    shifted = jnp.stack(
        [query_heads[row_lead - lag : row_lead - lag + shard_rows] for lag in range(QCONV)], axis=2
    )
    value_heads = value_all.reshape(seq_len, heads, head_dim)
    chunk = min(ROW_CHUNK * KEY_BLOCK * 8 // seq_len, shard_rows)
    if chunk == shard_rows:
        weighted = attend_chunk(
            shifted, band, query_first, key_pad, score_kernel, value_heads, head_mixing
        )
    else:
        chunks = shard_rows // chunk

        def one_chunk(index):
            start = index * chunk
            return attend_chunk(
                lax.dynamic_slice_in_dim(shifted, start, chunk, 0),
                lax.dynamic_slice_in_dim(band, start, chunk, 2),
                query_first + start,
                key_pad,
                score_kernel,
                value_heads,
                head_mixing,
            )

        weighted = lax.map(one_chunk, jnp.arange(chunks, dtype=jnp.int32))
        weighted = weighted.reshape((shard_rows,) + weighted.shape[2:])
    gain_local = head_gain.reshape(heads, head_dim)
    attended = normalize(weighted, gain_local)
    block_rows = shard_rows // groups
    returned = exchanged(
        lambda group: lax.dynamic_slice_in_dim(attended, group * block_rows, block_rows, 0),
        "uly",
    )
    return jnp.moveaxis(returned, 0, 1).reshape((block_rows, -1))


def solution(mesh):
    placed = (
        P(("ctx", "uly"), None),
        P(("ctx", "uly"), None),
        P(("ctx", "uly"), None),
        P("uly", None, None),
        P("uly", None),
        P("uly"),
    )
    return jax.shard_map(
        shards, mesh=mesh, in_specs=placed, out_specs=P(("ctx", "uly"), None), check_vma=False
    )
```

```python
import jax
import jax.numpy as jnp
from jax import lax
from jax.experimental import pallas as pl
from jax.experimental.pallas import tpu as pltpu
from jax.sharding import PartitionSpec as P

GROUP = 4
QCONV = 6
KCONV = 11
KEY_BLOCK = 128
KEY_SPAN = 1024
ROW_CHUNK = 128


lowest = -1e30
epsilon = 1e-06


def passed_along(shard, axis, by):
    peers = lax.axis_size(axis)
    pairs = [(i, i + by) for i in range(peers) if 0 <= i + by < peers]
    return lax.ppermute(shard, axis, pairs)


def exchanged(pieces_of, axis):
    peers = lax.axis_size(axis)
    place = lax.axis_index(axis)
    received = [pieces_of(place)]
    for shift in range(1, peers):
        outgoing = pieces_of((place + shift) % peers)
        pairs = [(i, (i + shift) % peers) for i in range(peers)]
        received.append(lax.ppermute(outgoing, axis, pairs))
    order = (place - jnp.arange(peers, dtype=jnp.int32)) % peers
    return jnp.take(jnp.stack(received), order, axis=0)


def gathered(shard, axis):
    peers = lax.axis_size(axis)
    place = lax.axis_index(axis)
    if peers & (peers - 1):
        return lax.all_gather(shard, axis, axis=0, tiled=False)
    bits = peers.bit_length() - 1
    held = shard[None]
    for level in reversed(range(bits)):
        bit = 1 << level
        incoming = lax.ppermute(held, axis, [(i, i ^ bit) for i in range(peers)])
        upper = (place & bit) != 0
        held = jnp.where(
            upper,
            jnp.concatenate([incoming, held], axis=0),
            jnp.concatenate([held, incoming], axis=0),
        )
    held = held.reshape((2,) * bits + shard.shape)
    return jnp.transpose(held, tuple(reversed(range(bits))) + tuple(range(bits, held.ndim)))


def doubling_step(held, axis, bit):
    peers = lax.axis_size(axis)
    place = lax.axis_index(axis)
    incoming = lax.ppermute(held, axis, [(i, i ^ bit) for i in range(peers)])
    return jnp.where(
        (place & bit) != 0,
        jnp.concatenate([incoming, held], axis=0),
        jnp.concatenate([held, incoming], axis=0),
    )


def doubling_done(held, peers, shard_shape):
    bits = peers.bit_length() - 1
    held = held.reshape((2,) * bits + shard_shape)
    return jnp.transpose(held, tuple(reversed(range(bits))) + tuple(range(bits, held.ndim)))


def gathered_pair(first, second, axis):
    peers = lax.axis_size(axis)
    if peers & (peers - 1) or peers < 4:
        return gathered(first, axis), gathered(second, axis)
    levels = list(reversed(range(peers.bit_length() - 1)))
    held = first[None]
    for level in levels[:-1]:
        held = doubling_step(held, axis, 1 << level)
    held, later = lax.optimization_barrier((held, second[None]))
    held = doubling_step(held, axis, 1 << levels[-1])
    for level in levels:
        later = doubling_step(later, axis, 1 << level)
    return doubling_done(held, peers, first.shape), doubling_done(later, peers, second.shape)


def logits_kernel(taps_ref, query_ref, keys_ref, out_ref, high_ref, low_ref, conv_ref):
    head = pl.program_id(0)
    group = pl.program_id(1)
    edge = 16

    @pl.when(group == 0)
    def _():
        lane = lax.broadcasted_iota(jnp.int32, (1, 2 * KEY_BLOCK), 1)
        for row_lag in range(QCONV):
            row = jnp.zeros(lane.shape, jnp.float32)
            for col_lag in range(KCONV):
                tap = taps_ref[(head * QCONV + row_lag) * KCONV + col_lag]
                row = jnp.where(lane == KEY_BLOCK - col_lag, tap, row)
            toeplitz = pltpu.roll(
                jnp.broadcast_to(row, (KEY_BLOCK, 2 * KEY_BLOCK)), 0, 1, stride=1, stride_axis=0
            )
            high = toeplitz.astype(jnp.bfloat16)
            low = (toeplitz - high.astype(jnp.float32)).astype(jnp.bfloat16)
            high_ref[row_lag * KEY_BLOCK : (row_lag + 1) * KEY_BLOCK] = high[:, KEY_BLOCK:]
            low_ref[row_lag * KEY_BLOCK : (row_lag + 1) * KEY_BLOCK] = low[:, KEY_BLOCK:]
            top = QCONV * KEY_BLOCK + row_lag * edge
            high_ref[top : top + edge] = high[:edge, :KEY_BLOCK]
            low_ref[top : top + edge] = low[:edge, :KEY_BLOCK]

    blocks = conv_ref.shape[1] // KEY_BLOCK
    body = QCONV * KEY_BLOCK
    for block in range(blocks):
        start = pl.multiple_of((group * blocks + block) * KEY_BLOCK, KEY_BLOCK)
        before_start = pl.multiple_of(jnp.maximum(start - KEY_BLOCK, 0), KEY_BLOCK)
        before = keys_ref[pl.ds(before_start, KEY_BLOCK), :]
        before = jnp.where(start > 0, before, jnp.zeros(before.shape, before.dtype))
        current = keys_ref[pl.ds(start, KEY_BLOCK), :]
        conv_body = jnp.dot(
            high_ref[:body], current, preferred_element_type=jnp.float32
        ) + jnp.dot(low_ref[:body], current, preferred_element_type=jnp.float32)
        conv_top = jnp.dot(
            high_ref[body:], before, preferred_element_type=jnp.float32
        ) + jnp.dot(low_ref[body:], before, preferred_element_type=jnp.float32)
        base = block * KEY_BLOCK
        for row_lag in range(QCONV):
            first = row_lag * KEY_BLOCK
            head_rows = conv_body[first : first + edge] + conv_top[
                row_lag * edge : (row_lag + 1) * edge
            ]
            rest_rows = conv_body[first + edge : first + KEY_BLOCK]
            cols = slice(row_lag * KEY_BLOCK, (row_lag + 1) * KEY_BLOCK)
            for part, rows in ((head_rows, slice(base, base + edge)),
                               (rest_rows, slice(base + edge, base + KEY_BLOCK))):
                part_high = part.astype(jnp.bfloat16)
                part_low = (part - part_high.astype(jnp.float32)).astype(jnp.bfloat16)
                conv_ref[0, rows, cols] = part_high
                conv_ref[1, rows, cols] = part_low
    query = query_ref[0]
    out_ref[0] = jnp.dot(conv_ref[0], query, preferred_element_type=jnp.float32) + jnp.dot(
        conv_ref[1], query, preferred_element_type=jnp.float32
    )


def conv_logits(shifted_t, score_kernel, key_pad):
    heads, contract, row_count = shifted_t.shape
    seq_len = key_pad.shape[0]
    head_dim = key_pad.shape[1] // heads
    span = min(seq_len, KEY_SPAN)
    taps = (score_kernel * head_dim ** (-0.5)).reshape(-1)
    return pl.pallas_call(
        logits_kernel,
        grid=(heads, seq_len // span),
        in_specs=[
            pl.BlockSpec(memory_space=pltpu.SMEM),
            pl.BlockSpec((1, contract, row_count), lambda h, g: (h, 0, 0)),
            pl.BlockSpec((key_pad.shape[0], head_dim), lambda h, g: (0, h)),
        ],
        out_specs=pl.BlockSpec((1, span, row_count), lambda h, g: (h, g, 0)),
        out_shape=jax.ShapeDtypeStruct((heads, seq_len, row_count), jnp.float32),
        scratch_shapes=[
            pltpu.VMEM((QCONV * (KEY_BLOCK + 16), KEY_BLOCK), jnp.bfloat16),
            pltpu.VMEM((QCONV * (KEY_BLOCK + 16), KEY_BLOCK), jnp.bfloat16),
            pltpu.VMEM((2, span, QCONV * head_dim), jnp.bfloat16),
        ],
    )(taps, shifted_t, key_pad)


def band_terms(query_rows, query_first, key_flat, score_kernel):
    row_lead = QCONV - 1
    heads = score_kernel.shape[0]
    ext_count = query_rows.shape[0]
    row_count = ext_count - row_lead
    near = lax.dynamic_slice_in_dim(key_flat, query_first + 4, ext_count + QCONV - 2, 0)
    query_heads = query_rows.reshape(ext_count, heads, -1).astype(jnp.float32)
    near_heads = near.reshape(near.shape[0], heads, -1).astype(jnp.float32)
    scale = query_heads.shape[2] ** (-0.5)
    diagonals = [
        jnp.sum(query_heads * near_heads[lag - 1 : lag - 1 + ext_count], axis=2) * scale
        for lag in range(1, QCONV)
    ]
    band = []
    for gap in range(QCONV - 1):
        acc = jnp.zeros((row_count, heads), jnp.float32)
        for row_lag in range(gap + 1, QCONV):
            for col_lag in range(row_lag - gap):
                lag = row_lag - col_lag - gap
                acc = acc - score_kernel[None, :, row_lag, col_lag] * diagonals[lag - 1][
                    row_lead - row_lag : row_lead - row_lag + row_count
                ]
        band.append(acc.T)
    return jnp.stack(band)


def attend_chunk(shifted, band, query_first, key_pad, score_kernel, value_heads, head_mixing):
    row_count, heads = shifted.shape[:2]
    seq_len = value_heads.shape[0]
    shifted_t = jnp.transpose(shifted, (1, 2, 3, 0)).reshape((heads, -1, row_count))
    convolved = conv_logits(shifted_t, score_kernel, key_pad)
    query_pos = query_first + lax.iota(jnp.int32, row_count)
    gap = query_pos[None, :] - lax.iota(jnp.int32, seq_len)[:, None]
    for lag in range(QCONV - 1):
        convolved = convolved + jnp.where(gap == lag, band[lag][:, None, :], 0.0)
    logits = jnp.where(gap >= 0, convolved, lowest)
    peak = jnp.max(logits, axis=1, keepdims=True)
    expd = jnp.exp(logits - peak)
    probabilities = expd / jnp.sum(expd, axis=1, keepdims=True)
    grouped = probabilities.reshape(heads // GROUP, GROUP, seq_len, row_count)
    weights = head_mixing.reshape(heads // GROUP, GROUP, GROUP)
    mixed_probs = jnp.zeros_like(grouped)
    for source in range(GROUP):
        mixed_probs = mixed_probs + weights[:, :, source, None, None] * grouped[:, source, None]
    mixed_probs = mixed_probs.reshape(heads, seq_len, row_count).astype(jnp.bfloat16)
    return jnp.einsum(
        "hki,khd->ihd", mixed_probs, value_heads, preferred_element_type=jnp.float32
    )


def normalize(weighted, gain_local):
    factor = lax.rsqrt(jnp.mean(weighted * weighted, axis=2, keepdims=True) + epsilon)
    return (
        (weighted * factor * gain_local[None]).astype(jnp.bfloat16).reshape(weighted.shape[0], -1)
    )


def shards(query_states, key_states, value_states, score_kernel, head_mixing, head_gain):
    groups = lax.axis_size("uly")
    stacked = jnp.stack([query_states, key_states, value_states])
    group_width = stacked.shape[2] // groups
    pieces = exchanged(
        lambda group: lax.dynamic_slice_in_dim(stacked, group * group_width, group_width, 2),
        "uly",
    )
    pieces = jnp.moveaxis(pieces, 0, 1)
    query_local, key_local, value_local = pieces.reshape(
        (pieces.shape[0], -1, pieces.shape[-1])
    )
    shard_rows = query_local.shape[0]
    width = query_local.shape[1]
    row_lead = QCONV - 1
    heads = score_kernel.shape[0]
    head_dim = width // heads
    ctx_place = lax.axis_index("ctx")
    query_first = ctx_place * shard_rows
    earlier = passed_along(query_local[shard_rows - row_lead :], "ctx", 1)
    query_ext = jnp.concatenate([earlier, query_local], axis=0)
    key_all, value_all = gathered_pair(key_local, value_local, "ctx")
    key_all = key_all.reshape((-1, width))
    value_all = value_all.reshape((-1, width))
    seq_len = key_all.shape[0]
    key_pad = key_all
    edge = jnp.zeros((8, width), key_all.dtype)
    key_flat = jnp.concatenate([edge, key_all, edge], axis=0)
    band = band_terms(query_ext, query_first, key_flat, score_kernel)
    query_heads = query_ext.reshape(shard_rows + row_lead, heads, head_dim)
    shifted = jnp.stack(
        [query_heads[row_lead - lag : row_lead - lag + shard_rows] for lag in range(QCONV)], axis=2
    )
    value_heads = value_all.reshape(seq_len, heads, head_dim)
    chunk = min(ROW_CHUNK * KEY_BLOCK * 8 // seq_len, shard_rows)
    if chunk == shard_rows:
        weighted = attend_chunk(
            shifted, band, query_first, key_pad, score_kernel, value_heads, head_mixing
        )
    else:
        chunks = shard_rows // chunk

        def one_chunk(index):
            start = index * chunk
            return attend_chunk(
                lax.dynamic_slice_in_dim(shifted, start, chunk, 0),
                lax.dynamic_slice_in_dim(band, start, chunk, 2),
                query_first + start,
                key_pad,
                score_kernel,
                value_heads,
                head_mixing,
            )

        weighted = lax.map(one_chunk, jnp.arange(chunks, dtype=jnp.int32))
        weighted = weighted.reshape((shard_rows,) + weighted.shape[2:])
    gain_local = head_gain.reshape(heads, head_dim)
    attended = normalize(weighted, gain_local)
    block_rows = shard_rows // groups
    returned = exchanged(
        lambda group: lax.dynamic_slice_in_dim(attended, group * block_rows, block_rows, 0),
        "uly",
    )
    return jnp.moveaxis(returned, 0, 1).reshape((block_rows, -1))


def solution(mesh):
    placed = (
        P(("ctx", "uly"), None),
        P(("ctx", "uly"), None),
        P(("ctx", "uly"), None),
        P("uly", None, None),
        P("uly", None),
        P("uly"),
    )
    return jax.shard_map(
        shards, mesh=mesh, in_specs=placed, out_specs=P(("ctx", "uly"), None), check_vma=False
    )
```

```python
import jax
import jax.numpy as jnp
from jax import lax
from jax.experimental import pallas as pl
from jax.experimental.pallas import tpu as pltpu
from jax.sharding import PartitionSpec as P

GROUP = 4
QCONV = 6
KCONV = 11
KEY_BLOCK = 128
KEY_SPAN = 1024
ROW_CHUNK = 128


lowest = -1e30
epsilon = 1e-06


def passed_along(shard, axis, by):
    peers = lax.axis_size(axis)
    pairs = [(i, i + by) for i in range(peers) if 0 <= i + by < peers]
    return lax.ppermute(shard, axis, pairs)


def exchanged(pieces_of, axis):
    peers = lax.axis_size(axis)
    place = lax.axis_index(axis)
    received = [pieces_of(place)]
    for shift in range(1, peers):
        outgoing = pieces_of((place + shift) % peers)
        pairs = [(i, (i + shift) % peers) for i in range(peers)]
        received.append(lax.ppermute(outgoing, axis, pairs))
    order = (place - jnp.arange(peers, dtype=jnp.int32)) % peers
    return jnp.take(jnp.stack(received), order, axis=0)


def gathered(shard, axis):
    peers = lax.axis_size(axis)
    place = lax.axis_index(axis)
    if peers & (peers - 1):
        return lax.all_gather(shard, axis, axis=0, tiled=False)
    bits = peers.bit_length() - 1
    held = shard[None]
    for level in reversed(range(bits)):
        bit = 1 << level
        incoming = lax.ppermute(held, axis, [(i, i ^ bit) for i in range(peers)])
        upper = (place & bit) != 0
        held = jnp.where(
            upper,
            jnp.concatenate([incoming, held], axis=0),
            jnp.concatenate([held, incoming], axis=0),
        )
    held = held.reshape((2,) * bits + shard.shape)
    return jnp.transpose(held, tuple(reversed(range(bits))) + tuple(range(bits, held.ndim)))


def logits_kernel(taps_ref, query_ref, keys_ref, out_ref, high_ref, low_ref, conv_ref):
    head = pl.program_id(0)
    group = pl.program_id(1)
    edge = 16

    @pl.when(group == 0)
    def _():
        lane = lax.broadcasted_iota(jnp.int32, (1, 2 * KEY_BLOCK), 1)
        for row_lag in range(QCONV):
            row = jnp.zeros(lane.shape, jnp.float32)
            for col_lag in range(KCONV):
                tap = taps_ref[(head * QCONV + row_lag) * KCONV + col_lag]
                row = jnp.where(lane == KEY_BLOCK - col_lag, tap, row)
            toeplitz = pltpu.roll(
                jnp.broadcast_to(row, (KEY_BLOCK, 2 * KEY_BLOCK)), 0, 1, stride=1, stride_axis=0
            )
            high = toeplitz.astype(jnp.bfloat16)
            low = (toeplitz - high.astype(jnp.float32)).astype(jnp.bfloat16)
            high_ref[row_lag * KEY_BLOCK : (row_lag + 1) * KEY_BLOCK] = high[:, KEY_BLOCK:]
            low_ref[row_lag * KEY_BLOCK : (row_lag + 1) * KEY_BLOCK] = low[:, KEY_BLOCK:]
            top = QCONV * KEY_BLOCK + row_lag * edge
            high_ref[top : top + edge] = high[:edge, :KEY_BLOCK]
            low_ref[top : top + edge] = low[:edge, :KEY_BLOCK]

    blocks = conv_ref.shape[1] // KEY_BLOCK
    body = QCONV * KEY_BLOCK
    for block in range(blocks):
        start = pl.multiple_of((group * blocks + block) * KEY_BLOCK, KEY_BLOCK)
        before_start = pl.multiple_of(jnp.maximum(start - KEY_BLOCK, 0), KEY_BLOCK)
        before = keys_ref[pl.ds(before_start, KEY_BLOCK), :]
        before = jnp.where(start > 0, before, jnp.zeros(before.shape, before.dtype))
        current = keys_ref[pl.ds(start, KEY_BLOCK), :]
        conv_body = jnp.dot(
            high_ref[:body], current, preferred_element_type=jnp.float32
        ) + jnp.dot(low_ref[:body], current, preferred_element_type=jnp.float32)
        conv_top = jnp.dot(
            high_ref[body:], before, preferred_element_type=jnp.float32
        ) + jnp.dot(low_ref[body:], before, preferred_element_type=jnp.float32)
        base = block * KEY_BLOCK
        for row_lag in range(QCONV):
            first = row_lag * KEY_BLOCK
            head_rows = conv_body[first : first + edge] + conv_top[
                row_lag * edge : (row_lag + 1) * edge
            ]
            rest_rows = conv_body[first + edge : first + KEY_BLOCK]
            cols = slice(row_lag * KEY_BLOCK, (row_lag + 1) * KEY_BLOCK)
            for part, rows in ((head_rows, slice(base, base + edge)),
                               (rest_rows, slice(base + edge, base + KEY_BLOCK))):
                part_high = part.astype(jnp.bfloat16)
                part_low = (part - part_high.astype(jnp.float32)).astype(jnp.bfloat16)
                conv_ref[0, rows, cols] = part_high
                conv_ref[1, rows, cols] = part_low
    query = query_ref[0]
    out_ref[0] = jnp.dot(conv_ref[0], query, preferred_element_type=jnp.float32) + jnp.dot(
        conv_ref[1], query, preferred_element_type=jnp.float32
    )


def conv_logits(shifted_t, score_kernel, key_pad):
    heads, contract, row_count = shifted_t.shape
    seq_len = key_pad.shape[0]
    head_dim = key_pad.shape[1] // heads
    span = min(seq_len, KEY_SPAN)
    taps = (score_kernel * head_dim ** (-0.5)).reshape(-1)
    return pl.pallas_call(
        logits_kernel,
        grid=(heads, seq_len // span),
        in_specs=[
            pl.BlockSpec(memory_space=pltpu.SMEM),
            pl.BlockSpec((1, contract, row_count), lambda h, g: (h, 0, 0)),
            pl.BlockSpec((key_pad.shape[0], head_dim), lambda h, g: (0, h)),
        ],
        out_specs=pl.BlockSpec((1, span, row_count), lambda h, g: (h, g, 0)),
        out_shape=jax.ShapeDtypeStruct((heads, seq_len, row_count), jnp.float32),
        scratch_shapes=[
            pltpu.VMEM((QCONV * (KEY_BLOCK + 16), KEY_BLOCK), jnp.bfloat16),
            pltpu.VMEM((QCONV * (KEY_BLOCK + 16), KEY_BLOCK), jnp.bfloat16),
            pltpu.VMEM((2, span, QCONV * head_dim), jnp.bfloat16),
        ],
    )(taps, shifted_t, key_pad)


def band_terms(query_rows, query_first, key_flat, score_kernel):
    row_lead = QCONV - 1
    heads = score_kernel.shape[0]
    ext_count = query_rows.shape[0]
    row_count = ext_count - row_lead
    near = lax.dynamic_slice_in_dim(key_flat, query_first + 4, ext_count + QCONV - 2, 0)
    query_heads = query_rows.reshape(ext_count, heads, -1).astype(jnp.float32)
    near_heads = near.reshape(near.shape[0], heads, -1).astype(jnp.float32)
    scale = query_heads.shape[2] ** (-0.5)
    diagonals = [
        jnp.sum(query_heads * near_heads[lag - 1 : lag - 1 + ext_count], axis=2) * scale
        for lag in range(1, QCONV)
    ]
    band = []
    for gap in range(QCONV - 1):
        acc = jnp.zeros((row_count, heads), jnp.float32)
        for row_lag in range(gap + 1, QCONV):
            for col_lag in range(row_lag - gap):
                lag = row_lag - col_lag - gap
                acc = acc - score_kernel[None, :, row_lag, col_lag] * diagonals[lag - 1][
                    row_lead - row_lag : row_lead - row_lag + row_count
                ]
        band.append(acc.T)
    return jnp.stack(band)


def attend_chunk(shifted, band, query_first, key_pad, score_kernel, value_heads, head_mixing):
    row_count, heads = shifted.shape[:2]
    seq_len = value_heads.shape[0]
    shifted_t = jnp.transpose(shifted, (1, 2, 3, 0)).reshape((heads, -1, row_count))
    convolved = conv_logits(shifted_t, score_kernel, key_pad)
    query_pos = query_first + lax.iota(jnp.int32, row_count)
    gap = query_pos[None, :] - lax.iota(jnp.int32, seq_len)[:, None]
    for lag in range(QCONV - 1):
        convolved = convolved + jnp.where(gap == lag, band[lag][:, None, :], 0.0)
    logits = jnp.where(gap >= 0, convolved, lowest)
    peak = jnp.max(logits, axis=1, keepdims=True)
    expd = jnp.exp(logits - peak)
    probabilities = expd * (1.0 / jnp.sum(expd, axis=1, keepdims=True))
    grouped = probabilities.reshape(heads // GROUP, GROUP, seq_len, row_count)
    weights = head_mixing.reshape(heads // GROUP, GROUP, GROUP)
    mixed_probs = jnp.zeros_like(grouped)
    for source in range(GROUP):
        mixed_probs = mixed_probs + weights[:, :, source, None, None] * grouped[:, source, None]
    mixed_probs = mixed_probs.reshape(heads, seq_len, row_count).astype(jnp.bfloat16)
    return jnp.einsum(
        "hki,khd->ihd", mixed_probs, value_heads, preferred_element_type=jnp.float32
    )


def normalize(weighted, gain_local):
    factor = lax.rsqrt(jnp.mean(weighted * weighted, axis=2, keepdims=True) + epsilon)
    return (
        (weighted * factor * gain_local[None]).astype(jnp.bfloat16).reshape(weighted.shape[0], -1)
    )


def shards(query_states, key_states, value_states, score_kernel, head_mixing, head_gain):
    groups = lax.axis_size("uly")
    stacked = jnp.stack([query_states, key_states, value_states])
    group_width = stacked.shape[2] // groups
    pieces = exchanged(
        lambda group: lax.dynamic_slice_in_dim(stacked, group * group_width, group_width, 2),
        "uly",
    )
    pieces = jnp.moveaxis(pieces, 0, 1)
    query_local, key_local, value_local = pieces.reshape(
        (pieces.shape[0], -1, pieces.shape[-1])
    )
    shard_rows = query_local.shape[0]
    width = query_local.shape[1]
    row_lead = QCONV - 1
    heads = score_kernel.shape[0]
    head_dim = width // heads
    ctx_place = lax.axis_index("ctx")
    query_first = ctx_place * shard_rows
    earlier = passed_along(query_local[shard_rows - row_lead :], "ctx", 1)
    query_ext = jnp.concatenate([earlier, query_local], axis=0)
    key_all = gathered(key_local, "ctx").reshape((-1, width))
    key_all, value_local = lax.optimization_barrier((key_all, value_local))
    value_all = gathered(value_local, "ctx").reshape((-1, width))
    seq_len = key_all.shape[0]
    key_pad = key_all
    edge = jnp.zeros((8, width), key_all.dtype)
    key_flat = jnp.concatenate([edge, key_all, edge], axis=0)
    band = band_terms(query_ext, query_first, key_flat, score_kernel)
    query_heads = query_ext.reshape(shard_rows + row_lead, heads, head_dim)
    shifted = jnp.stack(
        [query_heads[row_lead - lag : row_lead - lag + shard_rows] for lag in range(QCONV)], axis=2
    )
    value_heads = value_all.reshape(seq_len, heads, head_dim)
    chunk = min(ROW_CHUNK * KEY_BLOCK * 8 // seq_len, shard_rows)
    if chunk == shard_rows:
        weighted = attend_chunk(
            shifted, band, query_first, key_pad, score_kernel, value_heads, head_mixing
        )
    else:
        chunks = shard_rows // chunk

        def one_chunk(index):
            start = index * chunk
            return attend_chunk(
                lax.dynamic_slice_in_dim(shifted, start, chunk, 0),
                lax.dynamic_slice_in_dim(band, start, chunk, 2),
                query_first + start,
                key_pad,
                score_kernel,
                value_heads,
                head_mixing,
            )

        weighted = lax.map(one_chunk, jnp.arange(chunks, dtype=jnp.int32))
        weighted = weighted.reshape((shard_rows,) + weighted.shape[2:])
    gain_local = head_gain.reshape(heads, head_dim)
    attended = normalize(weighted, gain_local)
    block_rows = shard_rows // groups
    returned = exchanged(
        lambda group: lax.dynamic_slice_in_dim(attended, group * block_rows, block_rows, 0),
        "uly",
    )
    return jnp.moveaxis(returned, 0, 1).reshape((block_rows, -1))


def solution(mesh):
    placed = (
        P(("ctx", "uly"), None),
        P(("ctx", "uly"), None),
        P(("ctx", "uly"), None),
        P("uly", None, None),
        P("uly", None),
        P("uly"),
    )
    return jax.shard_map(
        shards, mesh=mesh, in_specs=placed, out_specs=P(("ctx", "uly"), None), check_vma=False
    )
```

```python
import jax
import jax.numpy as jnp
from jax import lax
from jax.experimental import pallas as pl
from jax.experimental.pallas import tpu as pltpu
from jax.sharding import PartitionSpec as P

GROUP = 4
QCONV = 6
KCONV = 11
KEY_BLOCK = 128
KEY_SPAN = 1024
ROW_CHUNK = 128


lowest = -1e30
epsilon = 1e-06


def passed_along(shard, axis, by):
    peers = lax.axis_size(axis)
    pairs = [(i, i + by) for i in range(peers) if 0 <= i + by < peers]
    return lax.ppermute(shard, axis, pairs)


def exchanged(pieces_of, axis):
    peers = lax.axis_size(axis)
    place = lax.axis_index(axis)
    received = [pieces_of(place)]
    for shift in range(1, peers):
        outgoing = pieces_of((place + shift) % peers)
        pairs = [(i, (i + shift) % peers) for i in range(peers)]
        received.append(lax.ppermute(outgoing, axis, pairs))
    order = (place - jnp.arange(peers, dtype=jnp.int32)) % peers
    return jnp.take(jnp.stack(received), order, axis=0)


def gathered(shard, axis):
    peers = lax.axis_size(axis)
    place = lax.axis_index(axis)
    if peers & (peers - 1):
        return lax.all_gather(shard, axis, axis=0, tiled=False)
    bits = peers.bit_length() - 1
    held = shard[None]
    for level in reversed(range(bits)):
        bit = 1 << level
        incoming = lax.ppermute(held, axis, [(i, i ^ bit) for i in range(peers)])
        upper = (place & bit) != 0
        held = jnp.where(
            upper,
            jnp.concatenate([incoming, held], axis=0),
            jnp.concatenate([held, incoming], axis=0),
        )
    held = held.reshape((2,) * bits + shard.shape)
    return jnp.transpose(held, tuple(reversed(range(bits))) + tuple(range(bits, held.ndim)))


def logits_kernel(taps_ref, query_ref, keys_ref, out_ref, high_ref, low_ref, conv_ref):
    head = pl.program_id(0)
    group = pl.program_id(1)
    edge = 16

    @pl.when(group == 0)
    def _():
        lane = lax.broadcasted_iota(jnp.int32, (1, 2 * KEY_BLOCK), 1)
        for row_lag in range(QCONV):
            row = jnp.zeros(lane.shape, jnp.float32)
            for col_lag in range(KCONV):
                tap = taps_ref[(head * QCONV + row_lag) * KCONV + col_lag]
                row = jnp.where(lane == KEY_BLOCK - col_lag, tap, row)
            toeplitz = pltpu.roll(
                jnp.broadcast_to(row, (KEY_BLOCK, 2 * KEY_BLOCK)), 0, 1, stride=1, stride_axis=0
            )
            high = toeplitz.astype(jnp.bfloat16)
            low = (toeplitz - high.astype(jnp.float32)).astype(jnp.bfloat16)
            high_ref[row_lag * KEY_BLOCK : (row_lag + 1) * KEY_BLOCK] = high[:, KEY_BLOCK:]
            low_ref[row_lag * KEY_BLOCK : (row_lag + 1) * KEY_BLOCK] = low[:, KEY_BLOCK:]
            top = QCONV * KEY_BLOCK + row_lag * edge
            high_ref[top : top + edge] = high[:edge, :KEY_BLOCK]
            low_ref[top : top + edge] = low[:edge, :KEY_BLOCK]

    blocks = conv_ref.shape[1] // KEY_BLOCK
    body = QCONV * KEY_BLOCK
    for block in range(blocks):
        start = pl.multiple_of((group * blocks + block) * KEY_BLOCK, KEY_BLOCK)
        before_start = pl.multiple_of(jnp.maximum(start - KEY_BLOCK, 0), KEY_BLOCK)
        before = keys_ref[pl.ds(before_start, KEY_BLOCK), :]
        before = jnp.where(start > 0, before, jnp.zeros(before.shape, before.dtype))
        current = keys_ref[pl.ds(start, KEY_BLOCK), :]
        conv_body = jnp.dot(
            high_ref[:body], current, preferred_element_type=jnp.float32
        ) + jnp.dot(low_ref[:body], current, preferred_element_type=jnp.float32)
        conv_top = jnp.dot(
            high_ref[body:], before, preferred_element_type=jnp.float32
        ) + jnp.dot(low_ref[body:], before, preferred_element_type=jnp.float32)
        base = block * KEY_BLOCK
        for row_lag in range(QCONV):
            first = row_lag * KEY_BLOCK
            head_rows = conv_body[first : first + edge] + conv_top[
                row_lag * edge : (row_lag + 1) * edge
            ]
            rest_rows = conv_body[first + edge : first + KEY_BLOCK]
            cols = slice(row_lag * KEY_BLOCK, (row_lag + 1) * KEY_BLOCK)
            for part, rows in ((head_rows, slice(base, base + edge)),
                               (rest_rows, slice(base + edge, base + KEY_BLOCK))):
                part_high = part.astype(jnp.bfloat16)
                part_low = (part - part_high.astype(jnp.float32)).astype(jnp.bfloat16)
                conv_ref[0, rows, cols] = part_high
                conv_ref[1, rows, cols] = part_low
    query = query_ref[0]
    out_ref[0] = jnp.dot(conv_ref[0], query, preferred_element_type=jnp.float32) + jnp.dot(
        conv_ref[1], query, preferred_element_type=jnp.float32
    )


def conv_logits(shifted_t, score_kernel, key_pad):
    heads, contract, row_count = shifted_t.shape
    seq_len = key_pad.shape[0]
    head_dim = key_pad.shape[1] // heads
    span = min(seq_len, KEY_SPAN)
    taps = (score_kernel * head_dim ** (-0.5)).reshape(-1)
    return pl.pallas_call(
        logits_kernel,
        grid=(heads, seq_len // span),
        in_specs=[
            pl.BlockSpec(memory_space=pltpu.SMEM),
            pl.BlockSpec((1, contract, row_count), lambda h, g: (h, 0, 0)),
            pl.BlockSpec((key_pad.shape[0], head_dim), lambda h, g: (0, h)),
        ],
        out_specs=pl.BlockSpec((1, span, row_count), lambda h, g: (h, g, 0)),
        out_shape=jax.ShapeDtypeStruct((heads, seq_len, row_count), jnp.float32),
        scratch_shapes=[
            pltpu.VMEM((QCONV * (KEY_BLOCK + 16), KEY_BLOCK), jnp.bfloat16),
            pltpu.VMEM((QCONV * (KEY_BLOCK + 16), KEY_BLOCK), jnp.bfloat16),
            pltpu.VMEM((2, span, QCONV * head_dim), jnp.bfloat16),
        ],
    )(taps, shifted_t, key_pad)


def band_terms(query_rows, query_first, key_flat, score_kernel):
    row_lead = QCONV - 1
    heads = score_kernel.shape[0]
    ext_count = query_rows.shape[0]
    row_count = ext_count - row_lead
    near = lax.dynamic_slice_in_dim(key_flat, query_first + 4, ext_count + QCONV - 2, 0)
    query_heads = query_rows.reshape(ext_count, heads, -1).astype(jnp.float32)
    near_heads = near.reshape(near.shape[0], heads, -1).astype(jnp.float32)
    scale = query_heads.shape[2] ** (-0.5)
    diagonals = [
        jnp.sum(query_heads * near_heads[lag - 1 : lag - 1 + ext_count], axis=2) * scale
        for lag in range(1, QCONV)
    ]
    band = []
    for gap in range(QCONV - 1):
        acc = jnp.zeros((row_count, heads), jnp.float32)
        for row_lag in range(gap + 1, QCONV):
            for col_lag in range(row_lag - gap):
                lag = row_lag - col_lag - gap
                acc = acc - score_kernel[None, :, row_lag, col_lag] * diagonals[lag - 1][
                    row_lead - row_lag : row_lead - row_lag + row_count
                ]
        band.append(acc.T)
    return jnp.stack(band)


def attend_chunk(shifted, band, query_first, key_pad, score_kernel, value_heads, head_mixing):
    row_count, heads = shifted.shape[:2]
    seq_len = value_heads.shape[0]
    shifted_t = jnp.transpose(shifted, (1, 2, 3, 0)).reshape((heads, -1, row_count))
    convolved = conv_logits(shifted_t, score_kernel, key_pad)
    query_pos = query_first + lax.iota(jnp.int32, row_count)
    gap = query_pos[None, :] - lax.iota(jnp.int32, seq_len)[:, None]
    for lag in range(QCONV - 1):
        convolved = convolved + jnp.where(gap == lag, band[lag][:, None, :], 0.0)
    logits = jnp.where(gap >= 0, convolved, lowest)
    peak = jnp.max(logits, axis=1, keepdims=True)
    expd = jnp.exp(logits - peak)
    probabilities = expd / jnp.sum(expd, axis=1, keepdims=True)
    grouped = probabilities.reshape(heads // GROUP, GROUP, seq_len, row_count)
    weights = head_mixing.reshape(heads // GROUP, GROUP, GROUP)
    mixed_probs = jnp.zeros_like(grouped)
    for source in range(GROUP):
        mixed_probs = mixed_probs + weights[:, :, source, None, None] * grouped[:, source, None]
    mixed_probs = mixed_probs.reshape(heads, seq_len, row_count).astype(jnp.bfloat16)
    return jnp.einsum(
        "hki,khd->ihd", mixed_probs, value_heads, preferred_element_type=jnp.float32
    )


def normalize(weighted, gain_local):
    factor = lax.rsqrt(jnp.mean(weighted * weighted, axis=2, keepdims=True) + epsilon)
    return (
        (weighted * factor * gain_local[None]).astype(jnp.bfloat16).reshape(weighted.shape[0], -1)
    )


def shards(query_states, key_states, value_states, score_kernel, head_mixing, head_gain):
    groups = lax.axis_size("uly")
    stacked = jnp.stack([query_states, key_states, value_states])
    group_width = stacked.shape[2] // groups
    pieces = exchanged(
        lambda group: lax.dynamic_slice_in_dim(stacked, group * group_width, group_width, 2),
        "uly",
    )
    pieces = jnp.moveaxis(pieces, 0, 1)
    query_local, key_local, value_local = pieces.reshape(
        (pieces.shape[0], -1, pieces.shape[-1])
    )
    shard_rows = query_local.shape[0]
    width = query_local.shape[1]
    row_lead = QCONV - 1
    heads = score_kernel.shape[0]
    head_dim = width // heads
    ctx_place = lax.axis_index("ctx")
    query_first = ctx_place * shard_rows
    earlier = passed_along(query_local[shard_rows - row_lead :], "ctx", 1)
    query_ext = jnp.concatenate([earlier, query_local], axis=0)
    key_all = gathered(key_local, "ctx").reshape((-1, width))
    key_all, value_local = lax.optimization_barrier((key_all, value_local))
    value_all = gathered(value_local, "ctx").reshape((-1, width))
    seq_len = key_all.shape[0]
    key_pad = key_all
    edge = jnp.zeros((8, width), key_all.dtype)
    key_flat = jnp.concatenate([edge, key_all, edge], axis=0)
    band = band_terms(query_ext, query_first, key_flat, score_kernel)
    query_heads = query_ext.reshape(shard_rows + row_lead, heads, head_dim)
    shifted = jnp.stack(
        [query_heads[row_lead - lag : row_lead - lag + shard_rows] for lag in range(QCONV)], axis=2
    )
    value_heads = value_all.reshape(seq_len, heads, head_dim)
    chunk = min(ROW_CHUNK * KEY_BLOCK * 8 // seq_len, shard_rows)
    if chunk == shard_rows:
        weighted = attend_chunk(
            shifted, band, query_first, key_pad, score_kernel, value_heads, head_mixing
        )
    else:
        chunks = shard_rows // chunk

        def one_chunk(index):
            start = index * chunk
            return attend_chunk(
                lax.dynamic_slice_in_dim(shifted, start, chunk, 0),
                lax.dynamic_slice_in_dim(band, start, chunk, 2),
                query_first + start,
                key_pad,
                score_kernel,
                value_heads,
                head_mixing,
            )

        weighted = lax.map(one_chunk, jnp.arange(chunks, dtype=jnp.int32))
        weighted = weighted.reshape((shard_rows,) + weighted.shape[2:])
    gain_local = head_gain.reshape(heads, head_dim)
    attended = normalize(weighted, gain_local)
    block_rows = shard_rows // groups
    attended = attended.reshape((groups, block_rows, -1))
    returned = exchanged(
        lambda group: lax.dynamic_index_in_dim(attended, group, 0, keepdims=False), "uly"
    )
    return jnp.moveaxis(returned, 0, 1).reshape((block_rows, -1))


def solution(mesh):
    placed = (
        P(("ctx", "uly"), None),
        P(("ctx", "uly"), None),
        P(("ctx", "uly"), None),
        P("uly", None, None),
        P("uly", None),
        P("uly"),
    )
    return jax.shard_map(
        shards, mesh=mesh, in_specs=placed, out_specs=P(("ctx", "uly"), None), check_vma=False
    )
```
